32 devices in a mesh: aux: 4 (over y, x), pair: 8 (over z, core).
Axes of the slice: x: 2, y: 2, z: 4, core: 2. Of those that a mesh axis runs over, the one named last changes fastest.
Arguments:
- three_index: bfloat16 [32, 2048, 256], P('pair', 'aux'), may hold values from -6 to 6
- pno_coef: bfloat16 [128, 2, 256, 192], P('pair'), may hold values from -0.375 to 0.375
- pair_orbitals: int32 [128, 2], P('pair'), may hold values from 0 to 31, as said below
- natural_orbital_class: int32 [128], P('pair'), may hold values from 0 to 3
- pno_energy: float32 [128, 192], P('pair'), may hold values from 0.5 to 4
- margin: bfloat16 [128, 2, 192, 192], P('pair'), may hold values from -0.4375 to 0.4375
- neighbour_pairs: int32 [128, 2], P('pair'), may hold values from 0 to 127, as said below
- fock_coupling: float32 [128, 2], P('pair'), may hold values from -0.9 to 0.9
Outputs:
- amplitudes: float32 [128, 192, 192], P('pair')
- residual: float32 [128, 192, 192], P('pair')
The draws below stay inside these ranges and needn't reach their ends.
Inputs may be any that keep to these rules, and one draw needn't show every extreme that they name: `pair_orbitals`: column 0 names an orbital of the pair's own block of 4 orbitals (pair p's block is p // 16); column 1 names one of that block or of the block just before or after it. `neighbour_pairs`: each entry names another pair of the pair's own block of 16 pairs or of the block just before or after it.
All inputs are finite; a program needn't handle non-finite values.
Results may differ from the reference program's by a relative error of at most 0.0032.
Values may be sent and summed in bfloat16 or wider, within the bound.
No kernel may reach another device: no remote copies, remote signals or barrier semaphores. Data moves between devices by JAX's collectives and lax.ppermute only.
A program may use at most 128 MiB of HBM per device.

```python
import math
import jax
import jax.numpy as jnp
from jax import lax

NFIT = 2048
NPAO = 256
NPNO = 192
NNB = 2
ITERS = 2
OCC_DEV = 4
PAIR_DEV = 16
NOCC = 32
NPAIRS = 128


def draw_pair_orbitals(key, part):
    n_blocks = NPAIRS // PAIR_DEV
    pair_index = jnp.arange(NPAIRS, dtype=jnp.int32)
    owner_block = pair_index // PAIR_DEV
    pair_slot = pair_index % PAIR_DEV
    key_one, key_two, third_random_key = jax.random.split(jax.random.fold_in(key, 11), 3)
    own_orbital = owner_block * OCC_DEV + jax.random.randint(key_one, (NPAIRS,), 0, OCC_DEV)
    block_step = jax.random.randint(key_two, (NPAIRS,), -1, 2)
    block_step = jnp.where(pair_slot == 0, -1, jnp.where(pair_slot == 1, 1, block_step))
    other_block = jnp.clip(owner_block + block_step, 0, n_blocks - 1)
    other_orbital = other_block * OCC_DEV + jax.random.randint(third_random_key, (NPAIRS,), 0, OCC_DEV)
    return jnp.stack([own_orbital, other_orbital], axis=1).astype(jnp.int32)


def draw_neighbour_pairs(key, part):
    n_blocks = NPAIRS // PAIR_DEV
    pair_index = jnp.arange(NPAIRS, dtype=jnp.int32)
    owner_block = (pair_index // PAIR_DEV)[:, None]
    pair_slot = (pair_index % PAIR_DEV)[:, None]
    column = jnp.arange(NNB, dtype=jnp.int32)[None, :]
    key_one, key_two = jax.random.split(jax.random.fold_in(key, 23), 2)
    block_step = jax.random.randint(key_one, (NPAIRS, NNB), -1, 2)
    block_step = jnp.where((pair_slot == 0) & (column == 0), -1, block_step)
    block_step = jnp.where((pair_slot == 1) & (column == NNB - 1), 1, block_step)
    target_block = jnp.clip(owner_block + block_step, 0, n_blocks - 1)
    target_slot = (pair_slot + 1 + jax.random.randint(key_two, (NPAIRS, NNB), 0, PAIR_DEV - 1)) % PAIR_DEV
    return (target_block * PAIR_DEV + target_slot).astype(jnp.int32)


def touch_ends(array, key, low, high):
    spot = [jax.random.randint(jax.random.fold_in(key, axis), (), 0, length) for axis, length in enumerate(array.shape)]
    widest = array.shape.index(max(array.shape))
    beside = spot[:widest] + [(spot[widest] + 1) % array.shape[widest]] + spot[widest + 1:]
    return array.at[tuple(spot)].set(low).at[tuple(beside)].set(high)


def block_scale(stream_key, shape, shards, low, high):
    factor_of = 1.0
    for axis_at, parts in shards:
        heights = jax.random.uniform(jax.random.fold_in(jax.random.fold_in(stream_key, 6), axis_at), (parts,), jnp.float32, low / len(shards), high / len(shards))
        factor_of = factor_of * jnp.repeat(jnp.exp(heights), shape[axis_at] // parts).reshape((-1,) + (1,) * (len(shape) - 1 - axis_at))
    return factor_of


def normal_values(stream_key, extent, scale, limit, cuts=(), kind=jnp.bfloat16):
    factor_of = block_scale(stream_key, extent, cuts, -0.22, 0.18) if cuts else 1.0
    array = jax.random.normal(stream_key, extent, jnp.float32) * scale * factor_of
    return jnp.minimum(jnp.maximum(array, -limit), limit).astype(kind)


def setup_inputs(seed: int = 0) -> dict:
    keys = jax.random.split(jax.random.key(seed), 9)
    return {
        "three_index": normal_values(keys[0], (NOCC, NFIT, NPAO), 1.0, 6.0, ((0, 8), (1, 4))),
        "pno_coef": normal_values(keys[1], (NPAIRS, 2, NPAO, NPNO), NPAO ** -0.5, 0.375, ((0, 8),)),
        "pair_orbitals": draw_pair_orbitals(jax.random.fold_in(keys[8], 71), 0),
        "natural_orbital_class": touch_ends(jax.random.randint(keys[3], (NPAIRS,), 0, 4), jax.random.fold_in(keys[3], 1), 0, 3).astype(jnp.int32),
        "pno_energy": jnp.clip(jnp.exp(math.log(4.0) - 2.0794415 * jax.random.uniform(keys[4], (NPAIRS, NPNO), jnp.float32) ** block_scale(keys[4], (NPAIRS, NPNO), ((0, 8),), -0.2, 0.2)), 0.5, 4.0),
        "margin": normal_values(keys[5], (NPAIRS, NNB, NPNO, NPNO), NPNO ** -0.5, 0.4375, ((0, 8),)),
        "neighbour_pairs": draw_neighbour_pairs(jax.random.fold_in(keys[8], 71), 0),
        "fock_coupling": jnp.clip(jax.random.uniform(keys[7], (NPAIRS, NNB), jnp.float32, -0.9, 0.9) * block_scale(keys[7], (NPAIRS, NNB), ((0, 8),), -0.4, 0.0), -0.9, 0.9),
    }


def class_mask(natural_orbital_class):
    counts = jnp.where(natural_orbital_class == 0, NPNO // 6, jnp.where(natural_orbital_class == 1, NPNO // 3, jnp.where(natural_orbital_class == 2, 2 * NPNO // 3, NPNO)))
    return (jnp.arange(NPNO, dtype=jnp.int32)[None, :] < counts[:, None]).astype(jnp.float32)


def reference(three_index, pno_coef, pair_orbitals, natural_orbital_class, pno_energy, margin, neighbour_pairs, fock_coupling):
    natural_orbital_mask = class_mask(natural_orbital_class)

    def one_pair(inputs):
        orbitals, coefficients, row_mask = inputs
        leading_block = three_index[orbitals[0]]
        trailing_block = three_index[orbitals[1]]
        first_coef = (coefficients[0].astype(jnp.float32) * row_mask[None, :]).astype(jnp.bfloat16)
        second_coef = (coefficients[1].astype(jnp.float32) * row_mask[None, :]).astype(jnp.bfloat16)
        left_half = jnp.dot(leading_block, first_coef, preferred_element_type=jnp.float32).astype(jnp.bfloat16)
        right_half = jnp.dot(trailing_block, second_coef, preferred_element_type=jnp.float32).astype(jnp.bfloat16)
        return jnp.dot(left_half.T, right_half, preferred_element_type=jnp.float32)

    exchange_ints = lax.map(one_pair, (pair_orbitals, pno_coef, natural_orbital_mask))
    denominator = pno_energy[:, :, None] + pno_energy[:, None, :]

    def coupling(current):
        def one_coupling(inputs):
            neighbours, margin_block, couplings, row_mask = inputs
            gathered = current[neighbours]
            sandwich_side = margin_block.astype(jnp.float32) * row_mask[None, :, None]
            inner_part = jnp.einsum('nab,nbc->nac', sandwich_side, gathered, precision=lax.Precision.HIGHEST)
            outer_part = jnp.einsum('nac,ndc->nad', inner_part, sandwich_side, precision=lax.Precision.HIGHEST)
            return jnp.einsum('n,nad->ad', couplings, outer_part, precision=lax.Precision.HIGHEST)
        return lax.map(one_coupling, (neighbour_pairs, margin, fock_coupling, natural_orbital_mask))

    amplitudes = jnp.zeros_like(exchange_ints)
    for iteration in range(ITERS):
        current_residual = exchange_ints + denominator * amplitudes
        if iteration > 0:
            current_residual = current_residual - coupling(amplitudes)
        amplitudes = amplitudes - current_residual / denominator
    residual = exchange_ints + denominator * amplitudes - coupling(amplitudes)
    return amplitudes, residual
```

```python
import functools

import jax
import jax.numpy as jnp
from jax import lax
from jax.experimental import pallas as pl
from jax.experimental.pallas import tpu as pltpu
from jax.sharding import PartitionSpec as P

NPNO = 192
ITERS = 2


def with_halo(cells, axis):
    count = lax.axis_size(axis)
    ends = count - 1
    from_left = lax.ppermute(cells, axis, [(i, i + 1) for i in range(ends)])
    from_right = lax.ppermute(cells, axis, [(i + 1, i) for i in range(ends)])
    return jnp.concatenate([from_left, cells, from_right], axis=0)


def class_size(natural_orbital_class):
    return jnp.where(
        natural_orbital_class == 0,
        NPNO // 6,
        jnp.where(
            natural_orbital_class == 1,
            NPNO // 3,
            jnp.where(natural_orbital_class == 2, 2 * NPNO // 3, NPNO),
        ),
    ).astype(jnp.int32)


def exchange_kernel(lead_ref, trail_ref, size_ref, x_lead, x_trail, coef_ref, out_ref):
    p = pl.program_id(0)
    keep = lax.broadcasted_iota(jnp.int32, (1, NPNO), 1) < size_ref[p]
    zero = jnp.zeros((), jnp.bfloat16)
    first = jnp.where(keep, coef_ref[0, 0], zero)
    second = jnp.where(keep, coef_ref[0, 1], zero)
    left = jnp.dot(x_lead[0], first, preferred_element_type=jnp.float32).astype(jnp.bfloat16)
    right = jnp.dot(x_trail[0], second, preferred_element_type=jnp.float32).astype(jnp.bfloat16)
    out_ref[0] = lax.dot_general(
        left, right, (((0,), (0,)), ((), ())), preferred_element_type=jnp.float32
    )


def partial_exchange(lead, trail, sizes, blocks, coef):
    pairs = coef.shape[0]
    nfit, npao = blocks.shape[1], blocks.shape[2]
    grid_spec = pltpu.PrefetchScalarGridSpec(
        num_scalar_prefetch=3,
        grid=(pairs,),
        in_specs=[
            pl.BlockSpec((1, nfit, npao), lambda i, a, b, s: (a[i], 0, 0)),
            pl.BlockSpec((1, nfit, npao), lambda i, a, b, s: (b[i], 0, 0)),
            pl.BlockSpec((1, 2, npao, NPNO), lambda i, a, b, s: (i, 0, 0, 0)),
        ],
        out_specs=pl.BlockSpec((1, NPNO, NPNO), lambda i, a, b, s: (i, 0, 0)),
    )
    flops = pairs * (2 * 2 * nfit * npao * NPNO + 2 * nfit * NPNO * NPNO)
    return pl.pallas_call(
        exchange_kernel,
        grid_spec=grid_spec,
        out_shape=jax.ShapeDtypeStruct((pairs, NPNO, NPNO), jnp.float32),
        cost_estimate=pl.CostEstimate(
            flops=flops,
            bytes_accessed=pairs * (2 * nfit * npao * 2 + 2 * npao * NPNO * 2 + NPNO * NPNO * 4),
            transcendentals=0,
        ),
    )(lead, trail, sizes, blocks, blocks, coef)


def split_bf16(value):
    hi = value.astype(jnp.bfloat16)
    lo = (value - hi.astype(jnp.float32)).astype(jnp.bfloat16)
    return hi, lo


def mm(lhs, rhs, dims=(((1,), (0,)), ((), ()))):
    return lax.dot_general(lhs, rhs, dims, preferred_element_type=jnp.float32)


def coupling_kernel(
    nb_ref, size_ref, fock_ref, t_first, t_second, margin_ref, ex_ref, col_ref, row_ref, own_ref, out_ref, *, final
):
    p = pl.program_id(0)
    keep = lax.broadcasted_iota(jnp.int32, (NPNO, 1), 0) < size_ref[p]
    zero = jnp.zeros((), jnp.bfloat16)
    transposed = (((1,), (1,)), ((), ()))
    total = None
    for n, t_ref in enumerate((t_first, t_second)):
        side = jnp.where(keep, margin_ref[0, n], zero)
        t_hi, t_lo = split_bf16(t_ref[0])
        inner = mm(side, t_hi) + mm(side, t_lo)
        w_hi, w_lo = split_bf16(fock_ref[2 * p + n] * inner)
        outer = mm(w_hi, side, transposed) + mm(w_lo, side, transposed)
        total = outer if total is None else total + outer
    denominator = col_ref[0] + row_ref[0]
    amplitudes = own_ref[0]
    residual = ex_ref[0] + denominator * amplitudes - total
    if final:
        out_ref[0] = residual
    else:
        out_ref[0] = amplitudes - residual / denominator


def coupling_step(nb, sizes, fock, padded, margin, exchange, energy, own, final):
    column = energy.reshape(energy.shape[0], NPNO, 1)
    row = energy.reshape(energy.shape[0], 1, NPNO)
    pairs = own.shape[0]
    grid_spec = pltpu.PrefetchScalarGridSpec(
        num_scalar_prefetch=3,
        grid=(pairs,),
        in_specs=[
            pl.BlockSpec((1, NPNO, NPNO), lambda i, q, s, f: (q[2 * i], 0, 0)),
            pl.BlockSpec((1, NPNO, NPNO), lambda i, q, s, f: (q[2 * i + 1], 0, 0)),
            pl.BlockSpec((1, 2, NPNO, NPNO), lambda i, q, s, f: (i, 0, 0, 0)),
            pl.BlockSpec((1, NPNO, NPNO), lambda i, q, s, f: (i, 0, 0)),
            pl.BlockSpec((1, NPNO, 1), lambda i, q, s, f: (i, 0, 0)),
            pl.BlockSpec((1, 1, NPNO), lambda i, q, s, f: (i, 0, 0)),
            pl.BlockSpec((1, NPNO, NPNO), lambda i, q, s, f: (i, 0, 0)),
        ],
        out_specs=pl.BlockSpec((1, NPNO, NPNO), lambda i, q, s, f: (i, 0, 0)),
    )
    flops = pairs * 2 * 4 * 2 * NPNO * NPNO * NPNO
    return pl.pallas_call(
        functools.partial(coupling_kernel, final=final),
        grid_spec=grid_spec,
        out_shape=jax.ShapeDtypeStruct((pairs, NPNO, NPNO), jnp.float32),
        cost_estimate=pl.CostEstimate(
            flops=flops,
            bytes_accessed=pairs * NPNO * NPNO * (2 * 4 + 2 * 2 + 3 * 4),
            transcendentals=0,
        ),
    )(nb, sizes, fock, padded, padded, margin, exchange, column, row, own)


def per_device(
    three_index,
    pno_coef,
    pair_orbitals,
    natural_orbital_class,
    pno_energy,
    margin,
    neighbour_pairs,
    fock_coupling,
):
    occ_dev = three_index.shape[0]
    pair_dev = pno_coef.shape[0]
    position = lax.axis_index("pair")
    sizes = class_size(natural_orbital_class)
    padded = with_halo(three_index, "pair")
    local_orbitals = (pair_orbitals - (position - 1) * occ_dev).astype(jnp.int32)
    partial_ints = partial_exchange(
        local_orbitals[:, 0], local_orbitals[:, 1], sizes, padded, pno_coef
    )
    exchange_ints = lax.psum(partial_ints, "aux")
    denominator = pno_energy[:, :, None] + pno_energy[:, None, :]
    local_rows = (neighbour_pairs - (position - 1) * pair_dev).astype(jnp.int32).reshape(-1)
    fock = fock_coupling.reshape(-1)

    amplitudes = -(exchange_ints / denominator)
    for iteration in range(1, ITERS):
        padded_amps = with_halo(amplitudes, "pair")
        amplitudes = coupling_step(
            local_rows, sizes, fock, padded_amps, margin, exchange_ints, pno_energy, amplitudes, False
        )
    padded_amps = with_halo(amplitudes, "pair")
    residual = coupling_step(
        local_rows, sizes, fock, padded_amps, margin, exchange_ints, pno_energy, amplitudes, True
    )
    return (amplitudes, residual)


def solution(mesh):
    return jax.shard_map(
        per_device,
        mesh=mesh,
        in_specs=(
            P("pair", "aux", None),
            P("pair", None, None, None),
            P("pair", None),
            P("pair"),
            P("pair", None),
            P("pair", None, None, None),
            P("pair", None),
            P("pair", None),
        ),
        out_specs=(P("pair", None, None), P("pair", None, None)),
        check_vma=False,
    )
```

```python
import functools

import jax
import jax.numpy as jnp
from jax import lax
from jax.experimental import pallas as pl
from jax.experimental.pallas import tpu as pltpu
from jax.sharding import PartitionSpec as P

NPNO = 192
ITERS = 2


def halo_sources(cells, axis):
    count = lax.axis_size(axis)
    ends = count - 1
    from_left = lax.ppermute(cells, axis, [(i, i + 1) for i in range(ends)])
    from_right = lax.ppermute(cells, axis, [(i + 1, i) for i in range(ends)])
    return (from_left, cells, from_right)


def source_index(local, width, source):
    return jnp.where(local // width == source, local % width, 0)


def halving_stream(piece, index, count, bits):
    for bit in bits:
        side = (index // bit) % 2
        half = piece.shape[0] // 2
        keep = lax.dynamic_slice_in_dim(piece, side * half, half, axis=0)
        send = lax.dynamic_slice_in_dim(piece, (1 - side) * half, half, axis=0)
        piece = keep + lax.ppermute(send, "aux", [(i, i ^ bit) for i in range(count)])
    for bit in reversed(bits):
        side = (index // bit) % 2
        other = lax.ppermute(piece, "aux", [(i, i ^ bit) for i in range(count)])
        length = piece.shape[0]
        full = jnp.zeros((2 * length,) + piece.shape[1:], piece.dtype)
        full = lax.dynamic_update_slice_in_dim(full, piece, side * length, axis=0)
        piece = lax.dynamic_update_slice_in_dim(full, other, (1 - side) * length, axis=0)
    return piece


def sum_over_aux(partial):
    count = lax.axis_size("aux")
    if count != 4 or partial.shape[0] % 8:
        return lax.psum(partial, "aux")
    index = lax.axis_index("aux")
    half = partial.shape[0] // 2
    first = halving_stream(partial[:half], index, count, (1, 2))
    second = halving_stream(partial[half:], index, count, (2, 1))
    return jnp.concatenate([first, second], axis=0)


def class_size(natural_orbital_class):
    return jnp.where(
        natural_orbital_class == 0,
        NPNO // 6,
        jnp.where(
            natural_orbital_class == 1,
            NPNO // 3,
            jnp.where(natural_orbital_class == 2, 2 * NPNO // 3, NPNO),
        ),
    ).astype(jnp.int32)


def exchange_kernel(lead_ref, trail_ref, size_ref, x_lead, t_left, t_own, t_right, coef_ref, out_ref, *, occ):
    p = pl.program_id(0)
    keep = lax.broadcasted_iota(jnp.int32, (NPNO, 1), 0) < size_ref[p]
    zero = jnp.zeros((), jnp.bfloat16)
    first = jnp.where(keep, coef_ref[0, 0], zero)
    second = jnp.where(keep, coef_ref[0, 1], zero)
    source = trail_ref[p] // occ
    x_trail = jnp.where(source == 0, t_left[0], jnp.where(source == 1, t_own[0], t_right[0]))
    transposed = (((1,), (1,)), ((), ()))
    left_t = lax.dot_general(first, x_lead[0], transposed, preferred_element_type=jnp.float32)
    right = lax.dot_general(x_trail, second, transposed, preferred_element_type=jnp.float32)
    out_ref[0] = jnp.dot(
        left_t.astype(jnp.bfloat16), right.astype(jnp.bfloat16), preferred_element_type=jnp.float32
    )


def partial_exchange(lead, trail, sizes, sources, coef_t):
    pairs = coef_t.shape[0]
    occ, nfit, npao = sources[1].shape
    block = (1, nfit, npao)

    def trail_spec(source):
        return pl.BlockSpec(block, lambda i, a, b, s: (source_index(b[i], occ, source), 0, 0))

    grid_spec = pltpu.PrefetchScalarGridSpec(
        num_scalar_prefetch=3,
        grid=(pairs,),
        in_specs=[
            pl.BlockSpec(block, lambda i, a, b, s: (a[i], 0, 0)),
            trail_spec(0),
            trail_spec(1),
            trail_spec(2),
            pl.BlockSpec((1, 2, NPNO, npao), lambda i, a, b, s: (i, 0, 0, 0)),
        ],
        out_specs=pl.BlockSpec((1, NPNO, NPNO), lambda i, a, b, s: (i, 0, 0)),
    )
    flops = pairs * (2 * 2 * nfit * npao * NPNO + 2 * nfit * NPNO * NPNO)
    return pl.pallas_call(
        functools.partial(exchange_kernel, occ=occ),
        grid_spec=grid_spec,
        out_shape=jax.ShapeDtypeStruct((pairs, NPNO, NPNO), jnp.float32),
        cost_estimate=pl.CostEstimate(
            flops=flops,
            bytes_accessed=pairs * (2 * nfit * npao * 2 + 2 * npao * NPNO * 2 + NPNO * NPNO * 4),
            transcendentals=0,
        ),
    )(lead, trail, sizes, sources[1], *sources, coef_t)


def split_bf16(value):
    hi = value.astype(jnp.bfloat16)
    lo = (value - hi.astype(jnp.float32)).astype(jnp.bfloat16)
    return hi, lo


def mm(lhs, rhs, dims=(((1,), (0,)), ((), ()))):
    return lax.dot_general(lhs, rhs, dims, preferred_element_type=jnp.float32)


def coupling_kernel(nb_ref, size_ref, fock_ref, *refs, final, width):
    t_refs = refs[:6]
    margin_ref, ex_ref, col_ref, row_ref, own_ref, out_ref = refs[6:]
    p = pl.program_id(0)
    keep = lax.broadcasted_iota(jnp.int32, (NPNO, 1), 0) < size_ref[p]
    zero = jnp.zeros((), jnp.bfloat16)
    transposed = (((1,), (1,)), ((), ()))
    total = None
    for n in range(2):
        source = nb_ref[2 * p + n] // width
        left, own, right = (t_refs[3 * n + k][0] for k in range(3))
        t = jnp.where(source == 0, left, jnp.where(source == 1, own, right))
        side = jnp.where(keep, margin_ref[0, n], zero)
        t_hi, t_lo = split_bf16(t)
        inner = mm(side, t_hi) + mm(side, t_lo)
        w_hi, w_lo = split_bf16(fock_ref[2 * p + n] * inner)
        outer = mm(w_hi, side, transposed) + mm(w_lo, side, transposed)
        total = outer if total is None else total + outer
    denominator = col_ref[0] + row_ref[0]
    amplitudes = own_ref[0]
    residual = ex_ref[0] + denominator * amplitudes - total
    if final:
        out_ref[0] = residual
    else:
        out_ref[0] = amplitudes - residual / denominator


def coupling_step(nb, sizes, fock, sources, margin, exchange, energy, own, final):
    column = energy.reshape(energy.shape[0], NPNO, 1)
    row = energy.reshape(energy.shape[0], 1, NPNO)
    pairs = own.shape[0]
    block = (1, NPNO, NPNO)

    def t_spec(n, source):
        return pl.BlockSpec(
            block, lambda i, q, s, f: (source_index(q[2 * i + n], pairs, source), 0, 0)
        )

    own_spec = pl.BlockSpec(block, lambda i, q, s, f: (i, 0, 0))
    grid_spec = pltpu.PrefetchScalarGridSpec(
        num_scalar_prefetch=3,
        grid=(pairs,),
        in_specs=[t_spec(n, k) for n in range(2) for k in range(3)]
        + [
            pl.BlockSpec((1, 2, NPNO, NPNO), lambda i, q, s, f: (i, 0, 0, 0)),
            own_spec,
            pl.BlockSpec((1, NPNO, 1), lambda i, q, s, f: (i, 0, 0)),
            pl.BlockSpec((1, 1, NPNO), lambda i, q, s, f: (i, 0, 0)),
            own_spec,
        ],
        out_specs=own_spec,
    )
    flops = pairs * 2 * 4 * 2 * NPNO * NPNO * NPNO
    return pl.pallas_call(
        functools.partial(coupling_kernel, final=final, width=pairs),
        grid_spec=grid_spec,
        out_shape=jax.ShapeDtypeStruct((pairs, NPNO, NPNO), jnp.float32),
        cost_estimate=pl.CostEstimate(
            flops=flops,
            bytes_accessed=pairs * NPNO * NPNO * (2 * 4 + 2 * 2 + 3 * 4),
            transcendentals=0,
        ),
    )(nb, sizes, fock, *sources, *sources, margin, exchange, column, row, own)


def per_device(
    three_index,
    pno_coef,
    pair_orbitals,
    natural_orbital_class,
    pno_energy,
    margin,
    neighbour_pairs,
    fock_coupling,
):
    occ_dev = three_index.shape[0]
    pair_dev = pno_coef.shape[0]
    position = lax.axis_index("pair")
    sizes = class_size(natural_orbital_class)
    blocks = halo_sources(three_index, "pair")
    local_orbitals = (pair_orbitals - (position - 1) * occ_dev).astype(jnp.int32)
    partial_ints = partial_exchange(
        local_orbitals[:, 0] - occ_dev,
        local_orbitals[:, 1],
        sizes,
        blocks,
        jnp.swapaxes(pno_coef, 2, 3),
    )
    exchange_ints = sum_over_aux(partial_ints)
    denominator = pno_energy[:, :, None] + pno_energy[:, None, :]
    local_rows = (neighbour_pairs - (position - 1) * pair_dev).astype(jnp.int32).reshape(-1)
    fock = fock_coupling.reshape(-1)

    amplitudes = -(exchange_ints / denominator)
    for iteration in range(1, ITERS):
        amplitudes = coupling_step(
            local_rows, sizes, fock, halo_sources(amplitudes, "pair"), margin, exchange_ints,
            pno_energy, amplitudes, False,
        )
    residual = coupling_step(
        local_rows, sizes, fock, halo_sources(amplitudes, "pair"), margin, exchange_ints,
        pno_energy, amplitudes, True,
    )
    return (amplitudes, residual)


def solution(mesh):
    return jax.shard_map(
        per_device,
        mesh=mesh,
        in_specs=(
            P("pair", "aux", None),
            P("pair", None, None, None),
            P("pair", None),
            P("pair"),
            P("pair", None),
            P("pair", None, None, None),
            P("pair", None),
            P("pair", None),
        ),
        out_specs=(P("pair", None, None), P("pair", None, None)),
        check_vma=False,
    )
```

```python
import functools

import jax
import jax.numpy as jnp
from jax import lax
from jax.experimental import pallas as pl
from jax.experimental.pallas import tpu as pltpu
from jax.sharding import PartitionSpec as P

NPNO = 192
ITERS = 2
CLASS_SIZES = (NPNO // 6, NPNO // 3, 2 * NPNO // 3, NPNO)


def halo_sources(cells, axis):
    count = lax.axis_size(axis)
    ends = count - 1
    from_left = lax.ppermute(cells, axis, [(i, i + 1) for i in range(ends)])
    from_right = lax.ppermute(cells, axis, [(i + 1, i) for i in range(ends)])
    return (from_left, cells, from_right)


def source_index(local, width, source):
    return jnp.where(local // width == source, local % width, 0)


def halving_stream(piece, index, count, bits):
    for bit in bits:
        side = (index // bit) % 2
        half = piece.shape[0] // 2
        keep = lax.dynamic_slice_in_dim(piece, side * half, half, axis=0)
        send = lax.dynamic_slice_in_dim(piece, (1 - side) * half, half, axis=0)
        piece = keep + lax.ppermute(send, "aux", [(i, i ^ bit) for i in range(count)])
    for bit in reversed(bits):
        side = (index // bit) % 2
        other = lax.ppermute(piece, "aux", [(i, i ^ bit) for i in range(count)])
        length = piece.shape[0]
        full = jnp.zeros((2 * length,) + piece.shape[1:], piece.dtype)
        full = lax.dynamic_update_slice_in_dim(full, piece, side * length, axis=0)
        piece = lax.dynamic_update_slice_in_dim(full, other, (1 - side) * length, axis=0)
    return piece


def sum_over_aux(partial):
    count = lax.axis_size("aux")
    if count != 4 or partial.shape[0] % 8:
        return lax.psum(partial, "aux")
    index = lax.axis_index("aux")
    half = partial.shape[0] // 2
    first = halving_stream(partial[:half], index, count, (1, 2))
    second = halving_stream(partial[half:], index, count, (2, 1))
    return jnp.concatenate([first, second], axis=0)


def class_size(natural_orbital_class):
    return jnp.where(
        natural_orbital_class == 0,
        NPNO // 6,
        jnp.where(
            natural_orbital_class == 1,
            NPNO // 3,
            jnp.where(natural_orbital_class == 2, 2 * NPNO // 3, NPNO),
        ),
    ).astype(jnp.int32)


def exchange_kernel(lead_ref, trail_ref, size_ref, x_lead, t_left, t_own, t_right, coef_ref, out_ref, *, occ):
    p = pl.program_id(0)
    size = size_ref[p]
    source = trail_ref[p] // occ
    x_trail = jnp.where(source == 0, t_left[0], jnp.where(source == 1, t_own[0], t_right[0]))
    transposed = (((1,), (1,)), ((), ()))
    out_ref[0] = jnp.zeros((NPNO, NPNO), jnp.float32)
    for m in CLASS_SIZES:

        @pl.when(size == m)
        def _():
            first = coef_ref[0, 0, :m, :]
            second = coef_ref[0, 1, :m, :]
            left_t = lax.dot_general(first, x_lead[0], transposed, preferred_element_type=jnp.float32)
            right = lax.dot_general(x_trail, second, transposed, preferred_element_type=jnp.float32)
            out_ref[0, :m, :m] = jnp.dot(
                left_t.astype(jnp.bfloat16), right.astype(jnp.bfloat16), preferred_element_type=jnp.float32
            )


def partial_exchange(lead, trail, sizes, sources, coef_t):
    pairs = coef_t.shape[0]
    occ, nfit, npao = sources[1].shape
    block = (1, nfit, npao)

    def trail_spec(source):
        return pl.BlockSpec(block, lambda i, a, b, s: (source_index(b[i], occ, source), 0, 0))

    grid_spec = pltpu.PrefetchScalarGridSpec(
        num_scalar_prefetch=3,
        grid=(pairs,),
        in_specs=[
            pl.BlockSpec(block, lambda i, a, b, s: (a[i], 0, 0)),
            trail_spec(0),
            trail_spec(1),
            trail_spec(2),
            pl.BlockSpec((1, 2, NPNO, npao), lambda i, a, b, s: (i, 0, 0, 0)),
        ],
        out_specs=pl.BlockSpec((1, NPNO, NPNO), lambda i, a, b, s: (i, 0, 0)),
    )
    flops = pairs * (2 * 2 * nfit * npao * NPNO + 2 * nfit * NPNO * NPNO)
    return pl.pallas_call(
        functools.partial(exchange_kernel, occ=occ),
        grid_spec=grid_spec,
        out_shape=jax.ShapeDtypeStruct((pairs, NPNO, NPNO), jnp.float32),
        cost_estimate=pl.CostEstimate(
            flops=flops,
            bytes_accessed=pairs * (2 * nfit * npao * 2 + 2 * npao * NPNO * 2 + NPNO * NPNO * 4),
            transcendentals=0,
        ),
    )(lead, trail, sizes, sources[1], *sources, coef_t)


def split_bf16(value):
    hi = value.astype(jnp.bfloat16)
    lo = (value - hi.astype(jnp.float32)).astype(jnp.bfloat16)
    return hi, lo


def mm(lhs, rhs, dims=(((1,), (0,)), ((), ()))):
    return lax.dot_general(lhs, rhs, dims, preferred_element_type=jnp.float32)


def coupling_kernel(nb_ref, size_ref, fock_ref, *refs, final, width):
    t_refs = refs[:6]
    margin_ref, ex_ref, col_ref, row_ref, own_ref, out_ref, acc_ref = refs[6:]
    p = pl.program_id(0)
    size = size_ref[p]
    transposed = (((1,), (1,)), ((), ()))
    splits = []
    for n in range(2):
        source = nb_ref[2 * p + n] // width
        left, own, right = (t_refs[3 * n + k][0] for k in range(3))
        splits.append(split_bf16(jnp.where(source == 0, left, jnp.where(source == 1, own, right))))
    acc_ref[...] = jnp.zeros((NPNO, NPNO), jnp.float32)
    for m in CLASS_SIZES:

        @pl.when(size == m)
        def _():
            total = None
            for n in range(2):
                side = margin_ref[0, n, :m, :]
                t_hi, t_lo = splits[n]
                inner = mm(side, t_hi) + mm(side, t_lo)
                w_hi, w_lo = split_bf16(fock_ref[2 * p + n] * inner)
                outer = mm(w_hi, side, transposed) + mm(w_lo, side, transposed)
                total = outer if total is None else total + outer
            acc_ref[:m, :m] = total

    denominator = col_ref[0] + row_ref[0]
    amplitudes = own_ref[0]
    residual = ex_ref[0] + denominator * amplitudes - acc_ref[...]
    if final:
        out_ref[0] = residual
    else:
        out_ref[0] = amplitudes - residual / denominator


def coupling_step(nb, sizes, fock, sources, margin, exchange, energy, own, final):
    column = energy.reshape(energy.shape[0], NPNO, 1)
    row = energy.reshape(energy.shape[0], 1, NPNO)
    pairs = own.shape[0]
    block = (1, NPNO, NPNO)

    def t_spec(n, source):
        return pl.BlockSpec(
            block, lambda i, q, s, f: (source_index(q[2 * i + n], pairs, source), 0, 0)
        )

    own_spec = pl.BlockSpec(block, lambda i, q, s, f: (i, 0, 0))
    grid_spec = pltpu.PrefetchScalarGridSpec(
        num_scalar_prefetch=3,
        grid=(pairs,),
        in_specs=[t_spec(n, k) for n in range(2) for k in range(3)]
        + [
            pl.BlockSpec((1, 2, NPNO, NPNO), lambda i, q, s, f: (i, 0, 0, 0)),
            own_spec,
            pl.BlockSpec((1, NPNO, 1), lambda i, q, s, f: (i, 0, 0)),
            pl.BlockSpec((1, 1, NPNO), lambda i, q, s, f: (i, 0, 0)),
            own_spec,
        ],
        out_specs=own_spec,
        scratch_shapes=[pltpu.VMEM((NPNO, NPNO), jnp.float32)],
    )
    flops = pairs * 2 * 4 * 2 * NPNO * NPNO * NPNO
    return pl.pallas_call(
        functools.partial(coupling_kernel, final=final, width=pairs),
        grid_spec=grid_spec,
        out_shape=jax.ShapeDtypeStruct((pairs, NPNO, NPNO), jnp.float32),
        cost_estimate=pl.CostEstimate(
            flops=flops,
            bytes_accessed=pairs * NPNO * NPNO * (2 * 4 + 2 * 2 + 3 * 4),
            transcendentals=0,
        ),
    )(nb, sizes, fock, *sources, *sources, margin, exchange, column, row, own)


def per_device(
    three_index,
    pno_coef,
    pair_orbitals,
    natural_orbital_class,
    pno_energy,
    margin,
    neighbour_pairs,
    fock_coupling,
):
    occ_dev = three_index.shape[0]
    pair_dev = pno_coef.shape[0]
    position = lax.axis_index("pair")
    sizes = class_size(natural_orbital_class)
    blocks = halo_sources(three_index, "pair")
    local_orbitals = (pair_orbitals - (position - 1) * occ_dev).astype(jnp.int32)
    partial_ints = partial_exchange(
        local_orbitals[:, 0] - occ_dev,
        local_orbitals[:, 1],
        sizes,
        blocks,
        jnp.swapaxes(pno_coef, 2, 3),
    )
    exchange_ints = sum_over_aux(partial_ints)
    denominator = pno_energy[:, :, None] + pno_energy[:, None, :]
    local_rows = (neighbour_pairs - (position - 1) * pair_dev).astype(jnp.int32).reshape(-1)
    fock = fock_coupling.reshape(-1)

    amplitudes = -(exchange_ints / denominator)
    for iteration in range(1, ITERS):
        amplitudes = coupling_step(
            local_rows, sizes, fock, halo_sources(amplitudes, "pair"), margin, exchange_ints,
            pno_energy, amplitudes, False,
        )
    residual = coupling_step(
        local_rows, sizes, fock, halo_sources(amplitudes, "pair"), margin, exchange_ints,
        pno_energy, amplitudes, True,
    )
    return (amplitudes, residual)


def solution(mesh):
    return jax.shard_map(
        per_device,
        mesh=mesh,
        in_specs=(
            P("pair", "aux", None),
            P("pair", None, None, None),
            P("pair", None),
            P("pair"),
            P("pair", None),
            P("pair", None, None, None),
            P("pair", None),
            P("pair", None),
        ),
        out_specs=(P("pair", None, None), P("pair", None, None)),
        check_vma=False,
    )
```

```python
import functools

import jax
import jax.numpy as jnp
from jax import lax
from jax.experimental import pallas as pl
from jax.experimental.pallas import tpu as pltpu
from jax.sharding import PartitionSpec as P

NPNO = 192
ITERS = 2
CLASS_SIZES = (NPNO // 6, NPNO // 3, 2 * NPNO // 3, NPNO)


def halo_sources(cells, axis):
    count = lax.axis_size(axis)
    ends = count - 1
    from_left = lax.ppermute(cells, axis, [(i, i + 1) for i in range(ends)])
    from_right = lax.ppermute(cells, axis, [(i + 1, i) for i in range(ends)])
    return (from_left, cells, from_right)


def halving_stream(piece, index, count, bits):
    for bit in bits:
        side = (index // bit) % 2
        half = piece.shape[0] // 2
        keep = lax.dynamic_slice_in_dim(piece, side * half, half, axis=0)
        send = lax.dynamic_slice_in_dim(piece, (1 - side) * half, half, axis=0)
        piece = keep + lax.ppermute(send, "aux", [(i, i ^ bit) for i in range(count)])
    for bit in reversed(bits):
        side = (index // bit) % 2
        other = lax.ppermute(piece, "aux", [(i, i ^ bit) for i in range(count)])
        length = piece.shape[0]
        full = jnp.zeros((2 * length,) + piece.shape[1:], piece.dtype)
        full = lax.dynamic_update_slice_in_dim(full, piece, side * length, axis=0)
        piece = lax.dynamic_update_slice_in_dim(full, other, (1 - side) * length, axis=0)
    return piece


def sum_over_aux(partial):
    count = lax.axis_size("aux")
    if count != 4 or partial.shape[0] % 8:
        return lax.psum(partial, "aux")
    index = lax.axis_index("aux")
    half = partial.shape[0] // 2
    first = halving_stream(partial[:half], index, count, (1, 2))
    second = halving_stream(partial[half:], index, count, (2, 1))
    return jnp.concatenate([first, second], axis=0)


def class_size(natural_orbital_class):
    return jnp.where(
        natural_orbital_class == 0,
        NPNO // 6,
        jnp.where(
            natural_orbital_class == 1,
            NPNO // 3,
            jnp.where(natural_orbital_class == 2, 2 * NPNO // 3, NPNO),
        ),
    ).astype(jnp.int32)


def exchange_kernel(lead_ref, trail_ref, size_ref, t_left, t_own, t_right, coef_ref, out_ref, *, occ):
    p = pl.program_id(0)
    size = size_ref[p]
    source = trail_ref[p] // occ
    slot = trail_ref[p] % occ
    x_trail = jnp.where(source == 0, t_left[slot], jnp.where(source == 1, t_own[slot], t_right[slot]))
    x_lead = t_own[lead_ref[p]]
    transposed = (((1,), (1,)), ((), ()))
    out_ref[0] = jnp.zeros((NPNO, NPNO), jnp.float32)
    for m in CLASS_SIZES:

        @pl.when(size == m)
        def _():
            first = coef_ref[0, 0, :m, :]
            second = coef_ref[0, 1, :m, :]
            left_t = lax.dot_general(first, x_lead, transposed, preferred_element_type=jnp.float32)
            right = lax.dot_general(x_trail, second, transposed, preferred_element_type=jnp.float32)
            out_ref[0, :m, :m] = jnp.dot(
                left_t.astype(jnp.bfloat16), right.astype(jnp.bfloat16), preferred_element_type=jnp.float32
            )


def partial_exchange(lead, trail, sizes, sources, coef_t):
    pairs = coef_t.shape[0]
    occ, nfit, npao = sources[1].shape
    whole = pl.BlockSpec((occ, nfit, npao), lambda i, a, b, s: (0, 0, 0))
    grid_spec = pltpu.PrefetchScalarGridSpec(
        num_scalar_prefetch=3,
        grid=(pairs,),
        in_specs=[
            whole,
            whole,
            whole,
            pl.BlockSpec((1, 2, NPNO, npao), lambda i, a, b, s: (i, 0, 0, 0)),
        ],
        out_specs=pl.BlockSpec((1, NPNO, NPNO), lambda i, a, b, s: (i, 0, 0)),
    )
    flops = pairs * (2 * 2 * nfit * npao * NPNO + 2 * nfit * NPNO * NPNO)
    return pl.pallas_call(
        functools.partial(exchange_kernel, occ=occ),
        grid_spec=grid_spec,
        out_shape=jax.ShapeDtypeStruct((pairs, NPNO, NPNO), jnp.float32),
        cost_estimate=pl.CostEstimate(
            flops=flops,
            bytes_accessed=pairs * (2 * nfit * npao * 2 + 2 * npao * NPNO * 2 + NPNO * NPNO * 4),
            transcendentals=0,
        ),
    )(lead, trail, sizes, *sources, coef_t)


def split_bf16(value):
    hi = value.astype(jnp.bfloat16)
    lo = (value - hi.astype(jnp.float32)).astype(jnp.bfloat16)
    return hi, lo


def mm(lhs, rhs, dims=(((1,), (0,)), ((), ()))):
    return lax.dot_general(lhs, rhs, dims, preferred_element_type=jnp.float32)


def coupling_kernel(nb_ref, size_ref, fock_ref, *refs, final, width):
    t_refs = refs[:3]
    margin_ref, ex_ref, col_ref, row_ref, own_ref, out_ref, acc_ref = refs[3:]
    p = pl.program_id(0)
    size = size_ref[p]
    transposed = (((1,), (1,)), ((), ()))
    splits = []
    for n in range(2):
        source = nb_ref[2 * p + n] // width
        slot = nb_ref[2 * p + n] % width
        left, own, right = (t_refs[k][slot] for k in range(3))
        splits.append(split_bf16(jnp.where(source == 0, left, jnp.where(source == 1, own, right))))
    acc_ref[...] = jnp.zeros((NPNO, NPNO), jnp.float32)
    for m in CLASS_SIZES:

        @pl.when(size == m)
        def _():
            total = None
            for n in range(2):
                side = margin_ref[0, n, :m, :]
                t_hi, t_lo = splits[n]
                inner = mm(side, t_hi) + mm(side, t_lo)
                w_hi, w_lo = split_bf16(fock_ref[2 * p + n] * inner)
                outer = mm(w_hi, side, transposed) + mm(w_lo, side, transposed)
                total = outer if total is None else total + outer
            acc_ref[:m, :m] = total

    denominator = col_ref[0] + row_ref[0]
    amplitudes = own_ref[0]
    residual = ex_ref[0] + denominator * amplitudes - acc_ref[...]
    if final:
        out_ref[0] = residual
    else:
        out_ref[0] = amplitudes - residual / denominator


def coupling_step(nb, sizes, fock, sources, margin, exchange, energy, own, final):
    column = energy.reshape(energy.shape[0], NPNO, 1)
    row = energy.reshape(energy.shape[0], 1, NPNO)
    pairs = own.shape[0]
    block = (1, NPNO, NPNO)

    whole = pl.BlockSpec((pairs, NPNO, NPNO), lambda i, q, s, f: (0, 0, 0))
    own_spec = pl.BlockSpec(block, lambda i, q, s, f: (i, 0, 0))
    grid_spec = pltpu.PrefetchScalarGridSpec(
        num_scalar_prefetch=3,
        grid=(pairs,),
        in_specs=[whole] * 3
        + [
            pl.BlockSpec((1, 2, NPNO, NPNO), lambda i, q, s, f: (i, 0, 0, 0)),
            own_spec,
            pl.BlockSpec((1, NPNO, 1), lambda i, q, s, f: (i, 0, 0)),
            pl.BlockSpec((1, 1, NPNO), lambda i, q, s, f: (i, 0, 0)),
            own_spec,
        ],
        out_specs=own_spec,
        scratch_shapes=[pltpu.VMEM((NPNO, NPNO), jnp.float32)],
    )
    flops = pairs * 2 * 4 * 2 * NPNO * NPNO * NPNO
    return pl.pallas_call(
        functools.partial(coupling_kernel, final=final, width=pairs),
        grid_spec=grid_spec,
        out_shape=jax.ShapeDtypeStruct((pairs, NPNO, NPNO), jnp.float32),
        cost_estimate=pl.CostEstimate(
            flops=flops,
            bytes_accessed=pairs * NPNO * NPNO * (2 * 4 + 2 * 2 + 3 * 4),
            transcendentals=0,
        ),
    )(nb, sizes, fock, *sources, margin, exchange, column, row, own)


def per_device(
    three_index,
    pno_coef,
    pair_orbitals,
    natural_orbital_class,
    pno_energy,
    margin,
    neighbour_pairs,
    fock_coupling,
):
    occ_dev = three_index.shape[0]
    pair_dev = pno_coef.shape[0]
    position = lax.axis_index("pair")
    sizes = class_size(natural_orbital_class)
    blocks = halo_sources(three_index, "pair")
    local_orbitals = (pair_orbitals - (position - 1) * occ_dev).astype(jnp.int32)
    partial_ints = partial_exchange(
        local_orbitals[:, 0] - occ_dev,
        local_orbitals[:, 1],
        sizes,
        blocks,
        jnp.swapaxes(pno_coef, 2, 3),
    )
    exchange_ints = sum_over_aux(partial_ints)
    denominator = pno_energy[:, :, None] + pno_energy[:, None, :]
    local_rows = (neighbour_pairs - (position - 1) * pair_dev).astype(jnp.int32).reshape(-1)
    fock = fock_coupling.reshape(-1)

    amplitudes = -(exchange_ints / denominator)
    for iteration in range(1, ITERS):
        amplitudes = coupling_step(
            local_rows, sizes, fock, halo_sources(amplitudes, "pair"), margin, exchange_ints,
            pno_energy, amplitudes, False,
        )
    residual = coupling_step(
        local_rows, sizes, fock, halo_sources(amplitudes, "pair"), margin, exchange_ints,
        pno_energy, amplitudes, True,
    )
    return (amplitudes, residual)


def solution(mesh):
    return jax.shard_map(
        per_device,
        mesh=mesh,
        in_specs=(
            P("pair", "aux", None),
            P("pair", None, None, None),
            P("pair", None),
            P("pair"),
            P("pair", None),
            P("pair", None, None, None),
            P("pair", None),
            P("pair", None),
        ),
        out_specs=(P("pair", None, None), P("pair", None, None)),
        check_vma=False,
    )
```

```python
import functools

import jax
import jax.numpy as jnp
from jax import lax
from jax.experimental import pallas as pl
from jax.experimental.pallas import tpu as pltpu
from jax.sharding import PartitionSpec as P

NPNO = 192
ITERS = 2
CLASS_SIZES = (NPNO // 6, NPNO // 3, 2 * NPNO // 3, NPNO)


def halo_sources(cells, axis):
    count = lax.axis_size(axis)
    ends = count - 1
    from_left = lax.ppermute(cells, axis, [(i, i + 1) for i in range(ends)])
    from_right = lax.ppermute(cells, axis, [(i + 1, i) for i in range(ends)])
    return (from_left, cells, from_right)


def halving_stream(piece, index, count, bits):
    for bit in bits:
        side = (index // bit) % 2
        half = piece.shape[0] // 2
        keep = lax.dynamic_slice_in_dim(piece, side * half, half, axis=0)
        send = lax.dynamic_slice_in_dim(piece, (1 - side) * half, half, axis=0)
        piece = keep + lax.ppermute(send, "aux", [(i, i ^ bit) for i in range(count)])
    for bit in reversed(bits):
        side = (index // bit) % 2
        other = lax.ppermute(piece, "aux", [(i, i ^ bit) for i in range(count)])
        length = piece.shape[0]
        full = jnp.zeros((2 * length,) + piece.shape[1:], piece.dtype)
        full = lax.dynamic_update_slice_in_dim(full, piece, side * length, axis=0)
        piece = lax.dynamic_update_slice_in_dim(full, other, (1 - side) * length, axis=0)
    return piece


def sum_over_aux(partial):
    count = lax.axis_size("aux")
    if count != 4 or partial.shape[0] % 8:
        return lax.psum(partial, "aux")
    index = lax.axis_index("aux")
    half = partial.shape[0] // 2
    first = halving_stream(partial[:half], index, count, (1, 2))
    second = halving_stream(partial[half:], index, count, (2, 1))
    return jnp.concatenate([first, second], axis=0)


def class_size(natural_orbital_class):
    return jnp.where(
        natural_orbital_class == 0,
        NPNO // 6,
        jnp.where(
            natural_orbital_class == 1,
            NPNO // 3,
            jnp.where(natural_orbital_class == 2, 2 * NPNO // 3, NPNO),
        ),
    ).astype(jnp.int32)


def exchange_kernel(lead_ref, trail_ref, size_ref, t_left, t_own, t_right, coef_ref, out_ref, *, occ):
    p = pl.program_id(0)
    size = size_ref[p]
    source = trail_ref[p] // occ
    slot = trail_ref[p] % occ
    x_trail = jnp.where(source == 0, t_left[slot], jnp.where(source == 1, t_own[slot], t_right[slot]))
    x_lead = t_own[lead_ref[p]]
    transposed = (((1,), (1,)), ((), ()))
    out_ref[0] = jnp.zeros((NPNO, NPNO), jnp.float32)
    for m in CLASS_SIZES:

        @pl.when(size == m)
        def _():
            first = coef_ref[0, 0, :m, :]
            second = coef_ref[0, 1, :m, :]
            left_t = lax.dot_general(first, x_lead, transposed, preferred_element_type=jnp.float32)
            right = lax.dot_general(x_trail, second, transposed, preferred_element_type=jnp.float32)
            out_ref[0, :m, :m] = jnp.dot(
                left_t.astype(jnp.bfloat16), right.astype(jnp.bfloat16), preferred_element_type=jnp.float32
            )


def partial_exchange(lead, trail, sizes, sources, coef_t):
    pairs = coef_t.shape[0]
    occ, nfit, npao = sources[1].shape
    whole = pl.BlockSpec((occ, nfit, npao), lambda i, a, b, s: (0, 0, 0))
    grid_spec = pltpu.PrefetchScalarGridSpec(
        num_scalar_prefetch=3,
        grid=(pairs,),
        in_specs=[
            whole,
            whole,
            whole,
            pl.BlockSpec((1, 2, NPNO, npao), lambda i, a, b, s: (i, 0, 0, 0)),
        ],
        out_specs=pl.BlockSpec((1, NPNO, NPNO), lambda i, a, b, s: (i, 0, 0)),
    )
    flops = pairs * (2 * 2 * nfit * npao * NPNO + 2 * nfit * NPNO * NPNO)
    return pl.pallas_call(
        functools.partial(exchange_kernel, occ=occ),
        grid_spec=grid_spec,
        out_shape=jax.ShapeDtypeStruct((pairs, NPNO, NPNO), jnp.float32),
        cost_estimate=pl.CostEstimate(
            flops=flops,
            bytes_accessed=pairs * (2 * nfit * npao * 2 + 2 * npao * NPNO * 2 + NPNO * NPNO * 4),
            transcendentals=0,
        ),
    )(lead, trail, sizes, *sources, coef_t)


def split_bf16(value):
    hi = value.astype(jnp.bfloat16)
    lo = (value - hi.astype(jnp.float32)).astype(jnp.bfloat16)
    return hi, lo


def mm(lhs, rhs, dims=(((1,), (0,)), ((), ()))):
    return lax.dot_general(lhs, rhs, dims, preferred_element_type=jnp.float32)


def coupling_kernel(nb_ref, size_ref, fock_ref, *refs, final, width, start):
    t_refs = refs[:3]
    margin_ref, ex_ref, col_ref, row_ref, own_ref, out_ref, acc_ref = refs[3:]
    p = pl.program_id(0) + start
    size = size_ref[p]
    transposed = (((1,), (1,)), ((), ()))
    splits = []
    for n in range(2):
        source = nb_ref[2 * p + n] // width
        slot = nb_ref[2 * p + n] % width
        left, own, right = (t_refs[k][slot] for k in range(3))
        splits.append(split_bf16(jnp.where(source == 0, left, jnp.where(source == 1, own, right))))
    acc_ref[...] = jnp.zeros((NPNO, NPNO), jnp.float32)
    for m in CLASS_SIZES:

        @pl.when(size == m)
        def _():
            total = None
            for n in range(2):
                side = margin_ref[0, n, :m, :]
                t_hi, t_lo = splits[n]
                inner = mm(side, t_hi) + mm(side, t_lo)
                w_hi, w_lo = split_bf16(fock_ref[2 * p + n] * inner)
                outer = mm(w_hi, side, transposed) + mm(w_lo, side, transposed)
                total = outer if total is None else total + outer
            acc_ref[:m, :m] = total

    denominator = col_ref[0] + row_ref[0]
    amplitudes = own_ref[0]
    residual = ex_ref[0] + denominator * amplitudes - acc_ref[...]
    if final:
        out_ref[0] = residual
    else:
        out_ref[0] = amplitudes - residual / denominator


def coupling_step(nb, sizes, fock, sources, margin, exchange, energy, own, final, start=0, count=None):
    pairs = own.shape[0]
    count = pairs if count is None else count
    column = energy.reshape(pairs, NPNO, 1)
    row = energy.reshape(pairs, 1, NPNO)
    block = (1, NPNO, NPNO)
    whole = pl.BlockSpec((pairs, NPNO, NPNO), lambda i, q, s, f: (0, 0, 0))
    own_spec = pl.BlockSpec(block, lambda i, q, s, f: (i + start, 0, 0))
    grid_spec = pltpu.PrefetchScalarGridSpec(
        num_scalar_prefetch=3,
        grid=(count,),
        in_specs=[whole] * 3
        + [
            pl.BlockSpec((1, 2, NPNO, NPNO), lambda i, q, s, f: (i + start, 0, 0, 0)),
            own_spec,
            pl.BlockSpec((1, NPNO, 1), lambda i, q, s, f: (i + start, 0, 0)),
            pl.BlockSpec((1, 1, NPNO), lambda i, q, s, f: (i + start, 0, 0)),
            own_spec,
        ],
        out_specs=pl.BlockSpec(block, lambda i, q, s, f: (i, 0, 0)),
        scratch_shapes=[pltpu.VMEM((NPNO, NPNO), jnp.float32)],
    )
    flops = count * 2 * 4 * 2 * NPNO * NPNO * NPNO
    return pl.pallas_call(
        functools.partial(coupling_kernel, final=final, width=pairs, start=start),
        grid_spec=grid_spec,
        out_shape=jax.ShapeDtypeStruct((count, NPNO, NPNO), jnp.float32),
        cost_estimate=pl.CostEstimate(
            flops=flops,
            bytes_accessed=count * NPNO * NPNO * (2 * 4 + 2 * 2 + 3 * 4),
            transcendentals=0,
        ),
    )(nb, sizes, fock, *sources, margin, exchange, column, row, own)


def joined_halo(parts, axis):
    received = [halo_sources(part, axis) for part in parts]
    return tuple(jnp.concatenate([r[k] for r in received], axis=0) for k in range(3))


def per_device(
    three_index,
    pno_coef,
    pair_orbitals,
    natural_orbital_class,
    pno_energy,
    margin,
    neighbour_pairs,
    fock_coupling,
):
    occ_dev = three_index.shape[0]
    pair_dev = pno_coef.shape[0]
    position = lax.axis_index("pair")
    sizes = class_size(natural_orbital_class)
    blocks = halo_sources(three_index, "pair")
    local_orbitals = (pair_orbitals - (position - 1) * occ_dev).astype(jnp.int32)
    partial_ints = partial_exchange(
        local_orbitals[:, 0] - occ_dev,
        local_orbitals[:, 1],
        sizes,
        blocks,
        jnp.swapaxes(pno_coef, 2, 3),
    )
    exchange_ints = sum_over_aux(partial_ints)
    denominator = pno_energy[:, :, None] + pno_energy[:, None, :]
    local_rows = (neighbour_pairs - (position - 1) * pair_dev).astype(jnp.int32).reshape(-1)
    fock = fock_coupling.reshape(-1)

    amplitudes = -(exchange_ints / denominator)
    sources = halo_sources(amplitudes, "pair")
    half = pair_dev // 2
    for iteration in range(1, ITERS):
        parts = [
            coupling_step(
                local_rows, sizes, fock, sources, margin, exchange_ints, pno_energy, amplitudes,
                False, start, half,
            )
            for start in (0, half)
        ]
        sources = joined_halo(parts, "pair")
        amplitudes = sources[1]
    residual = coupling_step(
        local_rows, sizes, fock, sources, margin, exchange_ints, pno_energy, amplitudes, True
    )
    return (amplitudes, residual)


def solution(mesh):
    return jax.shard_map(
        per_device,
        mesh=mesh,
        in_specs=(
            P("pair", "aux", None),
            P("pair", None, None, None),
            P("pair", None),
            P("pair"),
            P("pair", None),
            P("pair", None, None, None),
            P("pair", None),
            P("pair", None),
        ),
        out_specs=(P("pair", None, None), P("pair", None, None)),
        check_vma=False,
    )
```

```python
import functools

import jax
import jax.numpy as jnp
from jax import lax
from jax.experimental import pallas as pl
from jax.experimental.pallas import tpu as pltpu
from jax.sharding import PartitionSpec as P

NPNO = 192
ITERS = 2
CLASS_SIZES = (NPNO // 6, NPNO // 3, 2 * NPNO // 3, NPNO)


def halo_sources(cells, axis):
    count = lax.axis_size(axis)
    ends = count - 1
    from_left = lax.ppermute(cells, axis, [(i, i + 1) for i in range(ends)])
    from_right = lax.ppermute(cells, axis, [(i + 1, i) for i in range(ends)])
    return (from_left, cells, from_right)


def halving_stream(piece, index, count, bits):
    for bit in bits:
        side = (index // bit) % 2
        half = piece.shape[0] // 2
        keep = lax.dynamic_slice_in_dim(piece, side * half, half, axis=0)
        send = lax.dynamic_slice_in_dim(piece, (1 - side) * half, half, axis=0)
        piece = keep + lax.ppermute(send, "aux", [(i, i ^ bit) for i in range(count)])
    for bit in reversed(bits):
        side = (index // bit) % 2
        other = lax.ppermute(piece, "aux", [(i, i ^ bit) for i in range(count)])
        length = piece.shape[0]
        full = jnp.zeros((2 * length,) + piece.shape[1:], piece.dtype)
        full = lax.dynamic_update_slice_in_dim(full, piece, side * length, axis=0)
        piece = lax.dynamic_update_slice_in_dim(full, other, (1 - side) * length, axis=0)
    return piece


def sum_over_aux(partial):
    count = lax.axis_size("aux")
    if count != 4 or partial.shape[0] % 8:
        return lax.psum(partial, "aux")
    index = lax.axis_index("aux")
    half = partial.shape[0] // 2
    first = halving_stream(partial[:half], index, count, (1, 2))
    second = halving_stream(partial[half:], index, count, (2, 1))
    return jnp.concatenate([first, second], axis=0)


def class_size(natural_orbital_class):
    return jnp.where(
        natural_orbital_class == 0,
        NPNO // 6,
        jnp.where(
            natural_orbital_class == 1,
            NPNO // 3,
            jnp.where(natural_orbital_class == 2, 2 * NPNO // 3, NPNO),
        ),
    ).astype(jnp.int32)


def fetch_block(sources, width, local, dst, sem):
    source = local // width
    block = local % width
    conditions = (source == 0, (source != 0) & (source != 2), source == 2)
    for src, condition in zip(sources, conditions):

        @pl.when(condition)
        def _():
            pltpu.make_async_copy(src.at[block], dst, sem).start()


def exchange_kernel(
    lead_ref, trail_ref, size_ref, x_lead, t_left, t_own, t_right, coef_ref, out_ref, xbuf, sems, *, occ
):
    i = pl.program_id(0)
    steps = pl.num_programs(0)
    sources = (t_left, t_own, t_right)

    @pl.when(i == 0)
    def _():
        fetch_block(sources, occ, trail_ref[0], xbuf.at[0], sems.at[0])

    @pl.when(i + 1 < steps)
    def _():
        fetch_block(sources, occ, trail_ref[i + 1], xbuf.at[(i + 1) % 2], sems.at[(i + 1) % 2])

    slot = i % 2
    pltpu.make_async_copy(t_own.at[0], xbuf.at[slot], sems.at[slot]).wait()
    size = size_ref[i]
    transposed = (((1,), (1,)), ((), ()))
    out_ref[0] = jnp.zeros((NPNO, NPNO), jnp.float32)
    for m in CLASS_SIZES:

        @pl.when(size == m)
        def _():
            first = coef_ref[0, 0, :m, :]
            second = coef_ref[0, 1, :m, :]
            left_t = lax.dot_general(first, x_lead[0], transposed, preferred_element_type=jnp.float32)
            right = lax.dot_general(xbuf[slot], second, transposed, preferred_element_type=jnp.float32)
            out_ref[0, :m, :m] = jnp.dot(
                left_t.astype(jnp.bfloat16), right.astype(jnp.bfloat16), preferred_element_type=jnp.float32
            )


def partial_exchange(lead, trail, sizes, sources, coef_t):
    pairs = coef_t.shape[0]
    occ, nfit, npao = sources[1].shape
    hbm = pl.BlockSpec(memory_space=pl.ANY)
    grid_spec = pltpu.PrefetchScalarGridSpec(
        num_scalar_prefetch=3,
        grid=(pairs,),
        in_specs=[
            pl.BlockSpec((1, nfit, npao), lambda i, a, b, s: (a[i], 0, 0)),
            hbm,
            hbm,
            hbm,
            pl.BlockSpec((1, 2, NPNO, npao), lambda i, a, b, s: (i, 0, 0, 0)),
        ],
        out_specs=pl.BlockSpec((1, NPNO, NPNO), lambda i, a, b, s: (i, 0, 0)),
        scratch_shapes=[
            pltpu.VMEM((2, nfit, npao), sources[1].dtype),
            pltpu.SemaphoreType.DMA((2,)),
        ],
    )
    flops = pairs * (2 * 2 * nfit * npao * NPNO + 2 * nfit * NPNO * NPNO)
    return pl.pallas_call(
        functools.partial(exchange_kernel, occ=occ),
        grid_spec=grid_spec,
        out_shape=jax.ShapeDtypeStruct((pairs, NPNO, NPNO), jnp.float32),
        cost_estimate=pl.CostEstimate(
            flops=flops,
            bytes_accessed=pairs * (2 * nfit * npao * 2 + 2 * npao * NPNO * 2 + NPNO * NPNO * 4),
            transcendentals=0,
        ),
    )(lead, trail, sizes, sources[1], *sources, coef_t)


def split_bf16(value):
    hi = value.astype(jnp.bfloat16)
    lo = (value - hi.astype(jnp.float32)).astype(jnp.bfloat16)
    return hi, lo


def mm(lhs, rhs, dims=(((1,), (0,)), ((), ()))):
    return lax.dot_general(lhs, rhs, dims, preferred_element_type=jnp.float32)


def coupling_kernel(nb_ref, size_ref, fock_ref, *refs, final, width):
    sources = refs[:3]
    margin_ref, ex_ref, col_ref, row_ref, own_ref, out_ref, tbuf, sems, acc_ref = refs[3:]
    i = pl.program_id(0)
    steps = pl.num_programs(0)

    def fetch(step, slot):
        for n in range(2):
            fetch_block(sources, width, nb_ref[2 * step + n], tbuf.at[slot, n], sems.at[slot, n])

    @pl.when(i == 0)
    def _():
        fetch(0, 0)

    @pl.when(i + 1 < steps)
    def _():
        fetch(i + 1, (i + 1) % 2)

    slot = i % 2
    splits = []
    for n in range(2):
        pltpu.make_async_copy(sources[1].at[0], tbuf.at[slot, n], sems.at[slot, n]).wait()
        splits.append(split_bf16(tbuf[slot, n]))
    size = size_ref[i]
    transposed = (((1,), (1,)), ((), ()))
    acc_ref[...] = jnp.zeros((NPNO, NPNO), jnp.float32)
    for m in CLASS_SIZES:

        @pl.when(size == m)
        def _():
            total = None
            for n in range(2):
                side = margin_ref[0, n, :m, :]
                t_hi, t_lo = splits[n]
                inner = mm(side, t_hi) + mm(side, t_lo)
                w_hi, w_lo = split_bf16(fock_ref[2 * i + n] * inner)
                outer = mm(w_hi, side, transposed) + mm(w_lo, side, transposed)
                total = outer if total is None else total + outer
            acc_ref[:m, :m] = total

    denominator = col_ref[0] + row_ref[0]
    amplitudes = own_ref[0]
    residual = ex_ref[0] + denominator * amplitudes - acc_ref[...]
    if final:
        out_ref[0] = residual
    else:
        out_ref[0] = amplitudes - residual / denominator


def coupling_step(nb, sizes, fock, sources, margin, exchange, energy, own, final):
    pairs = own.shape[0]
    column = energy.reshape(pairs, NPNO, 1)
    row = energy.reshape(pairs, 1, NPNO)
    block = (1, NPNO, NPNO)
    hbm = pl.BlockSpec(memory_space=pl.ANY)
    own_spec = pl.BlockSpec(block, lambda i, q, s, f: (i, 0, 0))
    grid_spec = pltpu.PrefetchScalarGridSpec(
        num_scalar_prefetch=3,
        grid=(pairs,),
        in_specs=[hbm] * 3
        + [
            pl.BlockSpec((1, 2, NPNO, NPNO), lambda i, q, s, f: (i, 0, 0, 0)),
            own_spec,
            pl.BlockSpec((1, NPNO, 1), lambda i, q, s, f: (i, 0, 0)),
            pl.BlockSpec((1, 1, NPNO), lambda i, q, s, f: (i, 0, 0)),
            own_spec,
        ],
        out_specs=own_spec,
        scratch_shapes=[
            pltpu.VMEM((2, 2, NPNO, NPNO), jnp.float32),
            pltpu.SemaphoreType.DMA((2, 2)),
            pltpu.VMEM((NPNO, NPNO), jnp.float32),
        ],
    )
    flops = pairs * 2 * 4 * 2 * NPNO * NPNO * NPNO
    return pl.pallas_call(
        functools.partial(coupling_kernel, final=final, width=pairs),
        grid_spec=grid_spec,
        out_shape=jax.ShapeDtypeStruct((pairs, NPNO, NPNO), jnp.float32),
        cost_estimate=pl.CostEstimate(
            flops=flops,
            bytes_accessed=pairs * NPNO * NPNO * (2 * 4 + 2 * 2 + 3 * 4),
            transcendentals=0,
        ),
    )(nb, sizes, fock, *sources, margin, exchange, column, row, own)


def per_device(
    three_index,
    pno_coef,
    pair_orbitals,
    natural_orbital_class,
    pno_energy,
    margin,
    neighbour_pairs,
    fock_coupling,
):
    occ_dev = three_index.shape[0]
    pair_dev = pno_coef.shape[0]
    position = lax.axis_index("pair")
    sizes = class_size(natural_orbital_class)
    blocks = halo_sources(three_index, "pair")
    local_orbitals = (pair_orbitals - (position - 1) * occ_dev).astype(jnp.int32)
    partial_ints = partial_exchange(
        local_orbitals[:, 0] - occ_dev,
        local_orbitals[:, 1],
        sizes,
        blocks,
        jnp.swapaxes(pno_coef, 2, 3),
    )
    exchange_ints = sum_over_aux(partial_ints)
    denominator = pno_energy[:, :, None] + pno_energy[:, None, :]
    local_rows = (neighbour_pairs - (position - 1) * pair_dev).astype(jnp.int32).reshape(-1)
    fock = fock_coupling.reshape(-1)

    amplitudes = -(exchange_ints / denominator)
    for iteration in range(1, ITERS):
        amplitudes = coupling_step(
            local_rows, sizes, fock, halo_sources(amplitudes, "pair"), margin, exchange_ints,
            pno_energy, amplitudes, False,
        )
    residual = coupling_step(
        local_rows, sizes, fock, halo_sources(amplitudes, "pair"), margin, exchange_ints,
        pno_energy, amplitudes, True,
    )
    return (amplitudes, residual)


def solution(mesh):
    return jax.shard_map(
        per_device,
        mesh=mesh,
        in_specs=(
            P("pair", "aux", None),
            P("pair", None, None, None),
            P("pair", None),
            P("pair"),
            P("pair", None),
            P("pair", None, None, None),
            P("pair", None),
            P("pair", None),
        ),
        out_specs=(P("pair", None, None), P("pair", None, None)),
        check_vma=False,
    )
```

```python
import functools

import jax
import jax.numpy as jnp
from jax import lax
from jax.experimental import pallas as pl
from jax.experimental.pallas import tpu as pltpu
from jax.sharding import PartitionSpec as P

NPNO = 192
ITERS = 2
CLASS_SIZES = (NPNO // 6, NPNO // 3, 2 * NPNO // 3, NPNO)


def halo_sources(cells, axis):
    count = lax.axis_size(axis)
    ends = count - 1
    from_left = lax.ppermute(cells, axis, [(i, i + 1) for i in range(ends)])
    from_right = lax.ppermute(cells, axis, [(i + 1, i) for i in range(ends)])
    return (from_left, cells, from_right)


def halving_stream(piece, index, count, bits):
    for bit in bits:
        side = (index // bit) % 2
        half = piece.shape[0] // 2
        keep = lax.dynamic_slice_in_dim(piece, side * half, half, axis=0)
        send = lax.dynamic_slice_in_dim(piece, (1 - side) * half, half, axis=0)
        piece = keep + lax.ppermute(send, "aux", [(i, i ^ bit) for i in range(count)])
    for bit in reversed(bits):
        side = (index // bit) % 2
        other = lax.ppermute(piece, "aux", [(i, i ^ bit) for i in range(count)])
        length = piece.shape[0]
        full = jnp.zeros((2 * length,) + piece.shape[1:], piece.dtype)
        full = lax.dynamic_update_slice_in_dim(full, piece, side * length, axis=0)
        piece = lax.dynamic_update_slice_in_dim(full, other, (1 - side) * length, axis=0)
    return piece


def sum_over_aux(partial):
    count = lax.axis_size("aux")
    if count != 4 or partial.shape[0] % 8:
        return lax.psum(partial, "aux")
    index = lax.axis_index("aux")
    half = partial.shape[0] // 2
    first = halving_stream(partial[:half], index, count, (1, 2))
    second = halving_stream(partial[half:], index, count, (2, 1))
    return jnp.concatenate([first, second], axis=0)


def class_size(natural_orbital_class):
    return jnp.where(
        natural_orbital_class == 0,
        NPNO // 6,
        jnp.where(
            natural_orbital_class == 1,
            NPNO // 3,
            jnp.where(natural_orbital_class == 2, 2 * NPNO // 3, NPNO),
        ),
    ).astype(jnp.int32)


def fetch_block(sources, width, local, dst, sem):
    source = local // width
    block = local % width
    conditions = (source == 0, (source != 0) & (source != 2), source == 2)
    for src, condition in zip(sources, conditions):

        @pl.when(condition)
        def _():
            pltpu.make_async_copy(src.at[block], dst, sem).start()


def exchange_kernel(
    lead_ref, trail_ref, size_ref, x_lead, t_left, t_own, t_right, coef_ref, out_ref, xbuf, sems, *, occ
):
    i = pl.program_id(0)
    steps = pl.num_programs(0)
    sources = (t_left, t_own, t_right)

    @pl.when(i == 0)
    def _():
        fetch_block(sources, occ, trail_ref[0], xbuf.at[0], sems.at[0])

    @pl.when(i + 1 < steps)
    def _():
        fetch_block(sources, occ, trail_ref[i + 1], xbuf.at[(i + 1) % 2], sems.at[(i + 1) % 2])

    slot = i % 2
    pltpu.make_async_copy(t_own.at[0], xbuf.at[slot], sems.at[slot]).wait()
    size = size_ref[i]
    transposed = (((1,), (1,)), ((), ()))
    out_ref[0] = jnp.zeros((NPNO, NPNO), jnp.float32)
    for m in CLASS_SIZES:

        @pl.when(size == m)
        def _():
            first = coef_ref[0, 0, :m, :]
            second = coef_ref[0, 1, :m, :]
            left_t = lax.dot_general(first, x_lead[0], transposed, preferred_element_type=jnp.float32)
            right = lax.dot_general(xbuf[slot], second, transposed, preferred_element_type=jnp.float32)
            out_ref[0, :m, :m] = jnp.dot(
                left_t.astype(jnp.bfloat16), right.astype(jnp.bfloat16), preferred_element_type=jnp.float32
            )


def partial_exchange(lead, trail, sizes, sources, coef_t):
    pairs = coef_t.shape[0]
    occ, nfit, npao = sources[1].shape
    hbm = pl.BlockSpec(memory_space=pl.ANY)
    grid_spec = pltpu.PrefetchScalarGridSpec(
        num_scalar_prefetch=3,
        grid=(pairs,),
        in_specs=[
            pl.BlockSpec((1, nfit, npao), lambda i, a, b, s: (a[i], 0, 0)),
            hbm,
            hbm,
            hbm,
            pl.BlockSpec((1, 2, NPNO, npao), lambda i, a, b, s: (i, 0, 0, 0)),
        ],
        out_specs=pl.BlockSpec((1, NPNO, NPNO), lambda i, a, b, s: (i, 0, 0)),
        scratch_shapes=[
            pltpu.VMEM((2, nfit, npao), sources[1].dtype),
            pltpu.SemaphoreType.DMA((2,)),
        ],
    )
    flops = pairs * (2 * 2 * nfit * npao * NPNO + 2 * nfit * NPNO * NPNO)
    return pl.pallas_call(
        functools.partial(exchange_kernel, occ=occ),
        grid_spec=grid_spec,
        out_shape=jax.ShapeDtypeStruct((pairs, NPNO, NPNO), jnp.float32),
        cost_estimate=pl.CostEstimate(
            flops=flops,
            bytes_accessed=pairs * (2 * nfit * npao * 2 + 2 * npao * NPNO * 2 + NPNO * NPNO * 4),
            transcendentals=0,
        ),
    )(lead, trail, sizes, sources[1], *sources, coef_t)


def split_bf16(value):
    hi = value.astype(jnp.bfloat16)
    lo = (value - hi.astype(jnp.float32)).astype(jnp.bfloat16)
    return hi, lo


def mm(lhs, rhs, dims=(((1,), (0,)), ((), ()))):
    return lax.dot_general(lhs, rhs, dims, preferred_element_type=jnp.float32)


def coupling_kernel(nb_ref, size_ref, fock_ref, *refs, final, width, group):
    sources = refs[:3]
    margin_ref, ex_ref, col_ref, row_ref, own_ref, out_ref, tbuf, sems, acc_ref = refs[3:]
    i = pl.program_id(0)
    steps = pl.num_programs(0)

    def fetch(step, slot):
        for k in range(2 * group):
            fetch_block(sources, width, nb_ref[2 * group * step + k], tbuf.at[slot, k], sems.at[slot, k])

    @pl.when(i == 0)
    def _():
        fetch(0, 0)

    @pl.when(i + 1 < steps)
    def _():
        fetch(i + 1, (i + 1) % 2)

    slot = i % 2
    transposed = (((1,), (1,)), ((), ()))
    for g in range(group):
        p = i * group + g
        splits = []
        for n in range(2):
            k = 2 * g + n
            pltpu.make_async_copy(sources[1].at[0], tbuf.at[slot, k], sems.at[slot, k]).wait()
            splits.append(split_bf16(tbuf[slot, k]))
        size = size_ref[p]
        acc_ref[...] = jnp.zeros((NPNO, NPNO), jnp.float32)
        for m in CLASS_SIZES:

            @pl.when(size == m)
            def _():
                total = None
                for n in range(2):
                    side = margin_ref[g, n, :m, :]
                    t_hi, t_lo = splits[n]
                    inner = mm(side, t_hi) + mm(side, t_lo)
                    w_hi, w_lo = split_bf16(fock_ref[2 * p + n] * inner)
                    outer = mm(w_hi, side, transposed) + mm(w_lo, side, transposed)
                    total = outer if total is None else total + outer
                acc_ref[:m, :m] = total

        denominator = col_ref[g] + row_ref[g]
        amplitudes = own_ref[g]
        residual = ex_ref[g] + denominator * amplitudes - acc_ref[...]
        if final:
            out_ref[g] = residual
        else:
            out_ref[g] = amplitudes - residual / denominator


def coupling_step(nb, sizes, fock, sources, margin, exchange, energy, own, final):
    pairs = own.shape[0]
    group = next(g for g in (4, 2, 1) if pairs % g == 0)
    column = energy.reshape(pairs, NPNO, 1)
    row = energy.reshape(pairs, 1, NPNO)
    hbm = pl.BlockSpec(memory_space=pl.ANY)
    own_spec = pl.BlockSpec((group, NPNO, NPNO), lambda i, q, s, f: (i, 0, 0))
    grid_spec = pltpu.PrefetchScalarGridSpec(
        num_scalar_prefetch=3,
        grid=(pairs // group,),
        in_specs=[hbm] * 3
        + [
            pl.BlockSpec((group, 2, NPNO, NPNO), lambda i, q, s, f: (i, 0, 0, 0)),
            own_spec,
            pl.BlockSpec((group, NPNO, 1), lambda i, q, s, f: (i, 0, 0)),
            pl.BlockSpec((group, 1, NPNO), lambda i, q, s, f: (i, 0, 0)),
            own_spec,
        ],
        out_specs=own_spec,
        scratch_shapes=[
            pltpu.VMEM((2, 2 * group, NPNO, NPNO), jnp.float32),
            pltpu.SemaphoreType.DMA((2, 2 * group)),
            pltpu.VMEM((NPNO, NPNO), jnp.float32),
        ],
    )
    flops = pairs * 2 * 4 * 2 * NPNO * NPNO * NPNO
    return pl.pallas_call(
        functools.partial(coupling_kernel, final=final, width=pairs, group=group),
        grid_spec=grid_spec,
        out_shape=jax.ShapeDtypeStruct((pairs, NPNO, NPNO), jnp.float32),
        cost_estimate=pl.CostEstimate(
            flops=flops,
            bytes_accessed=pairs * NPNO * NPNO * (2 * 4 + 2 * 2 + 3 * 4),
            transcendentals=0,
        ),
    )(nb, sizes, fock, *sources, margin, exchange, column, row, own)


def per_device(
    three_index,
    pno_coef,
    pair_orbitals,
    natural_orbital_class,
    pno_energy,
    margin,
    neighbour_pairs,
    fock_coupling,
):
    occ_dev = three_index.shape[0]
    pair_dev = pno_coef.shape[0]
    position = lax.axis_index("pair")
    sizes = class_size(natural_orbital_class)
    blocks = halo_sources(three_index, "pair")
    local_orbitals = (pair_orbitals - (position - 1) * occ_dev).astype(jnp.int32)
    partial_ints = partial_exchange(
        local_orbitals[:, 0] - occ_dev,
        local_orbitals[:, 1],
        sizes,
        blocks,
        jnp.swapaxes(pno_coef, 2, 3),
    )
    exchange_ints = sum_over_aux(partial_ints)
    denominator = pno_energy[:, :, None] + pno_energy[:, None, :]
    local_rows = (neighbour_pairs - (position - 1) * pair_dev).astype(jnp.int32).reshape(-1)
    fock = fock_coupling.reshape(-1)

    amplitudes = -(exchange_ints / denominator)
    for iteration in range(1, ITERS):
        amplitudes = coupling_step(
            local_rows, sizes, fock, halo_sources(amplitudes, "pair"), margin, exchange_ints,
            pno_energy, amplitudes, False,
        )
    residual = coupling_step(
        local_rows, sizes, fock, halo_sources(amplitudes, "pair"), margin, exchange_ints,
        pno_energy, amplitudes, True,
    )
    return (amplitudes, residual)


def solution(mesh):
    return jax.shard_map(
        per_device,
        mesh=mesh,
        in_specs=(
            P("pair", "aux", None),
            P("pair", None, None, None),
            P("pair", None),
            P("pair"),
            P("pair", None),
            P("pair", None, None, None),
            P("pair", None),
            P("pair", None),
        ),
        out_specs=(P("pair", None, None), P("pair", None, None)),
        check_vma=False,
    )
```

```python
import functools

import jax
import jax.numpy as jnp
from jax import lax
from jax.experimental import pallas as pl
from jax.experimental.pallas import tpu as pltpu
from jax.sharding import PartitionSpec as P

NPNO = 192
ITERS = 2
CLASS_SIZES = (NPNO // 6, NPNO // 3, 2 * NPNO // 3, NPNO)


def halo_sources(cells, axis):
    count = lax.axis_size(axis)
    ends = count - 1
    from_left = lax.ppermute(cells, axis, [(i, i + 1) for i in range(ends)])
    from_right = lax.ppermute(cells, axis, [(i + 1, i) for i in range(ends)])
    return (from_left, cells, from_right)


def halving_stream(piece, index, count, bits):
    for bit in bits:
        side = (index // bit) % 2
        half = piece.shape[0] // 2
        keep = lax.dynamic_slice_in_dim(piece, side * half, half, axis=0)
        send = lax.dynamic_slice_in_dim(piece, (1 - side) * half, half, axis=0)
        piece = keep + lax.ppermute(send, "aux", [(i, i ^ bit) for i in range(count)])
    for bit in reversed(bits):
        side = (index // bit) % 2
        other = lax.ppermute(piece, "aux", [(i, i ^ bit) for i in range(count)])
        length = piece.shape[0]
        full = jnp.zeros((2 * length,) + piece.shape[1:], piece.dtype)
        full = lax.dynamic_update_slice_in_dim(full, piece, side * length, axis=0)
        piece = lax.dynamic_update_slice_in_dim(full, other, (1 - side) * length, axis=0)
    return piece


def sum_over_aux(partial):
    count = lax.axis_size("aux")
    if count != 4 or partial.shape[0] % 8:
        return lax.psum(partial, "aux")
    index = lax.axis_index("aux")
    half = partial.shape[0] // 2
    first = halving_stream(partial[:half], index, count, (1, 2))
    second = halving_stream(partial[half:], index, count, (2, 1))
    return jnp.concatenate([first, second], axis=0)


def class_size(natural_orbital_class):
    return jnp.where(
        natural_orbital_class == 0,
        NPNO // 6,
        jnp.where(
            natural_orbital_class == 1,
            NPNO // 3,
            jnp.where(natural_orbital_class == 2, 2 * NPNO // 3, NPNO),
        ),
    ).astype(jnp.int32)


def fetch_block(sources, width, local, dst, sem):
    source = local // width
    block = local % width
    conditions = (source == 0, (source != 0) & (source != 2), source == 2)
    for src, condition in zip(sources, conditions):

        @pl.when(condition)
        def _():
            pltpu.make_async_copy(src.at[block], dst, sem).start()


def exchange_kernel(
    lead_ref, trail_ref, size_ref, t_left, t_own, t_right, coef_ref, out_ref, lbuf, tbuf, sems, *, occ, group
):
    i = pl.program_id(0)
    steps = pl.num_programs(0)
    sources = (t_left, t_own, t_right)

    def fetch(step, slot):
        for g in range(group):
            p = step * group + g
            pltpu.make_async_copy(t_own.at[lead_ref[p] % occ], lbuf.at[slot, g], sems.at[slot, 0, g]).start()
            fetch_block(sources, occ, trail_ref[p], tbuf.at[slot, g], sems.at[slot, 1, g])

    @pl.when(i == 0)
    def _():
        fetch(0, 0)

    @pl.when(i + 1 < steps)
    def _():
        fetch(i + 1, (i + 1) % 2)

    slot = i % 2
    transposed = (((1,), (1,)), ((), ()))
    for g in range(group):
        p = i * group + g
        pltpu.make_async_copy(t_own.at[0], lbuf.at[slot, g], sems.at[slot, 0, g]).wait()
        pltpu.make_async_copy(t_own.at[0], tbuf.at[slot, g], sems.at[slot, 1, g]).wait()
        size = size_ref[p]
        out_ref[g] = jnp.zeros((NPNO, NPNO), jnp.float32)
        for m in CLASS_SIZES:

            @pl.when(size == m)
            def _():
                first = coef_ref[g, 0, :m, :]
                second = coef_ref[g, 1, :m, :]
                left_t = lax.dot_general(first, lbuf[slot, g], transposed, preferred_element_type=jnp.float32)
                right = lax.dot_general(tbuf[slot, g], second, transposed, preferred_element_type=jnp.float32)
                out_ref[g, :m, :m] = jnp.dot(
                    left_t.astype(jnp.bfloat16), right.astype(jnp.bfloat16), preferred_element_type=jnp.float32
                )


def partial_exchange(lead, trail, sizes, sources, coef_t):
    pairs = coef_t.shape[0]
    group = next(g for g in (4, 2, 1) if pairs % g == 0)
    occ, nfit, npao = sources[1].shape
    hbm = pl.BlockSpec(memory_space=pl.ANY)
    grid_spec = pltpu.PrefetchScalarGridSpec(
        num_scalar_prefetch=3,
        grid=(pairs // group,),
        in_specs=[
            hbm,
            hbm,
            hbm,
            pl.BlockSpec((group, 2, NPNO, npao), lambda i, a, b, s: (i, 0, 0, 0)),
        ],
        out_specs=pl.BlockSpec((group, NPNO, NPNO), lambda i, a, b, s: (i, 0, 0)),
        scratch_shapes=[
            pltpu.VMEM((2, group, nfit, npao), sources[1].dtype),
            pltpu.VMEM((2, group, nfit, npao), sources[1].dtype),
            pltpu.SemaphoreType.DMA((2, 2, group)),
        ],
    )
    flops = pairs * (2 * 2 * nfit * npao * NPNO + 2 * nfit * NPNO * NPNO)
    return pl.pallas_call(
        functools.partial(exchange_kernel, occ=occ, group=group),
        grid_spec=grid_spec,
        out_shape=jax.ShapeDtypeStruct((pairs, NPNO, NPNO), jnp.float32),
        cost_estimate=pl.CostEstimate(
            flops=flops,
            bytes_accessed=pairs * (2 * nfit * npao * 2 + 2 * npao * NPNO * 2 + NPNO * NPNO * 4),
            transcendentals=0,
        ),
    )(lead, trail, sizes, *sources, coef_t)


def split_bf16(value):
    hi = value.astype(jnp.bfloat16)
    lo = (value - hi.astype(jnp.float32)).astype(jnp.bfloat16)
    return hi, lo


def mm(lhs, rhs, dims=(((1,), (0,)), ((), ()))):
    return lax.dot_general(lhs, rhs, dims, preferred_element_type=jnp.float32)


def coupling_kernel(nb_ref, size_ref, fock_ref, *refs, final, width, group):
    sources = refs[:3]
    margin_ref, ex_ref, col_ref, row_ref, own_ref, out_ref, tbuf, sems, acc_ref = refs[3:]
    i = pl.program_id(0)
    steps = pl.num_programs(0)

    def fetch(step, slot):
        for k in range(2 * group):
            fetch_block(sources, width, nb_ref[2 * group * step + k], tbuf.at[slot, k], sems.at[slot, k])

    @pl.when(i == 0)
    def _():
        fetch(0, 0)

    @pl.when(i + 1 < steps)
    def _():
        fetch(i + 1, (i + 1) % 2)

    slot = i % 2
    transposed = (((1,), (1,)), ((), ()))
    for g in range(group):
        p = i * group + g
        splits = []
        for n in range(2):
            k = 2 * g + n
            pltpu.make_async_copy(sources[1].at[0], tbuf.at[slot, k], sems.at[slot, k]).wait()
            splits.append(split_bf16(tbuf[slot, k]))
        size = size_ref[p]
        acc_ref[...] = jnp.zeros((NPNO, NPNO), jnp.float32)
        for m in CLASS_SIZES:

            @pl.when(size == m)
            def _():
                total = None
                for n in range(2):
                    side = margin_ref[g, n, :m, :]
                    t_hi, t_lo = splits[n]
                    inner = mm(side, t_hi) + mm(side, t_lo)
                    w_hi, w_lo = split_bf16(fock_ref[2 * p + n] * inner)
                    outer = mm(w_hi, side, transposed) + mm(w_lo, side, transposed)
                    total = outer if total is None else total + outer
                acc_ref[:m, :m] = total

        denominator = col_ref[g] + row_ref[g]
        amplitudes = own_ref[g]
        residual = ex_ref[g] + denominator * amplitudes - acc_ref[...]
        if final:
            out_ref[g] = residual
        else:
            out_ref[g] = amplitudes - residual / denominator


def coupling_step(nb, sizes, fock, sources, margin, exchange, energy, own, final):
    pairs = own.shape[0]
    group = next(g for g in (4, 2, 1) if pairs % g == 0)
    column = energy.reshape(pairs, NPNO, 1)
    row = energy.reshape(pairs, 1, NPNO)
    hbm = pl.BlockSpec(memory_space=pl.ANY)
    own_spec = pl.BlockSpec((group, NPNO, NPNO), lambda i, q, s, f: (i, 0, 0))
    grid_spec = pltpu.PrefetchScalarGridSpec(
        num_scalar_prefetch=3,
        grid=(pairs // group,),
        in_specs=[hbm] * 3
        + [
            pl.BlockSpec((group, 2, NPNO, NPNO), lambda i, q, s, f: (i, 0, 0, 0)),
            own_spec,
            pl.BlockSpec((group, NPNO, 1), lambda i, q, s, f: (i, 0, 0)),
            pl.BlockSpec((group, 1, NPNO), lambda i, q, s, f: (i, 0, 0)),
            own_spec,
        ],
        out_specs=own_spec,
        scratch_shapes=[
            pltpu.VMEM((2, 2 * group, NPNO, NPNO), jnp.float32),
            pltpu.SemaphoreType.DMA((2, 2 * group)),
            pltpu.VMEM((NPNO, NPNO), jnp.float32),
        ],
    )
    flops = pairs * 2 * 4 * 2 * NPNO * NPNO * NPNO
    return pl.pallas_call(
        functools.partial(coupling_kernel, final=final, width=pairs, group=group),
        grid_spec=grid_spec,
        out_shape=jax.ShapeDtypeStruct((pairs, NPNO, NPNO), jnp.float32),
        cost_estimate=pl.CostEstimate(
            flops=flops,
            bytes_accessed=pairs * NPNO * NPNO * (2 * 4 + 2 * 2 + 3 * 4),
            transcendentals=0,
        ),
    )(nb, sizes, fock, *sources, margin, exchange, column, row, own)


def per_device(
    three_index,
    pno_coef,
    pair_orbitals,
    natural_orbital_class,
    pno_energy,
    margin,
    neighbour_pairs,
    fock_coupling,
):
    occ_dev = three_index.shape[0]
    pair_dev = pno_coef.shape[0]
    position = lax.axis_index("pair")
    sizes = class_size(natural_orbital_class)
    blocks = halo_sources(three_index, "pair")
    local_orbitals = (pair_orbitals - (position - 1) * occ_dev).astype(jnp.int32)
    partial_ints = partial_exchange(
        local_orbitals[:, 0] - occ_dev,
        local_orbitals[:, 1],
        sizes,
        blocks,
        jnp.swapaxes(pno_coef, 2, 3),
    )
    exchange_ints = sum_over_aux(partial_ints)
    denominator = pno_energy[:, :, None] + pno_energy[:, None, :]
    local_rows = (neighbour_pairs - (position - 1) * pair_dev).astype(jnp.int32).reshape(-1)
    fock = fock_coupling.reshape(-1)

    amplitudes = -(exchange_ints / denominator)
    for iteration in range(1, ITERS):
        amplitudes = coupling_step(
            local_rows, sizes, fock, halo_sources(amplitudes, "pair"), margin, exchange_ints,
            pno_energy, amplitudes, False,
        )
    residual = coupling_step(
        local_rows, sizes, fock, halo_sources(amplitudes, "pair"), margin, exchange_ints,
        pno_energy, amplitudes, True,
    )
    return (amplitudes, residual)


def solution(mesh):
    return jax.shard_map(
        per_device,
        mesh=mesh,
        in_specs=(
            P("pair", "aux", None),
            P("pair", None, None, None),
            P("pair", None),
            P("pair"),
            P("pair", None),
            P("pair", None, None, None),
            P("pair", None),
            P("pair", None),
        ),
        out_specs=(P("pair", None, None), P("pair", None, None)),
        check_vma=False,
    )
```

```python
import functools

import jax
import jax.numpy as jnp
from jax import lax
from jax.experimental import pallas as pl
from jax.experimental.pallas import tpu as pltpu
from jax.sharding import PartitionSpec as P

NPNO = 192
ITERS = 2
CLASS_SIZES = (NPNO // 6, NPNO // 3, 2 * NPNO // 3, NPNO)


def halo_sources(cells, axis):
    count = lax.axis_size(axis)
    ends = count - 1
    from_left = lax.ppermute(cells, axis, [(i, i + 1) for i in range(ends)])
    from_right = lax.ppermute(cells, axis, [(i + 1, i) for i in range(ends)])
    return (from_left, cells, from_right)


def halving_stream(piece, index, count, bits):
    for bit in bits:
        side = (index // bit) % 2
        half = piece.shape[0] // 2
        keep = lax.dynamic_slice_in_dim(piece, side * half, half, axis=0)
        send = lax.dynamic_slice_in_dim(piece, (1 - side) * half, half, axis=0)
        piece = keep + lax.ppermute(send, "aux", [(i, i ^ bit) for i in range(count)])
    for bit in reversed(bits):
        side = (index // bit) % 2
        other = lax.ppermute(piece, "aux", [(i, i ^ bit) for i in range(count)])
        length = piece.shape[0]
        full = jnp.zeros((2 * length,) + piece.shape[1:], piece.dtype)
        full = lax.dynamic_update_slice_in_dim(full, piece, side * length, axis=0)
        piece = lax.dynamic_update_slice_in_dim(full, other, (1 - side) * length, axis=0)
    return piece


def reduce_chunks(partial):
    count = lax.axis_size("aux")
    pairs = partial.shape[0]
    if count != 4 or pairs % 16:
        return [lax.psum(partial, "aux")]
    index = lax.axis_index("aux")
    chunk = pairs // 2
    stream = chunk // 2
    results = []
    pending = partial
    for c in range(2):
        part = pending[c * chunk:(c + 1) * chunk]
        first = halving_stream(part[:stream], index, count, (1, 2))
        second = halving_stream(part[stream:], index, count, (2, 1))
        results.append(jnp.concatenate([first, second], axis=0))
        if c == 0:
            results[0], pending = lax.optimization_barrier((results[0], pending))
    return results


def class_size(natural_orbital_class):
    return jnp.where(
        natural_orbital_class == 0,
        NPNO // 6,
        jnp.where(
            natural_orbital_class == 1,
            NPNO // 3,
            jnp.where(natural_orbital_class == 2, 2 * NPNO // 3, NPNO),
        ),
    ).astype(jnp.int32)


def fetch_block(sources, width, local, dst, sem):
    index = jnp.clip(local // width, 0, len(sources) - 1)
    row = local % width
    for k, src in enumerate(sources):

        @pl.when(index == k)
        def _():
            pltpu.make_async_copy(src.at[row], dst, sem).start()


def exchange_kernel(
    lead_ref, trail_ref, size_ref, t_left, t_own, t_right, coef_ref, out_ref, lbuf, tbuf, sems, *, occ, group
):
    i = pl.program_id(0)
    steps = pl.num_programs(0)
    sources = (t_left, t_own, t_right)

    def fetch(step, slot):
        for g in range(group):
            p = step * group + g
            pltpu.make_async_copy(t_own.at[lead_ref[p] % occ], lbuf.at[slot, g], sems.at[slot, 0, g]).start()
            fetch_block(sources, occ, trail_ref[p], tbuf.at[slot, g], sems.at[slot, 1, g])

    @pl.when(i == 0)
    def _():
        fetch(0, 0)

    @pl.when(i + 1 < steps)
    def _():
        fetch(i + 1, (i + 1) % 2)

    slot = i % 2
    transposed = (((1,), (1,)), ((), ()))
    for g in range(group):
        p = i * group + g
        pltpu.make_async_copy(t_own.at[0], lbuf.at[slot, g], sems.at[slot, 0, g]).wait()
        pltpu.make_async_copy(t_own.at[0], tbuf.at[slot, g], sems.at[slot, 1, g]).wait()
        size = size_ref[p]
        out_ref[g] = jnp.zeros((NPNO, NPNO), jnp.float32)
        for m in CLASS_SIZES:

            @pl.when(size == m)
            def _():
                first = coef_ref[g, 0, :m, :]
                second = coef_ref[g, 1, :m, :]
                left_t = lax.dot_general(first, lbuf[slot, g], transposed, preferred_element_type=jnp.float32)
                right = lax.dot_general(tbuf[slot, g], second, transposed, preferred_element_type=jnp.float32)
                out_ref[g, :m, :m] = jnp.dot(
                    left_t.astype(jnp.bfloat16), right.astype(jnp.bfloat16), preferred_element_type=jnp.float32
                )


def partial_exchange(lead, trail, sizes, sources, coef_t):
    pairs = coef_t.shape[0]
    group = next(g for g in (4, 2, 1) if pairs % g == 0)
    occ, nfit, npao = sources[1].shape
    hbm = pl.BlockSpec(memory_space=pl.ANY)
    grid_spec = pltpu.PrefetchScalarGridSpec(
        num_scalar_prefetch=3,
        grid=(pairs // group,),
        in_specs=[
            hbm,
            hbm,
            hbm,
            pl.BlockSpec((group, 2, NPNO, npao), lambda i, a, b, s: (i, 0, 0, 0)),
        ],
        out_specs=pl.BlockSpec((group, NPNO, NPNO), lambda i, a, b, s: (i, 0, 0)),
        scratch_shapes=[
            pltpu.VMEM((2, group, nfit, npao), sources[1].dtype),
            pltpu.VMEM((2, group, nfit, npao), sources[1].dtype),
            pltpu.SemaphoreType.DMA((2, 2, group)),
        ],
    )
    flops = pairs * (2 * 2 * nfit * npao * NPNO + 2 * nfit * NPNO * NPNO)
    return pl.pallas_call(
        functools.partial(exchange_kernel, occ=occ, group=group),
        grid_spec=grid_spec,
        out_shape=jax.ShapeDtypeStruct((pairs, NPNO, NPNO), jnp.float32),
        cost_estimate=pl.CostEstimate(
            flops=flops,
            bytes_accessed=pairs * (2 * nfit * npao * 2 + 2 * npao * NPNO * 2 + NPNO * NPNO * 4),
            transcendentals=0,
        ),
    )(lead, trail, sizes, *sources, coef_t)


def split_bf16(value):
    hi = value.astype(jnp.bfloat16)
    lo = (value - hi.astype(jnp.float32)).astype(jnp.bfloat16)
    return hi, lo


def mm(lhs, rhs, dims=(((1,), (0,)), ((), ()))):
    return lax.dot_general(lhs, rhs, dims, preferred_element_type=jnp.float32)


def coupling_kernel(nb_ref, size_ref, fock_ref, *refs, final, width, group, start, nsrc):
    sources = refs[:nsrc]
    margin_ref, ex_ref, col_ref, row_ref, own_ref, out_ref, tbuf, sems, acc_ref = refs[nsrc:]
    i = pl.program_id(0)
    steps = pl.num_programs(0)

    def fetch(step, slot):
        for k in range(2 * group):
            fetch_block(sources, width, nb_ref[2 * (start + group * step) + k], tbuf.at[slot, k], sems.at[slot, k])

    @pl.when(i == 0)
    def _():
        fetch(0, 0)

    @pl.when(i + 1 < steps)
    def _():
        fetch(i + 1, (i + 1) % 2)

    slot = i % 2
    transposed = (((1,), (1,)), ((), ()))
    for g in range(group):
        p = start + i * group + g
        splits = []
        for n in range(2):
            k = 2 * g + n
            pltpu.make_async_copy(sources[0].at[0], tbuf.at[slot, k], sems.at[slot, k]).wait()
            splits.append(split_bf16(tbuf[slot, k]))
        size = size_ref[p]
        acc_ref[...] = jnp.zeros((NPNO, NPNO), jnp.float32)
        for m in CLASS_SIZES:

            @pl.when(size == m)
            def _():
                total = None
                for n in range(2):
                    side = margin_ref[g, n, :m, :]
                    t_hi, t_lo = splits[n]
                    inner = mm(side, t_hi) + mm(side, t_lo)
                    w_hi, w_lo = split_bf16(fock_ref[2 * p + n] * inner)
                    outer = mm(w_hi, side, transposed) + mm(w_lo, side, transposed)
                    total = outer if total is None else total + outer
                acc_ref[:m, :m] = total

        denominator = col_ref[g] + row_ref[g]
        amplitudes = own_ref[g]
        residual = ex_ref[g] + denominator * amplitudes - acc_ref[...]
        if final:
            out_ref[g] = residual
        else:
            out_ref[g] = amplitudes - residual / denominator


def coupling_step(nb, sizes, fock, sources, margin, exchange, energy, own, final, start=0, count=None):
    pairs = own.shape[0]
    count = pairs if count is None else count
    group = next(g for g in (4, 2, 1) if count % g == 0 and start % g == 0)
    base = start // group
    column = energy.reshape(pairs, NPNO, 1)
    row = energy.reshape(pairs, 1, NPNO)
    hbm = pl.BlockSpec(memory_space=pl.ANY)
    own_spec = pl.BlockSpec((group, NPNO, NPNO), lambda i, q, s, f: (i + base, 0, 0))
    grid_spec = pltpu.PrefetchScalarGridSpec(
        num_scalar_prefetch=3,
        grid=(count // group,),
        in_specs=[hbm] * len(sources)
        + [
            pl.BlockSpec((group, 2, NPNO, NPNO), lambda i, q, s, f: (i + base, 0, 0, 0)),
            own_spec,
            pl.BlockSpec((group, NPNO, 1), lambda i, q, s, f: (i + base, 0, 0)),
            pl.BlockSpec((group, 1, NPNO), lambda i, q, s, f: (i + base, 0, 0)),
            own_spec,
        ],
        out_specs=pl.BlockSpec((group, NPNO, NPNO), lambda i, q, s, f: (i, 0, 0)),
        scratch_shapes=[
            pltpu.VMEM((2, 2 * group, NPNO, NPNO), jnp.float32),
            pltpu.SemaphoreType.DMA((2, 2 * group)),
            pltpu.VMEM((NPNO, NPNO), jnp.float32),
        ],
    )
    flops = count * 2 * 4 * 2 * NPNO * NPNO * NPNO
    kernel = functools.partial(
        coupling_kernel, final=final, width=sources[0].shape[0], group=group, start=start, nsrc=len(sources)
    )
    return pl.pallas_call(
        kernel,
        grid_spec=grid_spec,
        out_shape=jax.ShapeDtypeStruct((count, NPNO, NPNO), jnp.float32),
        cost_estimate=pl.CostEstimate(
            flops=flops,
            bytes_accessed=count * NPNO * NPNO * (2 * 4 + 2 * 2 + 3 * 4),
            transcendentals=0,
        ),
    )(nb, sizes, fock, *sources, margin, exchange, column, row, own)


def chunked_halo(chunks):
    received = [halo_sources(chunk, "pair") for chunk in chunks]
    return [r[k] for k in range(3) for r in received]


def per_device(
    three_index,
    pno_coef,
    pair_orbitals,
    natural_orbital_class,
    pno_energy,
    margin,
    neighbour_pairs,
    fock_coupling,
):
    occ_dev = three_index.shape[0]
    pair_dev = pno_coef.shape[0]
    position = lax.axis_index("pair")
    sizes = class_size(natural_orbital_class)
    blocks = halo_sources(three_index, "pair")
    local_orbitals = (pair_orbitals - (position - 1) * occ_dev).astype(jnp.int32)
    partial_ints = partial_exchange(
        local_orbitals[:, 0] - occ_dev,
        local_orbitals[:, 1],
        sizes,
        blocks,
        jnp.swapaxes(pno_coef, 2, 3),
    )
    exchange_chunks = reduce_chunks(partial_ints)
    exchange_ints = jnp.concatenate(exchange_chunks, axis=0)
    denominator = pno_energy[:, :, None] + pno_energy[:, None, :]
    local_rows = (neighbour_pairs - (position - 1) * pair_dev).astype(jnp.int32).reshape(-1)
    fock = fock_coupling.reshape(-1)

    chunk = exchange_chunks[0].shape[0]
    parts = [
        -(part / denominator[c * chunk:(c + 1) * chunk]) for c, part in enumerate(exchange_chunks)
    ]
    sources = chunked_halo(parts)
    amplitudes = jnp.concatenate(parts, axis=0)
    for iteration in range(1, ITERS):
        parts = [
            coupling_step(
                local_rows, sizes, fock, sources, margin, exchange_ints, pno_energy, amplitudes,
                False, c * chunk, chunk,
            )
            for c in range(len(parts))
        ]
        sources = chunked_halo(parts)
        amplitudes = jnp.concatenate(parts, axis=0)
    residual = coupling_step(
        local_rows, sizes, fock, sources, margin, exchange_ints, pno_energy, amplitudes, True
    )
    return (amplitudes, residual)


def solution(mesh):
    return jax.shard_map(
        per_device,
        mesh=mesh,
        in_specs=(
            P("pair", "aux", None),
            P("pair", None, None, None),
            P("pair", None),
            P("pair"),
            P("pair", None),
            P("pair", None, None, None),
            P("pair", None),
            P("pair", None),
        ),
        out_specs=(P("pair", None, None), P("pair", None, None)),
        check_vma=False,
    )
```

```python
import functools

import jax
import jax.numpy as jnp
from jax import lax
from jax.experimental import pallas as pl
from jax.experimental.pallas import tpu as pltpu
from jax.sharding import PartitionSpec as P

NPNO = 192
ITERS = 2
CLASS_SIZES = (NPNO // 6, NPNO // 3, 2 * NPNO // 3, NPNO)


def halo_sources(cells, axis):
    count = lax.axis_size(axis)
    ends = count - 1
    from_left = lax.ppermute(cells, axis, [(i, i + 1) for i in range(ends)])
    from_right = lax.ppermute(cells, axis, [(i + 1, i) for i in range(ends)])
    return (from_left, cells, from_right)


def halving_stream(piece, index, count, bits):
    for bit in bits:
        side = (index // bit) % 2
        half = piece.shape[0] // 2
        keep = lax.dynamic_slice_in_dim(piece, side * half, half, axis=0)
        send = lax.dynamic_slice_in_dim(piece, (1 - side) * half, half, axis=0)
        piece = keep + lax.ppermute(send, "aux", [(i, i ^ bit) for i in range(count)])
    for bit in reversed(bits):
        side = (index // bit) % 2
        other = lax.ppermute(piece, "aux", [(i, i ^ bit) for i in range(count)])
        length = piece.shape[0]
        full = jnp.zeros((2 * length,) + piece.shape[1:], piece.dtype)
        full = lax.dynamic_update_slice_in_dim(full, piece, side * length, axis=0)
        piece = lax.dynamic_update_slice_in_dim(full, other, (1 - side) * length, axis=0)
    return piece


def sum_over_aux(partial):
    count = lax.axis_size("aux")
    if count != 4 or partial.shape[0] % 8:
        return lax.psum(partial, "aux")
    index = lax.axis_index("aux")
    half = partial.shape[0] // 2
    first = halving_stream(partial[:half], index, count, (1, 2))
    second = halving_stream(partial[half:], index, count, (2, 1))
    return jnp.concatenate([first, second], axis=0)


def class_size(natural_orbital_class):
    return jnp.where(
        natural_orbital_class == 0,
        NPNO // 6,
        jnp.where(
            natural_orbital_class == 1,
            NPNO // 3,
            jnp.where(natural_orbital_class == 2, 2 * NPNO // 3, NPNO),
        ),
    ).astype(jnp.int32)


def fetch_block(sources, width, local, dst, sem):
    index = jnp.clip(local // width, 0, len(sources) - 1)
    row = local % width
    for k, src in enumerate(sources):

        @pl.when(index == k)
        def _():
            pltpu.make_async_copy(src.at[row], dst, sem).start()


def exchange_kernel(
    lead_ref, trail_ref, size_ref, t_left, t_own, t_right, coef_ref, out_ref, lbuf, tbuf, sems, *, occ, group
):
    i = pl.program_id(0)
    steps = pl.num_programs(0)
    sources = (t_left, t_own, t_right)

    def fetch(step, slot):
        for g in range(group):
            p = step * group + g
            pltpu.make_async_copy(t_own.at[lead_ref[p] % occ], lbuf.at[slot, g], sems.at[slot, 0, g]).start()
            fetch_block(sources, occ, trail_ref[p], tbuf.at[slot, g], sems.at[slot, 1, g])

    @pl.when(i == 0)
    def _():
        fetch(0, 0)

    @pl.when(i + 1 < steps)
    def _():
        fetch(i + 1, (i + 1) % 2)

    slot = i % 2
    transposed = (((1,), (1,)), ((), ()))
    for g in range(group):
        p = i * group + g
        pltpu.make_async_copy(t_own.at[0], lbuf.at[slot, g], sems.at[slot, 0, g]).wait()
        pltpu.make_async_copy(t_own.at[0], tbuf.at[slot, g], sems.at[slot, 1, g]).wait()
        size = size_ref[p]
        out_ref[g] = jnp.zeros((NPNO, NPNO), jnp.float32)
        for m in CLASS_SIZES:

            @pl.when(size == m)
            def _():
                first = coef_ref[g, 0, :m, :]
                second = coef_ref[g, 1, :m, :]
                left_t = lax.dot_general(first, lbuf[slot, g], transposed, preferred_element_type=jnp.float32)
                right = lax.dot_general(tbuf[slot, g], second, transposed, preferred_element_type=jnp.float32)
                out_ref[g, :m, :m] = jnp.dot(
                    left_t.astype(jnp.bfloat16), right.astype(jnp.bfloat16), preferred_element_type=jnp.float32
                )


def partial_exchange(lead, trail, sizes, sources, coef_t):
    pairs = coef_t.shape[0]
    group = next(g for g in (4, 2, 1) if pairs % g == 0)
    occ, nfit, npao = sources[1].shape
    hbm = pl.BlockSpec(memory_space=pl.ANY)
    grid_spec = pltpu.PrefetchScalarGridSpec(
        num_scalar_prefetch=3,
        grid=(pairs // group,),
        in_specs=[
            hbm,
            hbm,
            hbm,
            pl.BlockSpec((group, 2, NPNO, npao), lambda i, a, b, s: (i, 0, 0, 0)),
        ],
        out_specs=pl.BlockSpec((group, NPNO, NPNO), lambda i, a, b, s: (i, 0, 0)),
        scratch_shapes=[
            pltpu.VMEM((2, group, nfit, npao), sources[1].dtype),
            pltpu.VMEM((2, group, nfit, npao), sources[1].dtype),
            pltpu.SemaphoreType.DMA((2, 2, group)),
        ],
    )
    flops = pairs * (2 * 2 * nfit * npao * NPNO + 2 * nfit * NPNO * NPNO)
    return pl.pallas_call(
        functools.partial(exchange_kernel, occ=occ, group=group),
        grid_spec=grid_spec,
        out_shape=jax.ShapeDtypeStruct((pairs, NPNO, NPNO), jnp.float32),
        cost_estimate=pl.CostEstimate(
            flops=flops,
            bytes_accessed=pairs * (2 * nfit * npao * 2 + 2 * npao * NPNO * 2 + NPNO * NPNO * 4),
            transcendentals=0,
        ),
    )(lead, trail, sizes, *sources, coef_t)


def split_bf16(value):
    hi = value.astype(jnp.bfloat16)
    lo = (value - hi.astype(jnp.float32)).astype(jnp.bfloat16)
    return hi, lo


def mm(lhs, rhs, dims=(((1,), (0,)), ((), ()))):
    return lax.dot_general(lhs, rhs, dims, preferred_element_type=jnp.float32)


def coupling_kernel(nb_ref, size_ref, fock_ref, *refs, final, width, group, start, nsrc):
    sources = refs[:nsrc]
    margin_ref, ex_ref, col_ref, row_ref, own_ref, out_ref, tbuf, sems, acc_ref = refs[nsrc:]
    i = pl.program_id(0)
    steps = pl.num_programs(0)

    def fetch(step, slot):
        for k in range(2 * group):
            fetch_block(sources, width, nb_ref[2 * (start + group * step) + k], tbuf.at[slot, k], sems.at[slot, k])

    @pl.when(i == 0)
    def _():
        fetch(0, 0)

    @pl.when(i + 1 < steps)
    def _():
        fetch(i + 1, (i + 1) % 2)

    slot = i % 2
    transposed = (((1,), (1,)), ((), ()))
    for g in range(group):
        p = start + i * group + g
        splits = []
        for n in range(2):
            k = 2 * g + n
            pltpu.make_async_copy(sources[0].at[0], tbuf.at[slot, k], sems.at[slot, k]).wait()
            splits.append(split_bf16(tbuf[slot, k]))
        size = size_ref[p]
        acc_ref[...] = jnp.zeros((NPNO, NPNO), jnp.float32)
        for m in CLASS_SIZES:

            @pl.when(size == m)
            def _():
                total = None
                for n in range(2):
                    side = margin_ref[g, n, :m, :]
                    t_hi, t_lo = splits[n]
                    inner = mm(side, t_hi) + mm(side, t_lo)
                    w_hi, w_lo = split_bf16(fock_ref[2 * p + n] * inner)
                    outer = mm(w_hi, side, transposed) + mm(w_lo, side, transposed)
                    total = outer if total is None else total + outer
                acc_ref[:m, :m] = total

        denominator = col_ref[g] + row_ref[g]
        amplitudes = own_ref[g]
        residual = ex_ref[g] + denominator * amplitudes - acc_ref[...]
        if final:
            out_ref[g] = residual
        else:
            out_ref[g] = amplitudes - residual / denominator


def coupling_step(nb, sizes, fock, sources, margin, exchange, energy, own, final, start=0, count=None):
    pairs = own.shape[0]
    count = pairs if count is None else count
    group = next(g for g in (4, 2, 1) if count % g == 0 and start % g == 0)
    base = start // group
    column = energy.reshape(pairs, NPNO, 1)
    row = energy.reshape(pairs, 1, NPNO)
    hbm = pl.BlockSpec(memory_space=pl.ANY)
    own_spec = pl.BlockSpec((group, NPNO, NPNO), lambda i, q, s, f: (i + base, 0, 0))
    grid_spec = pltpu.PrefetchScalarGridSpec(
        num_scalar_prefetch=3,
        grid=(count // group,),
        in_specs=[hbm] * len(sources)
        + [
            pl.BlockSpec((group, 2, NPNO, NPNO), lambda i, q, s, f: (i + base, 0, 0, 0)),
            own_spec,
            pl.BlockSpec((group, NPNO, 1), lambda i, q, s, f: (i + base, 0, 0)),
            pl.BlockSpec((group, 1, NPNO), lambda i, q, s, f: (i + base, 0, 0)),
            own_spec,
        ],
        out_specs=pl.BlockSpec((group, NPNO, NPNO), lambda i, q, s, f: (i, 0, 0)),
        scratch_shapes=[
            pltpu.VMEM((2, 2 * group, NPNO, NPNO), jnp.float32),
            pltpu.SemaphoreType.DMA((2, 2 * group)),
            pltpu.VMEM((NPNO, NPNO), jnp.float32),
        ],
    )
    flops = count * 2 * 4 * 2 * NPNO * NPNO * NPNO
    kernel = functools.partial(
        coupling_kernel, final=final, width=sources[0].shape[0], group=group, start=start, nsrc=len(sources)
    )
    return pl.pallas_call(
        kernel,
        grid_spec=grid_spec,
        out_shape=jax.ShapeDtypeStruct((count, NPNO, NPNO), jnp.float32),
        cost_estimate=pl.CostEstimate(
            flops=flops,
            bytes_accessed=count * NPNO * NPNO * (2 * 4 + 2 * 2 + 3 * 4),
            transcendentals=0,
        ),
    )(nb, sizes, fock, *sources, margin, exchange, column, row, own)


def chunked_halo(chunks):
    received = [halo_sources(chunk, "pair") for chunk in chunks]
    return [r[k] for k in range(3) for r in received]


def per_device(
    three_index,
    pno_coef,
    pair_orbitals,
    natural_orbital_class,
    pno_energy,
    margin,
    neighbour_pairs,
    fock_coupling,
):
    occ_dev = three_index.shape[0]
    pair_dev = pno_coef.shape[0]
    position = lax.axis_index("pair")
    sizes = class_size(natural_orbital_class)
    blocks = halo_sources(three_index, "pair")
    local_orbitals = (pair_orbitals - (position - 1) * occ_dev).astype(jnp.int32)
    partial_ints = partial_exchange(
        local_orbitals[:, 0] - occ_dev,
        local_orbitals[:, 1],
        sizes,
        blocks,
        jnp.swapaxes(pno_coef, 2, 3),
    )
    exchange_ints = sum_over_aux(partial_ints)
    denominator = pno_energy[:, :, None] + pno_energy[:, None, :]
    local_rows = (neighbour_pairs - (position - 1) * pair_dev).astype(jnp.int32).reshape(-1)
    fock = fock_coupling.reshape(-1)

    chunk = pair_dev // 2 if pair_dev % 8 == 0 else pair_dev
    parts = [-(exchange_ints / denominator)]
    sources = chunked_halo(parts)
    amplitudes = jnp.concatenate(parts, axis=0)
    for iteration in range(1, ITERS):
        parts = [
            coupling_step(
                local_rows, sizes, fock, sources, margin, exchange_ints, pno_energy, amplitudes,
                False, c * chunk, chunk,
            )
            for c in range(pair_dev // chunk)
        ]
        sources = chunked_halo(parts)
        amplitudes = jnp.concatenate(parts, axis=0)
    residual = coupling_step(
        local_rows, sizes, fock, sources, margin, exchange_ints, pno_energy, amplitudes, True
    )
    return (amplitudes, residual)


def solution(mesh):
    return jax.shard_map(
        per_device,
        mesh=mesh,
        in_specs=(
            P("pair", "aux", None),
            P("pair", None, None, None),
            P("pair", None),
            P("pair"),
            P("pair", None),
            P("pair", None, None, None),
            P("pair", None),
            P("pair", None),
        ),
        out_specs=(P("pair", None, None), P("pair", None, None)),
        check_vma=False,
    )
```

```python
import functools

import jax
import jax.numpy as jnp
from jax import lax
from jax.experimental import pallas as pl
from jax.experimental.pallas import tpu as pltpu
from jax.sharding import PartitionSpec as P

NPNO = 192
ITERS = 2
CLASS_SIZES = (NPNO // 6, NPNO // 3, 2 * NPNO // 3, NPNO)


def halo_sources(cells, axis):
    count = lax.axis_size(axis)
    ends = count - 1
    from_left = lax.ppermute(cells, axis, [(i, i + 1) for i in range(ends)])
    from_right = lax.ppermute(cells, axis, [(i + 1, i) for i in range(ends)])
    return (from_left, cells, from_right)


def halving_stream(piece, index, count, bits):
    for bit in bits:
        side = (index // bit) % 2
        half = piece.shape[0] // 2
        keep = lax.dynamic_slice_in_dim(piece, side * half, half, axis=0)
        send = lax.dynamic_slice_in_dim(piece, (1 - side) * half, half, axis=0)
        piece = keep + lax.ppermute(send, "aux", [(i, i ^ bit) for i in range(count)])
    for bit in reversed(bits):
        side = (index // bit) % 2
        other = lax.ppermute(piece, "aux", [(i, i ^ bit) for i in range(count)])
        length = piece.shape[0]
        full = jnp.zeros((2 * length,) + piece.shape[1:], piece.dtype)
        full = lax.dynamic_update_slice_in_dim(full, piece, side * length, axis=0)
        piece = lax.dynamic_update_slice_in_dim(full, other, (1 - side) * length, axis=0)
    return piece


def sum_over_aux(halves):
    count = lax.axis_size("aux")
    if count != 4 or halves[0].shape[0] % 4:
        return lax.psum(jnp.concatenate(halves, axis=0), "aux")
    index = lax.axis_index("aux")
    first = halving_stream(halves[0], index, count, (1, 2))
    second = halving_stream(halves[1], index, count, (2, 1))
    return jnp.concatenate([first, second], axis=0)


def class_size(natural_orbital_class):
    return jnp.where(
        natural_orbital_class == 0,
        NPNO // 6,
        jnp.where(
            natural_orbital_class == 1,
            NPNO // 3,
            jnp.where(natural_orbital_class == 2, 2 * NPNO // 3, NPNO),
        ),
    ).astype(jnp.int32)


def fetch_block(sources, width, local, dst, sem):
    index = jnp.clip(local // width, 0, len(sources) - 1)
    row = local % width
    for k, src in enumerate(sources):

        @pl.when(index == k)
        def _():
            pltpu.make_async_copy(src.at[row], dst, sem).start()


def exchange_kernel(
    lead_ref, trail_ref, size_ref, t_left, t_own, t_right, coef_ref, out_ref, lbuf, tbuf, sems, *, occ, group, start
):
    i = pl.program_id(0)
    steps = pl.num_programs(0)
    sources = (t_left, t_own, t_right)

    def fetch(step, slot):
        for g in range(group):
            p = start + step * group + g
            pltpu.make_async_copy(t_own.at[lead_ref[p] % occ], lbuf.at[slot, g], sems.at[slot, 0, g]).start()
            fetch_block(sources, occ, trail_ref[p], tbuf.at[slot, g], sems.at[slot, 1, g])

    @pl.when(i == 0)
    def _():
        fetch(0, 0)

    @pl.when(i + 1 < steps)
    def _():
        fetch(i + 1, (i + 1) % 2)

    slot = i % 2
    transposed = (((1,), (1,)), ((), ()))
    for g in range(group):
        p = start + i * group + g
        pltpu.make_async_copy(t_own.at[0], lbuf.at[slot, g], sems.at[slot, 0, g]).wait()
        pltpu.make_async_copy(t_own.at[0], tbuf.at[slot, g], sems.at[slot, 1, g]).wait()
        size = size_ref[p]
        out_ref[g] = jnp.zeros((NPNO, NPNO), jnp.float32)
        for m in CLASS_SIZES:

            @pl.when(size == m)
            def _():
                first = coef_ref[g, 0, :m, :]
                second = coef_ref[g, 1, :m, :]
                left_t = lax.dot_general(first, lbuf[slot, g], transposed, preferred_element_type=jnp.float32)
                right = lax.dot_general(tbuf[slot, g], second, transposed, preferred_element_type=jnp.float32)
                out_ref[g, :m, :m] = jnp.dot(
                    left_t.astype(jnp.bfloat16), right.astype(jnp.bfloat16), preferred_element_type=jnp.float32
                )


def partial_exchange(lead, trail, sizes, sources, coef_t, start=0, count=None):
    pairs = coef_t.shape[0]
    count = pairs if count is None else count
    group = next(g for g in (4, 2, 1) if count % g == 0 and start % g == 0)
    base = start // group
    occ, nfit, npao = sources[1].shape
    hbm = pl.BlockSpec(memory_space=pl.ANY)
    grid_spec = pltpu.PrefetchScalarGridSpec(
        num_scalar_prefetch=3,
        grid=(count // group,),
        in_specs=[
            hbm,
            hbm,
            hbm,
            pl.BlockSpec((group, 2, NPNO, npao), lambda i, a, b, s: (i + base, 0, 0, 0)),
        ],
        out_specs=pl.BlockSpec((group, NPNO, NPNO), lambda i, a, b, s: (i, 0, 0)),
        scratch_shapes=[
            pltpu.VMEM((2, group, nfit, npao), sources[1].dtype),
            pltpu.VMEM((2, group, nfit, npao), sources[1].dtype),
            pltpu.SemaphoreType.DMA((2, 2, group)),
        ],
    )
    flops = count * (2 * 2 * nfit * npao * NPNO + 2 * nfit * NPNO * NPNO)
    return pl.pallas_call(
        functools.partial(exchange_kernel, occ=occ, group=group, start=start),
        grid_spec=grid_spec,
        out_shape=jax.ShapeDtypeStruct((count, NPNO, NPNO), jnp.float32),
        cost_estimate=pl.CostEstimate(
            flops=flops,
            bytes_accessed=count * (2 * nfit * npao * 2 + 2 * npao * NPNO * 2 + NPNO * NPNO * 4),
            transcendentals=0,
        ),
    )(lead, trail, sizes, *sources, coef_t)


def split_bf16(value):
    hi = value.astype(jnp.bfloat16)
    lo = (value - hi.astype(jnp.float32)).astype(jnp.bfloat16)
    return hi, lo


def mm(lhs, rhs, dims=(((1,), (0,)), ((), ()))):
    return lax.dot_general(lhs, rhs, dims, preferred_element_type=jnp.float32)


def coupling_kernel(nb_ref, size_ref, fock_ref, *refs, final, width, group, start, nsrc):
    sources = refs[:nsrc]
    margin_ref, ex_ref, col_ref, row_ref, own_ref, out_ref, tbuf, sems, acc_ref = refs[nsrc:]
    i = pl.program_id(0)
    steps = pl.num_programs(0)

    def fetch(step, slot):
        for k in range(2 * group):
            fetch_block(sources, width, nb_ref[2 * (start + group * step) + k], tbuf.at[slot, k], sems.at[slot, k])

    @pl.when(i == 0)
    def _():
        fetch(0, 0)

    @pl.when(i + 1 < steps)
    def _():
        fetch(i + 1, (i + 1) % 2)

    slot = i % 2
    transposed = (((1,), (1,)), ((), ()))
    for g in range(group):
        p = start + i * group + g
        splits = []
        for n in range(2):
            k = 2 * g + n
            pltpu.make_async_copy(sources[0].at[0], tbuf.at[slot, k], sems.at[slot, k]).wait()
            splits.append(split_bf16(tbuf[slot, k]))
        size = size_ref[p]
        acc_ref[...] = jnp.zeros((NPNO, NPNO), jnp.float32)
        for m in CLASS_SIZES:

            @pl.when(size == m)
            def _():
                total = None
                for n in range(2):
                    side = margin_ref[g, n, :m, :]
                    t_hi, t_lo = splits[n]
                    inner = mm(side, t_hi) + mm(side, t_lo)
                    w_hi, w_lo = split_bf16(fock_ref[2 * p + n] * inner)
                    outer = mm(w_hi, side, transposed) + mm(w_lo, side, transposed)
                    total = outer if total is None else total + outer
                acc_ref[:m, :m] = total

        denominator = col_ref[g] + row_ref[g]
        amplitudes = own_ref[g]
        residual = ex_ref[g] + denominator * amplitudes - acc_ref[...]
        if final:
            out_ref[g] = residual
        else:
            out_ref[g] = amplitudes - residual / denominator


def coupling_step(nb, sizes, fock, sources, margin, exchange, energy, own, final, start=0, count=None):
    pairs = own.shape[0]
    count = pairs if count is None else count
    group = next(g for g in (4, 2, 1) if count % g == 0 and start % g == 0)
    base = start // group
    column = energy.reshape(pairs, NPNO, 1)
    row = energy.reshape(pairs, 1, NPNO)
    hbm = pl.BlockSpec(memory_space=pl.ANY)
    own_spec = pl.BlockSpec((group, NPNO, NPNO), lambda i, q, s, f: (i + base, 0, 0))
    grid_spec = pltpu.PrefetchScalarGridSpec(
        num_scalar_prefetch=3,
        grid=(count // group,),
        in_specs=[hbm] * len(sources)
        + [
            pl.BlockSpec((group, 2, NPNO, NPNO), lambda i, q, s, f: (i + base, 0, 0, 0)),
            own_spec,
            pl.BlockSpec((group, NPNO, 1), lambda i, q, s, f: (i + base, 0, 0)),
            pl.BlockSpec((group, 1, NPNO), lambda i, q, s, f: (i + base, 0, 0)),
            own_spec,
        ],
        out_specs=pl.BlockSpec((group, NPNO, NPNO), lambda i, q, s, f: (i, 0, 0)),
        scratch_shapes=[
            pltpu.VMEM((2, 2 * group, NPNO, NPNO), jnp.float32),
            pltpu.SemaphoreType.DMA((2, 2 * group)),
            pltpu.VMEM((NPNO, NPNO), jnp.float32),
        ],
    )
    flops = count * 2 * 4 * 2 * NPNO * NPNO * NPNO
    kernel = functools.partial(
        coupling_kernel, final=final, width=sources[0].shape[0], group=group, start=start, nsrc=len(sources)
    )
    return pl.pallas_call(
        kernel,
        grid_spec=grid_spec,
        out_shape=jax.ShapeDtypeStruct((count, NPNO, NPNO), jnp.float32),
        cost_estimate=pl.CostEstimate(
            flops=flops,
            bytes_accessed=count * NPNO * NPNO * (2 * 4 + 2 * 2 + 3 * 4),
            transcendentals=0,
        ),
    )(nb, sizes, fock, *sources, margin, exchange, column, row, own)


def chunked_halo(chunks):
    received = [halo_sources(chunk, "pair") for chunk in chunks]
    return [r[k] for k in range(3) for r in received]


def per_device(
    three_index,
    pno_coef,
    pair_orbitals,
    natural_orbital_class,
    pno_energy,
    margin,
    neighbour_pairs,
    fock_coupling,
):
    occ_dev = three_index.shape[0]
    pair_dev = pno_coef.shape[0]
    position = lax.axis_index("pair")
    sizes = class_size(natural_orbital_class)
    blocks = halo_sources(three_index, "pair")
    local_orbitals = (pair_orbitals - (position - 1) * occ_dev).astype(jnp.int32)
    half = pair_dev // 2
    halves = [
        partial_exchange(
            local_orbitals[:, 0] - occ_dev,
            local_orbitals[:, 1],
            sizes,
            blocks,
            jnp.swapaxes(pno_coef, 2, 3),
            start,
            half,
        )
        for start in (0, half)
    ]
    exchange_ints = sum_over_aux(halves)
    denominator = pno_energy[:, :, None] + pno_energy[:, None, :]
    local_rows = (neighbour_pairs - (position - 1) * pair_dev).astype(jnp.int32).reshape(-1)
    fock = fock_coupling.reshape(-1)

    chunk = pair_dev // 2 if pair_dev % 8 == 0 else pair_dev
    parts = [-(exchange_ints / denominator)]
    sources = chunked_halo(parts)
    amplitudes = jnp.concatenate(parts, axis=0)
    for iteration in range(1, ITERS):
        parts = [
            coupling_step(
                local_rows, sizes, fock, sources, margin, exchange_ints, pno_energy, amplitudes,
                False, c * chunk, chunk,
            )
            for c in range(pair_dev // chunk)
        ]
        sources = chunked_halo(parts)
        amplitudes = jnp.concatenate(parts, axis=0)
    residual = coupling_step(
        local_rows, sizes, fock, sources, margin, exchange_ints, pno_energy, amplitudes, True
    )
    return (amplitudes, residual)


def solution(mesh):
    return jax.shard_map(
        per_device,
        mesh=mesh,
        in_specs=(
            P("pair", "aux", None),
            P("pair", None, None, None),
            P("pair", None),
            P("pair"),
            P("pair", None),
            P("pair", None, None, None),
            P("pair", None),
            P("pair", None),
        ),
        out_specs=(P("pair", None, None), P("pair", None, None)),
        check_vma=False,
    )
```

```python
import functools

import jax
import jax.numpy as jnp
from jax import lax
from jax.experimental import pallas as pl
from jax.experimental.pallas import tpu as pltpu
from jax.sharding import PartitionSpec as P

NPNO = 192
ITERS = 2
CLASS_SIZES = (NPNO // 6, NPNO // 3, 2 * NPNO // 3, NPNO)


def halo_sources(cells, axis):
    count = lax.axis_size(axis)
    ends = count - 1
    from_left = lax.ppermute(cells, axis, [(i, i + 1) for i in range(ends)])
    from_right = lax.ppermute(cells, axis, [(i + 1, i) for i in range(ends)])
    return (from_left, cells, from_right)


def halving_stream(piece, index, count, bits):
    for bit in bits:
        side = (index // bit) % 2
        half = piece.shape[0] // 2
        keep = lax.dynamic_slice_in_dim(piece, side * half, half, axis=0)
        send = lax.dynamic_slice_in_dim(piece, (1 - side) * half, half, axis=0)
        piece = keep + lax.ppermute(send, "aux", [(i, i ^ bit) for i in range(count)])
    for bit in reversed(bits):
        side = (index // bit) % 2
        other = lax.ppermute(piece, "aux", [(i, i ^ bit) for i in range(count)])
        length = piece.shape[0]
        full = jnp.zeros((2 * length,) + piece.shape[1:], piece.dtype)
        full = lax.dynamic_update_slice_in_dim(full, piece, side * length, axis=0)
        piece = lax.dynamic_update_slice_in_dim(full, other, (1 - side) * length, axis=0)
    return piece


def sum_over_aux(halves):
    count = lax.axis_size("aux")
    if count != 4 or halves[0].shape[0] % 4:
        return lax.psum(jnp.concatenate(halves, axis=0), "aux")
    index = lax.axis_index("aux")
    first = halving_stream(halves[0], index, count, (1, 2))
    second = halving_stream(halves[1], index, count, (2, 1))
    return jnp.concatenate([first, second], axis=0)


def class_size(natural_orbital_class):
    return jnp.where(
        natural_orbital_class == 0,
        NPNO // 6,
        jnp.where(
            natural_orbital_class == 1,
            NPNO // 3,
            jnp.where(natural_orbital_class == 2, 2 * NPNO // 3, NPNO),
        ),
    ).astype(jnp.int32)


def fetch_block(sources, width, local, dst, sem):
    index = jnp.clip(local // width, 0, len(sources) - 1)
    row = local % width
    for k, src in enumerate(sources):

        @pl.when(index == k)
        def _():
            pltpu.make_async_copy(src.at[row], dst, sem).start()


def exchange_kernel(
    lead_ref, trail_ref, size_ref, t_left, t_own, t_right, coef_ref, out_ref, lbuf, tbuf, sems, *, occ, group, start
):
    i = pl.program_id(0)
    steps = pl.num_programs(0)
    sources = (t_left, t_own, t_right)

    def fetch(step, slot):
        for g in range(group):
            p = start + step * group + g
            pltpu.make_async_copy(t_own.at[lead_ref[p] % occ], lbuf.at[slot, g], sems.at[slot, 0, g]).start()
            fetch_block(sources, occ, trail_ref[p], tbuf.at[slot, g], sems.at[slot, 1, g])

    @pl.when(i == 0)
    def _():
        fetch(0, 0)

    @pl.when(i + 1 < steps)
    def _():
        fetch(i + 1, (i + 1) % 2)

    slot = i % 2
    transposed = (((1,), (1,)), ((), ()))
    for g in range(group):
        p = start + i * group + g
        pltpu.make_async_copy(t_own.at[0], lbuf.at[slot, g], sems.at[slot, 0, g]).wait()
        pltpu.make_async_copy(t_own.at[0], tbuf.at[slot, g], sems.at[slot, 1, g]).wait()
        size = size_ref[p]
        out_ref[g] = jnp.zeros((NPNO, NPNO), jnp.float32)
        for m in CLASS_SIZES:

            @pl.when(size == m)
            def _():
                first = coef_ref[g, 0, :m, :]
                second = coef_ref[g, 1, :m, :]
                left_t = lax.dot_general(first, lbuf[slot, g], transposed, preferred_element_type=jnp.float32)
                right = lax.dot_general(tbuf[slot, g], second, transposed, preferred_element_type=jnp.float32)
                out_ref[g, :m, :m] = jnp.dot(
                    left_t.astype(jnp.bfloat16), right.astype(jnp.bfloat16), preferred_element_type=jnp.float32
                )


def partial_exchange(lead, trail, sizes, sources, coef_t, start=0, count=None):
    pairs = coef_t.shape[0]
    count = pairs if count is None else count
    group = next(g for g in (4, 2, 1) if count % g == 0 and start % g == 0)
    base = start // group
    occ, nfit, npao = sources[1].shape
    hbm = pl.BlockSpec(memory_space=pl.ANY)
    grid_spec = pltpu.PrefetchScalarGridSpec(
        num_scalar_prefetch=3,
        grid=(count // group,),
        in_specs=[
            hbm,
            hbm,
            hbm,
            pl.BlockSpec((group, 2, NPNO, npao), lambda i, a, b, s: (i + base, 0, 0, 0)),
        ],
        out_specs=pl.BlockSpec((group, NPNO, NPNO), lambda i, a, b, s: (i, 0, 0)),
        scratch_shapes=[
            pltpu.VMEM((2, group, nfit, npao), sources[1].dtype),
            pltpu.VMEM((2, group, nfit, npao), sources[1].dtype),
            pltpu.SemaphoreType.DMA((2, 2, group)),
        ],
    )
    flops = count * (2 * 2 * nfit * npao * NPNO + 2 * nfit * NPNO * NPNO)
    return pl.pallas_call(
        functools.partial(exchange_kernel, occ=occ, group=group, start=start),
        grid_spec=grid_spec,
        out_shape=jax.ShapeDtypeStruct((count, NPNO, NPNO), jnp.float32),
        cost_estimate=pl.CostEstimate(
            flops=flops,
            bytes_accessed=count * (2 * nfit * npao * 2 + 2 * npao * NPNO * 2 + NPNO * NPNO * 4),
            transcendentals=0,
        ),
    )(lead, trail, sizes, *sources, coef_t)


def split_bf16(value):
    hi = value.astype(jnp.bfloat16)
    lo = (value - hi.astype(jnp.float32)).astype(jnp.bfloat16)
    return hi, lo


def mm(lhs, rhs, dims=(((1,), (0,)), ((), ()))):
    return lax.dot_general(lhs, rhs, dims, preferred_element_type=jnp.float32)


def coupling_kernel(nb_ref, size_ref, fock_ref, *refs, mode, final, width, group, start, nsrc):
    sources = refs[:nsrc]
    margin_ref = refs[nsrc]
    if mode == "local":
        out_ref, tbuf, sems, acc_ref = refs[nsrc + 1:]
    else:
        ex_ref, col_ref, row_ref, own_ref = refs[nsrc + 1:nsrc + 5]
        partial_ref = refs[nsrc + 5] if mode == "remote" else None
        out_ref, tbuf, sems, acc_ref = refs[-4:]
    i = pl.program_id(0)
    steps = pl.num_programs(0)

    def taken(q):
        if mode == "local":
            return q // width == 1
        if mode == "remote":
            return q // width != 1
        return None

    def when(condition, body):
        if condition is None:
            body()
        else:
            pl.when(condition)(body)

    def fetch(step, slot):
        for k in range(2 * group):
            q = nb_ref[2 * (start + group * step) + k]
            if mode == "local":
                copy = pltpu.make_async_copy(sources[0].at[q % width], tbuf.at[slot, k], sems.at[slot, k])
                when(taken(q), copy.start)
            else:
                when(taken(q), functools.partial(fetch_block, sources, width, q, tbuf.at[slot, k], sems.at[slot, k]))

    @pl.when(i == 0)
    def _():
        fetch(0, 0)

    @pl.when(i + 1 < steps)
    def _():
        fetch(i + 1, (i + 1) % 2)

    slot = i % 2
    transposed = (((1,), (1,)), ((), ()))
    for g in range(group):
        p = start + i * group + g
        size = size_ref[p]
        if mode == "remote":
            acc_ref[...] = partial_ref[g]
        else:
            acc_ref[...] = jnp.zeros((NPNO, NPNO), jnp.float32)
        for n in range(2):
            k = 2 * g + n

            def term(g=g, n=n, k=k, p=p, size=size):
                pltpu.make_async_copy(sources[0].at[0], tbuf.at[slot, k], sems.at[slot, k]).wait()
                t_hi, t_lo = split_bf16(tbuf[slot, k])
                for m in CLASS_SIZES:

                    @pl.when(size == m)
                    def _():
                        side = margin_ref[g, n, :m, :]
                        inner = mm(side, t_hi) + mm(side, t_lo)
                        w_hi, w_lo = split_bf16(fock_ref[2 * p + n] * inner)
                        acc_ref[:m, :m] += mm(w_hi, side, transposed) + mm(w_lo, side, transposed)

            when(taken(nb_ref[2 * p + n]), term)

        if mode == "local":
            out_ref[g] = acc_ref[...]
            continue
        denominator = col_ref[g] + row_ref[g]
        amplitudes = own_ref[g]
        residual = ex_ref[g] + denominator * amplitudes - acc_ref[...]
        if final:
            out_ref[g] = residual
        else:
            out_ref[g] = amplitudes - residual / denominator


def coupling_step(
    nb, sizes, fock, sources, margin, exchange, energy, own, final, start=0, count=None, mode="all", partial=None
):
    pairs = margin.shape[0]
    count = pairs if count is None else count
    group = next(g for g in (4, 2, 1) if count % g == 0 and start % g == 0)
    base = start // group
    hbm = pl.BlockSpec(memory_space=pl.ANY)
    own_spec = pl.BlockSpec((group, NPNO, NPNO), lambda i, q, s, f: (i + base, 0, 0))
    in_specs = [hbm] * len(sources) + [
        pl.BlockSpec((group, 2, NPNO, NPNO), lambda i, q, s, f: (i + base, 0, 0, 0))
    ]
    operands = [*sources, margin]
    if mode != "local":
        in_specs += [
            own_spec,
            pl.BlockSpec((group, NPNO, 1), lambda i, q, s, f: (i + base, 0, 0)),
            pl.BlockSpec((group, 1, NPNO), lambda i, q, s, f: (i + base, 0, 0)),
            own_spec,
        ]
        operands += [exchange, energy.reshape(pairs, NPNO, 1), energy.reshape(pairs, 1, NPNO), own]
    if mode == "remote":
        in_specs.append(pl.BlockSpec((group, NPNO, NPNO), lambda i, q, s, f: (i, 0, 0)))
        operands.append(partial)
    grid_spec = pltpu.PrefetchScalarGridSpec(
        num_scalar_prefetch=3,
        grid=(count // group,),
        in_specs=in_specs,
        out_specs=pl.BlockSpec((group, NPNO, NPNO), lambda i, q, s, f: (i, 0, 0)),
        scratch_shapes=[
            pltpu.VMEM((2, 2 * group, NPNO, NPNO), jnp.float32),
            pltpu.SemaphoreType.DMA((2, 2 * group)),
            pltpu.VMEM((NPNO, NPNO), jnp.float32),
        ],
    )
    flops = count * 2 * 4 * 2 * NPNO * NPNO * NPNO
    kernel = functools.partial(
        coupling_kernel,
        mode=mode,
        final=final,
        width=sources[0].shape[0],
        group=group,
        start=start,
        nsrc=len(sources),
    )
    return pl.pallas_call(
        kernel,
        grid_spec=grid_spec,
        out_shape=jax.ShapeDtypeStruct((count, NPNO, NPNO), jnp.float32),
        cost_estimate=pl.CostEstimate(
            flops=flops,
            bytes_accessed=count * NPNO * NPNO * (2 * 4 + 2 * 2 + 3 * 4),
            transcendentals=0,
        ),
    )(nb, sizes, fock, *operands)


def chunked_halo(chunks):
    received = [halo_sources(chunk, "pair") for chunk in chunks]
    return [r[k] for k in range(3) for r in received]


def per_device(
    three_index,
    pno_coef,
    pair_orbitals,
    natural_orbital_class,
    pno_energy,
    margin,
    neighbour_pairs,
    fock_coupling,
):
    occ_dev = three_index.shape[0]
    pair_dev = pno_coef.shape[0]
    position = lax.axis_index("pair")
    sizes = class_size(natural_orbital_class)
    blocks = halo_sources(three_index, "pair")
    local_orbitals = (pair_orbitals - (position - 1) * occ_dev).astype(jnp.int32)
    half = pair_dev // 2
    halves = [
        partial_exchange(
            local_orbitals[:, 0] - occ_dev,
            local_orbitals[:, 1],
            sizes,
            blocks,
            jnp.swapaxes(pno_coef, 2, 3),
            start,
            half,
        )
        for start in (0, half)
    ]
    exchange_ints = sum_over_aux(halves)
    denominator = pno_energy[:, :, None] + pno_energy[:, None, :]
    local_rows = (neighbour_pairs - (position - 1) * pair_dev).astype(jnp.int32).reshape(-1)
    fock = fock_coupling.reshape(-1)

    chunk = pair_dev // 2 if pair_dev % 8 == 0 else pair_dev
    amplitudes = -(exchange_ints / denominator)
    sources = chunked_halo([amplitudes])
    for iteration in range(1, ITERS):
        local = coupling_step(
            local_rows, sizes, fock, [amplitudes], margin, None, None, None, False, mode="local"
        )
        parts = [
            coupling_step(
                local_rows, sizes, fock, sources, margin, exchange_ints, pno_energy, amplitudes,
                False, c * chunk, chunk, mode="remote", partial=local[c * chunk:(c + 1) * chunk],
            )
            for c in range(pair_dev // chunk)
        ]
        sources = chunked_halo(parts)
        amplitudes = jnp.concatenate(parts, axis=0)
    residual = coupling_step(
        local_rows, sizes, fock, sources, margin, exchange_ints, pno_energy, amplitudes, True
    )
    return (amplitudes, residual)


def solution(mesh):
    return jax.shard_map(
        per_device,
        mesh=mesh,
        in_specs=(
            P("pair", "aux", None),
            P("pair", None, None, None),
            P("pair", None),
            P("pair"),
            P("pair", None),
            P("pair", None, None, None),
            P("pair", None),
            P("pair", None),
        ),
        out_specs=(P("pair", None, None), P("pair", None, None)),
        check_vma=False,
    )
```

```python
import functools

import jax
import jax.numpy as jnp
from jax import lax
from jax.experimental import pallas as pl
from jax.experimental.pallas import tpu as pltpu
from jax.sharding import PartitionSpec as P

NPNO = 192
ITERS = 2
CLASS_SIZES = (NPNO // 6, NPNO // 3, 2 * NPNO // 3, NPNO)


def halo_sources(cells, axis):
    count = lax.axis_size(axis)
    ends = count - 1
    from_left = lax.ppermute(cells, axis, [(i, i + 1) for i in range(ends)])
    from_right = lax.ppermute(cells, axis, [(i + 1, i) for i in range(ends)])
    return (from_left, cells, from_right)


def halving_stream(piece, index, count, bits):
    for bit in bits:
        side = (index // bit) % 2
        half = piece.shape[0] // 2
        keep = lax.dynamic_slice_in_dim(piece, side * half, half, axis=0)
        send = lax.dynamic_slice_in_dim(piece, (1 - side) * half, half, axis=0)
        piece = keep + lax.ppermute(send, "aux", [(i, i ^ bit) for i in range(count)])
    for bit in reversed(bits):
        side = (index // bit) % 2
        other = lax.ppermute(piece, "aux", [(i, i ^ bit) for i in range(count)])
        length = piece.shape[0]
        full = jnp.zeros((2 * length,) + piece.shape[1:], piece.dtype)
        full = lax.dynamic_update_slice_in_dim(full, piece, side * length, axis=0)
        piece = lax.dynamic_update_slice_in_dim(full, other, (1 - side) * length, axis=0)
    return piece


def sum_over_aux(halves):
    count = lax.axis_size("aux")
    if count != 4 or halves[0].shape[0] % 4:
        return lax.psum(jnp.concatenate(halves, axis=0), "aux")
    index = lax.axis_index("aux")
    first = halving_stream(halves[0], index, count, (1, 2))
    second = halving_stream(halves[1], index, count, (2, 1))
    return jnp.concatenate([first, second], axis=0)


def class_size(natural_orbital_class):
    return jnp.where(
        natural_orbital_class == 0,
        NPNO // 6,
        jnp.where(
            natural_orbital_class == 1,
            NPNO // 3,
            jnp.where(natural_orbital_class == 2, 2 * NPNO // 3, NPNO),
        ),
    ).astype(jnp.int32)


def fetch_block(sources, width, local, dst, sem):
    index = jnp.clip(local // width, 0, len(sources) - 1)
    row = local % width
    for k, src in enumerate(sources):

        @pl.when(index == k)
        def _():
            pltpu.make_async_copy(src.at[row], dst, sem).start()


def exchange_kernel(
    lead_ref, trail_ref, size_ref, t_left, t_own, t_right, coef_ref, out_ref, lbuf, tbuf, sems, *, occ, group, start
):
    i = pl.program_id(0)
    steps = pl.num_programs(0)
    sources = (t_left, t_own, t_right)

    def fetch(step, slot):
        for g in range(group):
            p = start + step * group + g
            pltpu.make_async_copy(t_own.at[lead_ref[p] % occ], lbuf.at[slot, g], sems.at[slot, 0, g]).start()
            fetch_block(sources, occ, trail_ref[p], tbuf.at[slot, g], sems.at[slot, 1, g])

    @pl.when(i == 0)
    def _():
        fetch(0, 0)

    @pl.when(i + 1 < steps)
    def _():
        fetch(i + 1, (i + 1) % 2)

    slot = i % 2
    transposed = (((1,), (1,)), ((), ()))
    for g in range(group):
        p = start + i * group + g
        pltpu.make_async_copy(t_own.at[0], lbuf.at[slot, g], sems.at[slot, 0, g]).wait()
        pltpu.make_async_copy(t_own.at[0], tbuf.at[slot, g], sems.at[slot, 1, g]).wait()
        size = size_ref[p]
        out_ref[g] = jnp.zeros((NPNO, NPNO), jnp.float32)
        for m in CLASS_SIZES:

            @pl.when(size == m)
            def _():
                first = coef_ref[g, 0, :m, :]
                second = coef_ref[g, 1, :m, :]
                left_t = lax.dot_general(first, lbuf[slot, g], transposed, preferred_element_type=jnp.float32)
                right = lax.dot_general(tbuf[slot, g], second, transposed, preferred_element_type=jnp.float32)
                out_ref[g, :m, :m] = jnp.dot(
                    left_t.astype(jnp.bfloat16), right.astype(jnp.bfloat16), preferred_element_type=jnp.float32
                )


def partial_exchange(lead, trail, sizes, sources, coef_t, start=0, count=None):
    pairs = coef_t.shape[0]
    count = pairs if count is None else count
    group = next(g for g in (4, 2, 1) if count % g == 0 and start % g == 0)
    base = start // group
    occ, nfit, npao = sources[1].shape
    hbm = pl.BlockSpec(memory_space=pl.ANY)
    grid_spec = pltpu.PrefetchScalarGridSpec(
        num_scalar_prefetch=3,
        grid=(count // group,),
        in_specs=[
            hbm,
            hbm,
            hbm,
            pl.BlockSpec((group, 2, NPNO, npao), lambda i, a, b, s: (i + base, 0, 0, 0)),
        ],
        out_specs=pl.BlockSpec((group, NPNO, NPNO), lambda i, a, b, s: (i, 0, 0)),
        scratch_shapes=[
            pltpu.VMEM((2, group, nfit, npao), sources[1].dtype),
            pltpu.VMEM((2, group, nfit, npao), sources[1].dtype),
            pltpu.SemaphoreType.DMA((2, 2, group)),
        ],
    )
    flops = count * (2 * 2 * nfit * npao * NPNO + 2 * nfit * NPNO * NPNO)
    return pl.pallas_call(
        functools.partial(exchange_kernel, occ=occ, group=group, start=start),
        grid_spec=grid_spec,
        out_shape=jax.ShapeDtypeStruct((count, NPNO, NPNO), jnp.float32),
        cost_estimate=pl.CostEstimate(
            flops=flops,
            bytes_accessed=count * (2 * nfit * npao * 2 + 2 * npao * NPNO * 2 + NPNO * NPNO * 4),
            transcendentals=0,
        ),
    )(lead, trail, sizes, *sources, coef_t)


def split_bf16(value):
    hi = value.astype(jnp.bfloat16)
    lo = (value - hi.astype(jnp.float32)).astype(jnp.bfloat16)
    return hi, lo


def mm(lhs, rhs, dims=(((1,), (0,)), ((), ()))):
    return lax.dot_general(lhs, rhs, dims, preferred_element_type=jnp.float32)


def coupling_kernel(nb_ref, size_ref, fock_ref, *refs, final, width, group, start, nsrc):
    sources = refs[:nsrc]
    margin_ref, ex_ref, col_ref, row_ref, own_ref, out_ref, tbuf, sems = refs[nsrc:]
    i = pl.program_id(0)
    steps = pl.num_programs(0)

    def fetch(step, slot):
        for k in range(2 * group):
            fetch_block(sources, width, nb_ref[2 * (start + group * step) + k], tbuf.at[slot, k], sems.at[slot, k])

    @pl.when(i == 0)
    def _():
        fetch(0, 0)

    @pl.when(i + 1 < steps)
    def _():
        fetch(i + 1, (i + 1) % 2)

    slot = i % 2
    transposed = (((1,), (1,)), ((), ()))
    for g in range(group):
        p = start + i * group + g
        splits = []
        for n in range(2):
            k = 2 * g + n
            pltpu.make_async_copy(sources[0].at[0], tbuf.at[slot, k], sems.at[slot, k]).wait()
            splits.append(split_bf16(tbuf[slot, k]))
        size = size_ref[p]
        out_ref[g] = jnp.zeros((NPNO, NPNO), jnp.float32)
        for m in CLASS_SIZES:

            @pl.when(size == m)
            def _():
                total = None
                for n in range(2):
                    side = margin_ref[g, n, :m, :]
                    t_hi, t_lo = splits[n]
                    inner = mm(side, t_hi) + mm(side, t_lo)
                    w_hi, w_lo = split_bf16(fock_ref[2 * p + n] * inner)
                    outer = mm(w_hi, side, transposed) + mm(w_lo, side, transposed)
                    total = outer if total is None else total + outer
                denominator = col_ref[g, :m, :] + row_ref[g, :, :m]
                amplitudes = own_ref[g, :m, :m]
                residual = ex_ref[g, :m, :m] + denominator * amplitudes - total
                if final:
                    out_ref[g, :m, :m] = residual
                else:
                    out_ref[g, :m, :m] = amplitudes - residual / denominator


def coupling_step(nb, sizes, fock, sources, margin, exchange, energy, own, final, start=0, count=None):
    pairs = own.shape[0]
    count = pairs if count is None else count
    group = next(g for g in (4, 2, 1) if count % g == 0 and start % g == 0)
    base = start // group
    column = energy.reshape(pairs, NPNO, 1)
    row = energy.reshape(pairs, 1, NPNO)
    hbm = pl.BlockSpec(memory_space=pl.ANY)
    own_spec = pl.BlockSpec((group, NPNO, NPNO), lambda i, q, s, f: (i + base, 0, 0))
    grid_spec = pltpu.PrefetchScalarGridSpec(
        num_scalar_prefetch=3,
        grid=(count // group,),
        in_specs=[hbm] * len(sources)
        + [
            pl.BlockSpec((group, 2, NPNO, NPNO), lambda i, q, s, f: (i + base, 0, 0, 0)),
            own_spec,
            pl.BlockSpec((group, NPNO, 1), lambda i, q, s, f: (i + base, 0, 0)),
            pl.BlockSpec((group, 1, NPNO), lambda i, q, s, f: (i + base, 0, 0)),
            own_spec,
        ],
        out_specs=pl.BlockSpec((group, NPNO, NPNO), lambda i, q, s, f: (i, 0, 0)),
        scratch_shapes=[
            pltpu.VMEM((2, 2 * group, NPNO, NPNO), jnp.float32),
            pltpu.SemaphoreType.DMA((2, 2 * group)),
        ],
    )
    flops = count * 2 * 4 * 2 * NPNO * NPNO * NPNO
    kernel = functools.partial(
        coupling_kernel, final=final, width=sources[0].shape[0], group=group, start=start, nsrc=len(sources)
    )
    return pl.pallas_call(
        kernel,
        grid_spec=grid_spec,
        out_shape=jax.ShapeDtypeStruct((count, NPNO, NPNO), jnp.float32),
        cost_estimate=pl.CostEstimate(
            flops=flops,
            bytes_accessed=count * NPNO * NPNO * (2 * 4 + 2 * 2 + 3 * 4),
            transcendentals=0,
        ),
    )(nb, sizes, fock, *sources, margin, exchange, column, row, own)


def chunked_halo(chunks):
    received = [halo_sources(chunk, "pair") for chunk in chunks]
    return [r[k] for k in range(3) for r in received]


def per_device(
    three_index,
    pno_coef,
    pair_orbitals,
    natural_orbital_class,
    pno_energy,
    margin,
    neighbour_pairs,
    fock_coupling,
):
    occ_dev = three_index.shape[0]
    pair_dev = pno_coef.shape[0]
    position = lax.axis_index("pair")
    sizes = class_size(natural_orbital_class)
    blocks = halo_sources(three_index, "pair")
    local_orbitals = (pair_orbitals - (position - 1) * occ_dev).astype(jnp.int32)
    half = pair_dev // 2
    halves = [
        partial_exchange(
            local_orbitals[:, 0] - occ_dev,
            local_orbitals[:, 1],
            sizes,
            blocks,
            jnp.swapaxes(pno_coef, 2, 3),
            start,
            half,
        )
        for start in (0, half)
    ]
    exchange_ints = sum_over_aux(halves)
    denominator = pno_energy[:, :, None] + pno_energy[:, None, :]
    local_rows = (neighbour_pairs - (position - 1) * pair_dev).astype(jnp.int32).reshape(-1)
    fock = fock_coupling.reshape(-1)

    chunk = pair_dev // 2 if pair_dev % 8 == 0 else pair_dev
    parts = [-(exchange_ints / denominator)]
    sources = chunked_halo(parts)
    amplitudes = jnp.concatenate(parts, axis=0)
    for iteration in range(1, ITERS):
        parts = [
            coupling_step(
                local_rows, sizes, fock, sources, margin, exchange_ints, pno_energy, amplitudes,
                False, c * chunk, chunk,
            )
            for c in range(pair_dev // chunk)
        ]
        sources = chunked_halo(parts)
        amplitudes = jnp.concatenate(parts, axis=0)
    residual = coupling_step(
        local_rows, sizes, fock, sources, margin, exchange_ints, pno_energy, amplitudes, True
    )
    return (amplitudes, residual)


def solution(mesh):
    return jax.shard_map(
        per_device,
        mesh=mesh,
        in_specs=(
            P("pair", "aux", None),
            P("pair", None, None, None),
            P("pair", None),
            P("pair"),
            P("pair", None),
            P("pair", None, None, None),
            P("pair", None),
            P("pair", None),
        ),
        out_specs=(P("pair", None, None), P("pair", None, None)),
        check_vma=False,
    )
```

```python
import functools

import jax
import jax.numpy as jnp
from jax import lax
from jax.experimental import pallas as pl
from jax.experimental.pallas import tpu as pltpu
from jax.sharding import PartitionSpec as P

NPNO = 192
ITERS = 2
CLASS_SIZES = (NPNO // 6, NPNO // 3, 2 * NPNO // 3, NPNO)


def halo_sources(cells, axis):
    count = lax.axis_size(axis)
    ends = count - 1
    from_left = lax.ppermute(cells, axis, [(i, i + 1) for i in range(ends)])
    from_right = lax.ppermute(cells, axis, [(i + 1, i) for i in range(ends)])
    return (from_left, cells, from_right)


def halving_stream(piece, index, count, bits):
    for bit in bits:
        side = (index // bit) % 2
        half = piece.shape[0] // 2
        keep = lax.dynamic_slice_in_dim(piece, side * half, half, axis=0)
        send = lax.dynamic_slice_in_dim(piece, (1 - side) * half, half, axis=0)
        piece = keep + lax.ppermute(send, "aux", [(i, i ^ bit) for i in range(count)])
    for bit in reversed(bits):
        side = (index // bit) % 2
        other = lax.ppermute(piece, "aux", [(i, i ^ bit) for i in range(count)])
        length = piece.shape[0]
        full = jnp.zeros((2 * length,) + piece.shape[1:], piece.dtype)
        full = lax.dynamic_update_slice_in_dim(full, piece, side * length, axis=0)
        piece = lax.dynamic_update_slice_in_dim(full, other, (1 - side) * length, axis=0)
    return piece


def sum_over_aux(halves):
    count = lax.axis_size("aux")
    if count != 4 or halves[0].shape[0] % 4:
        return [lax.psum(half, "aux") for half in halves]
    index = lax.axis_index("aux")
    return [
        halving_stream(halves[0], index, count, (1, 2)),
        halving_stream(halves[1], index, count, (2, 1)),
    ]


def class_size(natural_orbital_class):
    return jnp.where(
        natural_orbital_class == 0,
        NPNO // 6,
        jnp.where(
            natural_orbital_class == 1,
            NPNO // 3,
            jnp.where(natural_orbital_class == 2, 2 * NPNO // 3, NPNO),
        ),
    ).astype(jnp.int32)


def fetch_block(sources, width, local, dst, sem):
    index = jnp.clip(local // width, 0, len(sources) - 1)
    row = local % width
    for k, src in enumerate(sources):

        @pl.when(index == k)
        def _():
            pltpu.make_async_copy(src.at[row], dst, sem).start()


def exchange_kernel(
    lead_ref, trail_ref, size_ref, t_left, t_own, t_right, coef_ref, out_ref, lbuf, tbuf, sems, *, occ, group, start
):
    i = pl.program_id(0)
    steps = pl.num_programs(0)
    sources = (t_left, t_own, t_right)

    def fetch(step, slot):
        for g in range(group):
            p = start + step * group + g
            pltpu.make_async_copy(t_own.at[lead_ref[p] % occ], lbuf.at[slot, g], sems.at[slot, 0, g]).start()
            fetch_block(sources, occ, trail_ref[p], tbuf.at[slot, g], sems.at[slot, 1, g])

    @pl.when(i == 0)
    def _():
        fetch(0, 0)

    @pl.when(i + 1 < steps)
    def _():
        fetch(i + 1, (i + 1) % 2)

    slot = i % 2
    transposed = (((1,), (1,)), ((), ()))
    for g in range(group):
        p = start + i * group + g
        pltpu.make_async_copy(t_own.at[0], lbuf.at[slot, g], sems.at[slot, 0, g]).wait()
        pltpu.make_async_copy(t_own.at[0], tbuf.at[slot, g], sems.at[slot, 1, g]).wait()
        size = size_ref[p]
        out_ref[g] = jnp.zeros((NPNO, NPNO), jnp.float32)
        for m in CLASS_SIZES:

            @pl.when(size == m)
            def _():
                first = coef_ref[g, 0, :m, :]
                second = coef_ref[g, 1, :m, :]
                left_t = lax.dot_general(first, lbuf[slot, g], transposed, preferred_element_type=jnp.float32)
                right = lax.dot_general(tbuf[slot, g], second, transposed, preferred_element_type=jnp.float32)
                out_ref[g, :m, :m] = jnp.dot(
                    left_t.astype(jnp.bfloat16), right.astype(jnp.bfloat16), preferred_element_type=jnp.float32
                )


def partial_exchange(lead, trail, sizes, sources, coef_t, start=0, count=None):
    pairs = coef_t.shape[0]
    count = pairs if count is None else count
    group = next(g for g in (4, 2, 1) if count % g == 0 and start % g == 0)
    base = start // group
    occ, nfit, npao = sources[1].shape
    hbm = pl.BlockSpec(memory_space=pl.ANY)
    grid_spec = pltpu.PrefetchScalarGridSpec(
        num_scalar_prefetch=3,
        grid=(count // group,),
        in_specs=[
            hbm,
            hbm,
            hbm,
            pl.BlockSpec((group, 2, NPNO, npao), lambda i, a, b, s: (i + base, 0, 0, 0)),
        ],
        out_specs=pl.BlockSpec((group, NPNO, NPNO), lambda i, a, b, s: (i, 0, 0)),
        scratch_shapes=[
            pltpu.VMEM((2, group, nfit, npao), sources[1].dtype),
            pltpu.VMEM((2, group, nfit, npao), sources[1].dtype),
            pltpu.SemaphoreType.DMA((2, 2, group)),
        ],
    )
    flops = count * (2 * 2 * nfit * npao * NPNO + 2 * nfit * NPNO * NPNO)
    return pl.pallas_call(
        functools.partial(exchange_kernel, occ=occ, group=group, start=start),
        grid_spec=grid_spec,
        out_shape=jax.ShapeDtypeStruct((count, NPNO, NPNO), jnp.float32),
        cost_estimate=pl.CostEstimate(
            flops=flops,
            bytes_accessed=count * (2 * nfit * npao * 2 + 2 * npao * NPNO * 2 + NPNO * NPNO * 4),
            transcendentals=0,
        ),
    )(lead, trail, sizes, *sources, coef_t)


def split_bf16(value):
    hi = value.astype(jnp.bfloat16)
    lo = (value - hi.astype(jnp.float32)).astype(jnp.bfloat16)
    return hi, lo


def mm(lhs, rhs, dims=(((1,), (0,)), ((), ()))):
    return lax.dot_general(lhs, rhs, dims, preferred_element_type=jnp.float32)


def coupling_kernel(nb_ref, size_ref, fock_ref, *refs, final, width, group, start, nsrc):
    sources = refs[:nsrc]
    margin_ref, ex_ref, col_ref, row_ref, own_ref, out_ref, tbuf, sems = refs[nsrc:]
    i = pl.program_id(0)
    steps = pl.num_programs(0)

    def fetch(step, slot):
        for k in range(2 * group):
            fetch_block(sources, width, nb_ref[2 * (start + group * step) + k], tbuf.at[slot, k], sems.at[slot, k])

    @pl.when(i == 0)
    def _():
        fetch(0, 0)

    @pl.when(i + 1 < steps)
    def _():
        fetch(i + 1, (i + 1) % 2)

    slot = i % 2
    transposed = (((1,), (1,)), ((), ()))
    for g in range(group):
        p = start + i * group + g
        splits = []
        for n in range(2):
            k = 2 * g + n
            pltpu.make_async_copy(sources[0].at[0], tbuf.at[slot, k], sems.at[slot, k]).wait()
            splits.append(split_bf16(tbuf[slot, k]))
        size = size_ref[p]
        out_ref[g] = jnp.zeros((NPNO, NPNO), jnp.float32)
        for m in CLASS_SIZES:

            @pl.when(size == m)
            def _():
                total = None
                for n in range(2):
                    side = margin_ref[g, n, :m, :]
                    t_hi, t_lo = splits[n]
                    inner = mm(side, t_hi) + mm(side, t_lo)
                    w_hi, w_lo = split_bf16(fock_ref[2 * p + n] * inner)
                    outer = mm(w_hi, side, transposed) + mm(w_lo, side, transposed)
                    total = outer if total is None else total + outer
                denominator = col_ref[g, :m, :] + row_ref[g, :, :m]
                amplitudes = own_ref[g, :m, :m]
                residual = ex_ref[g, :m, :m] + denominator * amplitudes - total
                if final:
                    out_ref[g, :m, :m] = residual
                else:
                    out_ref[g, :m, :m] = amplitudes - residual / denominator


def coupling_step(nb, sizes, fock, sources, margin, exchange, energy, own, final, start=0, count=None):
    pairs = own.shape[0]
    count = pairs if count is None else count
    group = next(g for g in (4, 2, 1) if count % g == 0 and start % g == 0)
    base = start // group
    column = energy.reshape(pairs, NPNO, 1)
    row = energy.reshape(pairs, 1, NPNO)
    hbm = pl.BlockSpec(memory_space=pl.ANY)
    own_spec = pl.BlockSpec((group, NPNO, NPNO), lambda i, q, s, f: (i + base, 0, 0))
    grid_spec = pltpu.PrefetchScalarGridSpec(
        num_scalar_prefetch=3,
        grid=(count // group,),
        in_specs=[hbm] * len(sources)
        + [
            pl.BlockSpec((group, 2, NPNO, NPNO), lambda i, q, s, f: (i + base, 0, 0, 0)),
            own_spec,
            pl.BlockSpec((group, NPNO, 1), lambda i, q, s, f: (i + base, 0, 0)),
            pl.BlockSpec((group, 1, NPNO), lambda i, q, s, f: (i + base, 0, 0)),
            own_spec,
        ],
        out_specs=pl.BlockSpec((group, NPNO, NPNO), lambda i, q, s, f: (i, 0, 0)),
        scratch_shapes=[
            pltpu.VMEM((2, 2 * group, NPNO, NPNO), jnp.float32),
            pltpu.SemaphoreType.DMA((2, 2 * group)),
        ],
    )
    flops = count * 2 * 4 * 2 * NPNO * NPNO * NPNO
    kernel = functools.partial(
        coupling_kernel, final=final, width=sources[0].shape[0], group=group, start=start, nsrc=len(sources)
    )
    return pl.pallas_call(
        kernel,
        grid_spec=grid_spec,
        out_shape=jax.ShapeDtypeStruct((count, NPNO, NPNO), jnp.float32),
        cost_estimate=pl.CostEstimate(
            flops=flops,
            bytes_accessed=count * NPNO * NPNO * (2 * 4 + 2 * 2 + 3 * 4),
            transcendentals=0,
        ),
    )(nb, sizes, fock, *sources, margin, exchange, column, row, own)


def chunked_halo(chunks):
    received = [halo_sources(chunk, "pair") for chunk in chunks]
    return [r[k] for k in range(3) for r in received]


def per_device(
    three_index,
    pno_coef,
    pair_orbitals,
    natural_orbital_class,
    pno_energy,
    margin,
    neighbour_pairs,
    fock_coupling,
):
    occ_dev = three_index.shape[0]
    pair_dev = pno_coef.shape[0]
    position = lax.axis_index("pair")
    sizes = class_size(natural_orbital_class)
    blocks = halo_sources(three_index, "pair")
    local_orbitals = (pair_orbitals - (position - 1) * occ_dev).astype(jnp.int32)
    half = pair_dev // 2
    halves = [
        partial_exchange(
            local_orbitals[:, 0] - occ_dev,
            local_orbitals[:, 1],
            sizes,
            blocks,
            jnp.swapaxes(pno_coef, 2, 3),
            start,
            half,
        )
        for start in (0, half)
    ]
    exchange_halves = sum_over_aux(halves)
    exchange_ints = jnp.concatenate(exchange_halves, axis=0)
    denominator = pno_energy[:, :, None] + pno_energy[:, None, :]
    local_rows = (neighbour_pairs - (position - 1) * pair_dev).astype(jnp.int32).reshape(-1)
    fock = fock_coupling.reshape(-1)

    chunk = pair_dev // 2 if pair_dev % 8 == 0 else pair_dev
    parts = [
        -(part / denominator[c * half:(c + 1) * half]) for c, part in enumerate(exchange_halves)
    ]
    sources = chunked_halo(parts)
    amplitudes = jnp.concatenate(parts, axis=0)
    for iteration in range(1, ITERS):
        parts = [
            coupling_step(
                local_rows, sizes, fock, sources, margin, exchange_ints, pno_energy, amplitudes,
                False, c * chunk, chunk,
            )
            for c in range(pair_dev // chunk)
        ]
        sources = chunked_halo(parts)
        amplitudes = jnp.concatenate(parts, axis=0)
    residual = coupling_step(
        local_rows, sizes, fock, sources, margin, exchange_ints, pno_energy, amplitudes, True
    )
    return (amplitudes, residual)


def solution(mesh):
    return jax.shard_map(
        per_device,
        mesh=mesh,
        in_specs=(
            P("pair", "aux", None),
            P("pair", None, None, None),
            P("pair", None),
            P("pair"),
            P("pair", None),
            P("pair", None, None, None),
            P("pair", None),
            P("pair", None),
        ),
        out_specs=(P("pair", None, None), P("pair", None, None)),
        check_vma=False,
    )
```

```python
import functools

import jax
import jax.numpy as jnp
from jax import lax
from jax.experimental import pallas as pl
from jax.experimental.pallas import tpu as pltpu
from jax.sharding import PartitionSpec as P

NPNO = 192
ITERS = 2
CLASS_SIZES = (NPNO // 6, NPNO // 3, 2 * NPNO // 3, NPNO)


def halo_sources(cells, axis):
    count = lax.axis_size(axis)
    ends = count - 1
    from_left = lax.ppermute(cells, axis, [(i, i + 1) for i in range(ends)])
    from_right = lax.ppermute(cells, axis, [(i + 1, i) for i in range(ends)])
    return (from_left, cells, from_right)


def halving_stream(piece, index, count, bits, presplit=False):
    for step, bit in enumerate(bits):
        side = (index // bit) % 2
        half = piece.shape[0] // 2
        if presplit and step == 0:
            keep, send = piece[half:], piece[:half]
        else:
            keep = lax.dynamic_slice_in_dim(piece, side * half, half, axis=0)
            send = lax.dynamic_slice_in_dim(piece, (1 - side) * half, half, axis=0)
        piece = keep + lax.ppermute(send, "aux", [(i, i ^ bit) for i in range(count)])
    for bit in reversed(bits):
        side = (index // bit) % 2
        other = lax.ppermute(piece, "aux", [(i, i ^ bit) for i in range(count)])
        length = piece.shape[0]
        full = jnp.zeros((2 * length,) + piece.shape[1:], piece.dtype)
        full = lax.dynamic_update_slice_in_dim(full, piece, side * length, axis=0)
        piece = lax.dynamic_update_slice_in_dim(full, other, (1 - side) * length, axis=0)
    return piece


def halving_ready(halves):
    return lax.axis_size("aux") == 4 and halves % 8 == 0


def send_first(half_index):
    index = lax.axis_index("aux")
    return (1 - (index // (1, 2)[half_index]) % 2).astype(jnp.int32).reshape(1)


def sum_over_aux(halves, presplit):
    count = lax.axis_size("aux")
    if not halving_ready(halves[0].shape[0]):
        return lax.psum(jnp.concatenate(halves, axis=0), "aux")
    index = lax.axis_index("aux")
    first = halving_stream(halves[0], index, count, (1, 2), presplit)
    second = halving_stream(halves[1], index, count, (2, 1), presplit)
    return jnp.concatenate([first, second], axis=0)


def class_size(natural_orbital_class):
    return jnp.where(
        natural_orbital_class == 0,
        NPNO // 6,
        jnp.where(
            natural_orbital_class == 1,
            NPNO // 3,
            jnp.where(natural_orbital_class == 2, 2 * NPNO // 3, NPNO),
        ),
    ).astype(jnp.int32)


def fetch_block(sources, width, local, dst, sem):
    index = jnp.clip(local // width, 0, len(sources) - 1)
    row = local % width
    for k, src in enumerate(sources):

        @pl.when(index == k)
        def _():
            pltpu.make_async_copy(src.at[row], dst, sem).start()


def exchange_kernel(
    lead_ref, trail_ref, size_ref, flip_ref, t_left, t_own, t_right, coef_ref, out_ref, lbuf, tbuf, sems, *, occ, group, start
):
    i = pl.program_id(0)
    steps = pl.num_programs(0)
    sources = (t_left, t_own, t_right)

    def fetch(step, slot):
        for g in range(group):
            p = start + step * group + g
            pltpu.make_async_copy(t_own.at[lead_ref[p] % occ], lbuf.at[slot, g], sems.at[slot, 0, g]).start()
            fetch_block(sources, occ, trail_ref[p], tbuf.at[slot, g], sems.at[slot, 1, g])

    @pl.when(i == 0)
    def _():
        fetch(0, 0)

    @pl.when(i + 1 < steps)
    def _():
        fetch(i + 1, (i + 1) % 2)

    slot = i % 2
    transposed = (((1,), (1,)), ((), ()))
    for g in range(group):
        p = start + i * group + g
        pltpu.make_async_copy(t_own.at[0], lbuf.at[slot, g], sems.at[slot, 0, g]).wait()
        pltpu.make_async_copy(t_own.at[0], tbuf.at[slot, g], sems.at[slot, 1, g]).wait()
        size = size_ref[p]
        out_ref[g] = jnp.zeros((NPNO, NPNO), jnp.float32)
        for m in CLASS_SIZES:

            @pl.when(size == m)
            def _():
                first = coef_ref[g, 0, :m, :]
                second = coef_ref[g, 1, :m, :]
                left_t = lax.dot_general(first, lbuf[slot, g], transposed, preferred_element_type=jnp.float32)
                right = lax.dot_general(tbuf[slot, g], second, transposed, preferred_element_type=jnp.float32)
                out_ref[g, :m, :m] = jnp.dot(
                    left_t.astype(jnp.bfloat16), right.astype(jnp.bfloat16), preferred_element_type=jnp.float32
                )


def partial_exchange(lead, trail, sizes, sources, coef_t, start=0, count=None, flip=None):
    pairs = coef_t.shape[0]
    count = pairs if count is None else count
    group = next(g for g in (4, 2, 1) if count % g == 0 and start % g == 0)
    base = start // group
    steps = count // group
    if flip is None or steps != 2:
        flip = jnp.zeros((1,), jnp.int32)
    occ, nfit, npao = sources[1].shape
    hbm = pl.BlockSpec(memory_space=pl.ANY)
    grid_spec = pltpu.PrefetchScalarGridSpec(
        num_scalar_prefetch=4,
        grid=(steps,),
        in_specs=[
            hbm,
            hbm,
            hbm,
            pl.BlockSpec((group, 2, NPNO, npao), lambda i, a, b, s, f: (i + base, 0, 0, 0)),
        ],
        out_specs=pl.BlockSpec((group, NPNO, NPNO), lambda i, a, b, s, f: ((i + f[0]) % steps, 0, 0)),
        scratch_shapes=[
            pltpu.VMEM((2, group, nfit, npao), sources[1].dtype),
            pltpu.VMEM((2, group, nfit, npao), sources[1].dtype),
            pltpu.SemaphoreType.DMA((2, 2, group)),
        ],
    )
    flops = count * (2 * 2 * nfit * npao * NPNO + 2 * nfit * NPNO * NPNO)
    return pl.pallas_call(
        functools.partial(exchange_kernel, occ=occ, group=group, start=start),
        grid_spec=grid_spec,
        out_shape=jax.ShapeDtypeStruct((count, NPNO, NPNO), jnp.float32),
        cost_estimate=pl.CostEstimate(
            flops=flops,
            bytes_accessed=count * (2 * nfit * npao * 2 + 2 * npao * NPNO * 2 + NPNO * NPNO * 4),
            transcendentals=0,
        ),
    )(lead, trail, sizes, flip, *sources, coef_t)


def split_bf16(value):
    hi = value.astype(jnp.bfloat16)
    lo = (value - hi.astype(jnp.float32)).astype(jnp.bfloat16)
    return hi, lo


def mm(lhs, rhs, dims=(((1,), (0,)), ((), ()))):
    return lax.dot_general(lhs, rhs, dims, preferred_element_type=jnp.float32)


def coupling_kernel(nb_ref, size_ref, fock_ref, *refs, final, width, group, start, nsrc):
    sources = refs[:nsrc]
    margin_ref, ex_ref, col_ref, row_ref, own_ref, out_ref, tbuf, sems = refs[nsrc:]
    i = pl.program_id(0)
    steps = pl.num_programs(0)

    def fetch(step, slot):
        for k in range(2 * group):
            fetch_block(sources, width, nb_ref[2 * (start + group * step) + k], tbuf.at[slot, k], sems.at[slot, k])

    @pl.when(i == 0)
    def _():
        fetch(0, 0)

    @pl.when(i + 1 < steps)
    def _():
        fetch(i + 1, (i + 1) % 2)

    slot = i % 2
    transposed = (((1,), (1,)), ((), ()))
    for g in range(group):
        p = start + i * group + g
        splits = []
        for n in range(2):
            k = 2 * g + n
            pltpu.make_async_copy(sources[0].at[0], tbuf.at[slot, k], sems.at[slot, k]).wait()
            splits.append(split_bf16(tbuf[slot, k]))
        size = size_ref[p]
        out_ref[g] = jnp.zeros((NPNO, NPNO), jnp.float32)
        for m in CLASS_SIZES:

            @pl.when(size == m)
            def _():
                total = None
                for n in range(2):
                    side = margin_ref[g, n, :m, :]
                    t_hi, t_lo = splits[n]
                    inner = mm(side, t_hi) + mm(side, t_lo)
                    w_hi, w_lo = split_bf16(fock_ref[2 * p + n] * inner)
                    outer = mm(w_hi, side, transposed) + mm(w_lo, side, transposed)
                    total = outer if total is None else total + outer
                denominator = col_ref[g, :m, :] + row_ref[g, :, :m]
                amplitudes = own_ref[g, :m, :m]
                residual = ex_ref[g, :m, :m] + denominator * amplitudes - total
                if final:
                    out_ref[g, :m, :m] = residual
                else:
                    out_ref[g, :m, :m] = amplitudes - residual / denominator


def coupling_step(nb, sizes, fock, sources, margin, exchange, energy, own, final, start=0, count=None):
    pairs = own.shape[0]
    count = pairs if count is None else count
    group = next(g for g in (4, 2, 1) if count % g == 0 and start % g == 0)
    base = start // group
    column = energy.reshape(pairs, NPNO, 1)
    row = energy.reshape(pairs, 1, NPNO)
    hbm = pl.BlockSpec(memory_space=pl.ANY)
    own_spec = pl.BlockSpec((group, NPNO, NPNO), lambda i, q, s, f: (i + base, 0, 0))
    grid_spec = pltpu.PrefetchScalarGridSpec(
        num_scalar_prefetch=3,
        grid=(count // group,),
        in_specs=[hbm] * len(sources)
        + [
            pl.BlockSpec((group, 2, NPNO, NPNO), lambda i, q, s, f: (i + base, 0, 0, 0)),
            own_spec,
            pl.BlockSpec((group, NPNO, 1), lambda i, q, s, f: (i + base, 0, 0)),
            pl.BlockSpec((group, 1, NPNO), lambda i, q, s, f: (i + base, 0, 0)),
            own_spec,
        ],
        out_specs=pl.BlockSpec((group, NPNO, NPNO), lambda i, q, s, f: (i, 0, 0)),
        scratch_shapes=[
            pltpu.VMEM((2, 2 * group, NPNO, NPNO), jnp.float32),
            pltpu.SemaphoreType.DMA((2, 2 * group)),
        ],
    )
    flops = count * 2 * 4 * 2 * NPNO * NPNO * NPNO
    kernel = functools.partial(
        coupling_kernel, final=final, width=sources[0].shape[0], group=group, start=start, nsrc=len(sources)
    )
    return pl.pallas_call(
        kernel,
        grid_spec=grid_spec,
        out_shape=jax.ShapeDtypeStruct((count, NPNO, NPNO), jnp.float32),
        cost_estimate=pl.CostEstimate(
            flops=flops,
            bytes_accessed=count * NPNO * NPNO * (2 * 4 + 2 * 2 + 3 * 4),
            transcendentals=0,
        ),
    )(nb, sizes, fock, *sources, margin, exchange, column, row, own)


def chunked_halo(chunks):
    received = [halo_sources(chunk, "pair") for chunk in chunks]
    return [r[k] for k in range(3) for r in received]


def per_device(
    three_index,
    pno_coef,
    pair_orbitals,
    natural_orbital_class,
    pno_energy,
    margin,
    neighbour_pairs,
    fock_coupling,
):
    occ_dev = three_index.shape[0]
    pair_dev = pno_coef.shape[0]
    position = lax.axis_index("pair")
    sizes = class_size(natural_orbital_class)
    blocks = halo_sources(three_index, "pair")
    local_orbitals = (pair_orbitals - (position - 1) * occ_dev).astype(jnp.int32)
    half = pair_dev // 2
    presplit = halving_ready(half) and half % 8 == 0
    halves = [
        partial_exchange(
            local_orbitals[:, 0] - occ_dev,
            local_orbitals[:, 1],
            sizes,
            blocks,
            jnp.swapaxes(pno_coef, 2, 3),
            c * half,
            half,
            send_first(c) if presplit else None,
        )
        for c in range(2)
    ]
    exchange_ints = sum_over_aux(halves, presplit)
    denominator = pno_energy[:, :, None] + pno_energy[:, None, :]
    local_rows = (neighbour_pairs - (position - 1) * pair_dev).astype(jnp.int32).reshape(-1)
    fock = fock_coupling.reshape(-1)

    chunk = pair_dev // 2 if pair_dev % 8 == 0 else pair_dev
    parts = [-(exchange_ints / denominator)]
    sources = chunked_halo(parts)
    amplitudes = jnp.concatenate(parts, axis=0)
    for iteration in range(1, ITERS):
        parts = [
            coupling_step(
                local_rows, sizes, fock, sources, margin, exchange_ints, pno_energy, amplitudes,
                False, c * chunk, chunk,
            )
            for c in range(pair_dev // chunk)
        ]
        sources = chunked_halo(parts)
        amplitudes = jnp.concatenate(parts, axis=0)
    residual = coupling_step(
        local_rows, sizes, fock, sources, margin, exchange_ints, pno_energy, amplitudes, True
    )
    return (amplitudes, residual)


def solution(mesh):
    return jax.shard_map(
        per_device,
        mesh=mesh,
        in_specs=(
            P("pair", "aux", None),
            P("pair", None, None, None),
            P("pair", None),
            P("pair"),
            P("pair", None),
            P("pair", None, None, None),
            P("pair", None),
            P("pair", None),
        ),
        out_specs=(P("pair", None, None), P("pair", None, None)),
        check_vma=False,
    )
```

```python
import functools

import jax
import jax.numpy as jnp
from jax import lax
from jax.experimental import pallas as pl
from jax.experimental.pallas import tpu as pltpu
from jax.sharding import PartitionSpec as P

NPNO = 192
ITERS = 2
CLASS_SIZES = (NPNO // 6, NPNO // 3, 2 * NPNO // 3, NPNO)


def halo_sources(cells, axis):
    count = lax.axis_size(axis)
    ends = count - 1
    from_left = lax.ppermute(cells, axis, [(i, i + 1) for i in range(ends)])
    from_right = lax.ppermute(cells, axis, [(i + 1, i) for i in range(ends)])
    return (from_left, cells, from_right)


def swap_over_aux(value, bit_even, bit_odd):
    pairs = lax.axis_size("pair")
    count = lax.axis_size("aux")
    perm = []
    for p in range(pairs):
        bit = bit_even if p % 2 == 0 else bit_odd
        perm += [(a * pairs + p, (a ^ bit) * pairs + p) for a in range(count)]
    return lax.ppermute(value, ("aux", "pair"), perm)


def halving_stream(piece, index, parity, bits, presplit=False):
    steps = [(b, o) for b, o in zip(bits, reversed(bits))]
    for step, (bit_even, bit_odd) in enumerate(steps):
        bit = jnp.where(parity == 0, bit_even, bit_odd)
        side = (index // bit) % 2
        half = piece.shape[0] // 2
        if presplit and step == 0:
            keep, send = piece[half:], piece[:half]
        else:
            keep = lax.dynamic_slice_in_dim(piece, side * half, half, axis=0)
            send = lax.dynamic_slice_in_dim(piece, (1 - side) * half, half, axis=0)
        piece = keep + swap_over_aux(send, bit_even, bit_odd)
    for bit_even, bit_odd in reversed(steps):
        bit = jnp.where(parity == 0, bit_even, bit_odd)
        side = (index // bit) % 2
        other = swap_over_aux(piece, bit_even, bit_odd)
        length = piece.shape[0]
        full = jnp.zeros((2 * length,) + piece.shape[1:], piece.dtype)
        full = lax.dynamic_update_slice_in_dim(full, piece, side * length, axis=0)
        piece = lax.dynamic_update_slice_in_dim(full, other, (1 - side) * length, axis=0)
    return piece


def halving_ready(halves):
    return lax.axis_size("aux") == 4 and halves % 8 == 0


STREAM_ORDERS = ((1, 2), (2, 1))


def send_first(half_index):
    index = lax.axis_index("aux")
    even, odd = STREAM_ORDERS[half_index][0], STREAM_ORDERS[half_index][1]
    bit = jnp.where(lax.axis_index("pair") % 2 == 0, even, odd)
    return (1 - (index // bit) % 2).astype(jnp.int32).reshape(1)


def sum_over_aux(halves, presplit):
    if not halving_ready(halves[0].shape[0]):
        return lax.psum(jnp.concatenate(halves, axis=0), "aux")
    index = lax.axis_index("aux")
    parity = lax.axis_index("pair") % 2
    first = halving_stream(halves[0], index, parity, STREAM_ORDERS[0], presplit)
    second = halving_stream(halves[1], index, parity, STREAM_ORDERS[1], presplit)
    return jnp.concatenate([first, second], axis=0)


def class_size(natural_orbital_class):
    return jnp.where(
        natural_orbital_class == 0,
        NPNO // 6,
        jnp.where(
            natural_orbital_class == 1,
            NPNO // 3,
            jnp.where(natural_orbital_class == 2, 2 * NPNO // 3, NPNO),
        ),
    ).astype(jnp.int32)


def fetch_block(sources, width, local, dst, sem):
    index = jnp.clip(local // width, 0, len(sources) - 1)
    row = local % width
    for k, src in enumerate(sources):

        @pl.when(index == k)
        def _():
            pltpu.make_async_copy(src.at[row], dst, sem).start()


def exchange_kernel(
    lead_ref, trail_ref, size_ref, flip_ref, t_left, t_own, t_right, coef_ref, out_ref, lbuf, tbuf, sems, *, occ, group, start
):
    i = pl.program_id(0)
    steps = pl.num_programs(0)
    sources = (t_left, t_own, t_right)

    def fetch(step, slot):
        for g in range(group):
            p = start + step * group + g
            pltpu.make_async_copy(t_own.at[lead_ref[p] % occ], lbuf.at[slot, g], sems.at[slot, 0, g]).start()
            fetch_block(sources, occ, trail_ref[p], tbuf.at[slot, g], sems.at[slot, 1, g])

    @pl.when(i == 0)
    def _():
        fetch(0, 0)

    @pl.when(i + 1 < steps)
    def _():
        fetch(i + 1, (i + 1) % 2)

    slot = i % 2
    transposed = (((1,), (1,)), ((), ()))
    for g in range(group):
        p = start + i * group + g
        pltpu.make_async_copy(t_own.at[0], lbuf.at[slot, g], sems.at[slot, 0, g]).wait()
        pltpu.make_async_copy(t_own.at[0], tbuf.at[slot, g], sems.at[slot, 1, g]).wait()
        size = size_ref[p]
        out_ref[g] = jnp.zeros((NPNO, NPNO), jnp.float32)
        for m in CLASS_SIZES:

            @pl.when(size == m)
            def _():
                first = coef_ref[g, 0, :m, :]
                second = coef_ref[g, 1, :m, :]
                left_t = lax.dot_general(first, lbuf[slot, g], transposed, preferred_element_type=jnp.float32)
                right = lax.dot_general(tbuf[slot, g], second, transposed, preferred_element_type=jnp.float32)
                out_ref[g, :m, :m] = jnp.dot(
                    left_t.astype(jnp.bfloat16), right.astype(jnp.bfloat16), preferred_element_type=jnp.float32
                )


def partial_exchange(lead, trail, sizes, sources, coef_t, start=0, count=None, flip=None):
    pairs = coef_t.shape[0]
    count = pairs if count is None else count
    group = next(g for g in (4, 2, 1) if count % g == 0 and start % g == 0)
    base = start // group
    steps = count // group
    if flip is None or steps != 2:
        flip = jnp.zeros((1,), jnp.int32)
    occ, nfit, npao = sources[1].shape
    hbm = pl.BlockSpec(memory_space=pl.ANY)
    grid_spec = pltpu.PrefetchScalarGridSpec(
        num_scalar_prefetch=4,
        grid=(steps,),
        in_specs=[
            hbm,
            hbm,
            hbm,
            pl.BlockSpec((group, 2, NPNO, npao), lambda i, a, b, s, f: (i + base, 0, 0, 0)),
        ],
        out_specs=pl.BlockSpec((group, NPNO, NPNO), lambda i, a, b, s, f: ((i + f[0]) % steps, 0, 0)),
        scratch_shapes=[
            pltpu.VMEM((2, group, nfit, npao), sources[1].dtype),
            pltpu.VMEM((2, group, nfit, npao), sources[1].dtype),
            pltpu.SemaphoreType.DMA((2, 2, group)),
        ],
    )
    flops = count * (2 * 2 * nfit * npao * NPNO + 2 * nfit * NPNO * NPNO)
    return pl.pallas_call(
        functools.partial(exchange_kernel, occ=occ, group=group, start=start),
        grid_spec=grid_spec,
        out_shape=jax.ShapeDtypeStruct((count, NPNO, NPNO), jnp.float32),
        cost_estimate=pl.CostEstimate(
            flops=flops,
            bytes_accessed=count * (2 * nfit * npao * 2 + 2 * npao * NPNO * 2 + NPNO * NPNO * 4),
            transcendentals=0,
        ),
    )(lead, trail, sizes, flip, *sources, coef_t)


def split_bf16(value):
    hi = value.astype(jnp.bfloat16)
    lo = (value - hi.astype(jnp.float32)).astype(jnp.bfloat16)
    return hi, lo


def mm(lhs, rhs, dims=(((1,), (0,)), ((), ()))):
    return lax.dot_general(lhs, rhs, dims, preferred_element_type=jnp.float32)


def coupling_kernel(nb_ref, size_ref, fock_ref, *refs, final, width, group, start, nsrc):
    sources = refs[:nsrc]
    margin_ref, ex_ref, col_ref, row_ref, own_ref, out_ref, tbuf, sems = refs[nsrc:]
    i = pl.program_id(0)
    steps = pl.num_programs(0)

    def fetch(step, slot):
        for k in range(2 * group):
            fetch_block(sources, width, nb_ref[2 * (start + group * step) + k], tbuf.at[slot, k], sems.at[slot, k])

    @pl.when(i == 0)
    def _():
        fetch(0, 0)

    @pl.when(i + 1 < steps)
    def _():
        fetch(i + 1, (i + 1) % 2)

    slot = i % 2
    transposed = (((1,), (1,)), ((), ()))
    for g in range(group):
        p = start + i * group + g
        splits = []
        for n in range(2):
            k = 2 * g + n
            pltpu.make_async_copy(sources[0].at[0], tbuf.at[slot, k], sems.at[slot, k]).wait()
            splits.append(split_bf16(tbuf[slot, k]))
        size = size_ref[p]
        out_ref[g] = jnp.zeros((NPNO, NPNO), jnp.float32)
        for m in CLASS_SIZES:

            @pl.when(size == m)
            def _():
                total = None
                for n in range(2):
                    side = margin_ref[g, n, :m, :]
                    t_hi, t_lo = splits[n]
                    inner = mm(side, t_hi) + mm(side, t_lo)
                    w_hi, w_lo = split_bf16(fock_ref[2 * p + n] * inner)
                    outer = mm(w_hi, side, transposed) + mm(w_lo, side, transposed)
                    total = outer if total is None else total + outer
                denominator = col_ref[g, :m, :] + row_ref[g, :, :m]
                amplitudes = own_ref[g, :m, :m]
                residual = ex_ref[g, :m, :m] + denominator * amplitudes - total
                if final:
                    out_ref[g, :m, :m] = residual
                else:
                    out_ref[g, :m, :m] = amplitudes - residual / denominator


def coupling_step(nb, sizes, fock, sources, margin, exchange, energy, own, final, start=0, count=None):
    pairs = own.shape[0]
    count = pairs if count is None else count
    group = next(g for g in (4, 2, 1) if count % g == 0 and start % g == 0)
    base = start // group
    column = energy.reshape(pairs, NPNO, 1)
    row = energy.reshape(pairs, 1, NPNO)
    hbm = pl.BlockSpec(memory_space=pl.ANY)
    own_spec = pl.BlockSpec((group, NPNO, NPNO), lambda i, q, s, f: (i + base, 0, 0))
    grid_spec = pltpu.PrefetchScalarGridSpec(
        num_scalar_prefetch=3,
        grid=(count // group,),
        in_specs=[hbm] * len(sources)
        + [
            pl.BlockSpec((group, 2, NPNO, NPNO), lambda i, q, s, f: (i + base, 0, 0, 0)),
            own_spec,
            pl.BlockSpec((group, NPNO, 1), lambda i, q, s, f: (i + base, 0, 0)),
            pl.BlockSpec((group, 1, NPNO), lambda i, q, s, f: (i + base, 0, 0)),
            own_spec,
        ],
        out_specs=pl.BlockSpec((group, NPNO, NPNO), lambda i, q, s, f: (i, 0, 0)),
        scratch_shapes=[
            pltpu.VMEM((2, 2 * group, NPNO, NPNO), jnp.float32),
            pltpu.SemaphoreType.DMA((2, 2 * group)),
        ],
    )
    flops = count * 2 * 4 * 2 * NPNO * NPNO * NPNO
    kernel = functools.partial(
        coupling_kernel, final=final, width=sources[0].shape[0], group=group, start=start, nsrc=len(sources)
    )
    return pl.pallas_call(
        kernel,
        grid_spec=grid_spec,
        out_shape=jax.ShapeDtypeStruct((count, NPNO, NPNO), jnp.float32),
        cost_estimate=pl.CostEstimate(
            flops=flops,
            bytes_accessed=count * NPNO * NPNO * (2 * 4 + 2 * 2 + 3 * 4),
            transcendentals=0,
        ),
    )(nb, sizes, fock, *sources, margin, exchange, column, row, own)


def chunked_halo(chunks):
    received = [halo_sources(chunk, "pair") for chunk in chunks]
    return [r[k] for k in range(3) for r in received]


def per_device(
    three_index,
    pno_coef,
    pair_orbitals,
    natural_orbital_class,
    pno_energy,
    margin,
    neighbour_pairs,
    fock_coupling,
):
    occ_dev = three_index.shape[0]
    pair_dev = pno_coef.shape[0]
    position = lax.axis_index("pair")
    sizes = class_size(natural_orbital_class)
    blocks = halo_sources(three_index, "pair")
    local_orbitals = (pair_orbitals - (position - 1) * occ_dev).astype(jnp.int32)
    half = pair_dev // 2
    presplit = halving_ready(half) and half % 8 == 0
    halves = [
        partial_exchange(
            local_orbitals[:, 0] - occ_dev,
            local_orbitals[:, 1],
            sizes,
            blocks,
            jnp.swapaxes(pno_coef, 2, 3),
            c * half,
            half,
            send_first(c) if presplit else None,
        )
        for c in range(2)
    ]
    exchange_ints = sum_over_aux(halves, presplit)
    denominator = pno_energy[:, :, None] + pno_energy[:, None, :]
    local_rows = (neighbour_pairs - (position - 1) * pair_dev).astype(jnp.int32).reshape(-1)
    fock = fock_coupling.reshape(-1)

    chunk = pair_dev // 2 if pair_dev % 8 == 0 else pair_dev
    parts = [-(exchange_ints / denominator)]
    sources = chunked_halo(parts)
    amplitudes = jnp.concatenate(parts, axis=0)
    for iteration in range(1, ITERS):
        parts = [
            coupling_step(
                local_rows, sizes, fock, sources, margin, exchange_ints, pno_energy, amplitudes,
                False, c * chunk, chunk,
            )
            for c in range(pair_dev // chunk)
        ]
        sources = chunked_halo(parts)
        amplitudes = jnp.concatenate(parts, axis=0)
    residual = coupling_step(
        local_rows, sizes, fock, sources, margin, exchange_ints, pno_energy, amplitudes, True
    )
    return (amplitudes, residual)


def solution(mesh):
    return jax.shard_map(
        per_device,
        mesh=mesh,
        in_specs=(
            P("pair", "aux", None),
            P("pair", None, None, None),
            P("pair", None),
            P("pair"),
            P("pair", None),
            P("pair", None, None, None),
            P("pair", None),
            P("pair", None),
        ),
        out_specs=(P("pair", None, None), P("pair", None, None)),
        check_vma=False,
    )
```

```python
import functools

import jax
import jax.numpy as jnp
from jax import lax
from jax.experimental import pallas as pl
from jax.experimental.pallas import tpu as pltpu
from jax.sharding import PartitionSpec as P

NPNO = 192
ITERS = 2
CLASS_SIZES = (NPNO // 6, NPNO // 3, 2 * NPNO // 3, NPNO)


def halo_sources(cells, axis):
    count = lax.axis_size(axis)
    ends = count - 1
    from_left = lax.ppermute(cells, axis, [(i, i + 1) for i in range(ends)])
    from_right = lax.ppermute(cells, axis, [(i + 1, i) for i in range(ends)])
    return (from_left, cells, from_right)


def swap_over_aux(value, bit_even, bit_odd):
    pairs = lax.axis_size("pair")
    count = lax.axis_size("aux")
    perm = []
    for p in range(pairs):
        bit = bit_even if p % 2 == 0 else bit_odd
        perm += [(a * pairs + p, (a ^ bit) * pairs + p) for a in range(count)]
    return lax.ppermute(value, ("aux", "pair"), perm)


def halving_stream(piece, index, parity, bits, presplit=False):
    steps = [(b, o) for b, o in zip(bits, reversed(bits))]
    for step, (bit_even, bit_odd) in enumerate(steps):
        bit = jnp.where(parity == 0, bit_even, bit_odd)
        side = (index // bit) % 2
        half = piece[0].shape[0] if presplit and step == 0 else piece.shape[0] // 2
        if presplit and step == 0:
            send, keep = piece
        else:
            keep = lax.dynamic_slice_in_dim(piece, side * half, half, axis=0)
            send = lax.dynamic_slice_in_dim(piece, (1 - side) * half, half, axis=0)
        piece = keep + swap_over_aux(send, bit_even, bit_odd)
    for bit_even, bit_odd in reversed(steps):
        bit = jnp.where(parity == 0, bit_even, bit_odd)
        side = (index // bit) % 2
        other = swap_over_aux(piece, bit_even, bit_odd)
        length = piece.shape[0]
        full = jnp.zeros((2 * length,) + piece.shape[1:], piece.dtype)
        full = lax.dynamic_update_slice_in_dim(full, piece, side * length, axis=0)
        piece = lax.dynamic_update_slice_in_dim(full, other, (1 - side) * length, axis=0)
    return piece


def halving_ready(halves):
    return lax.axis_size("aux") == 4 and halves % 8 == 0


STREAM_ORDERS = ((1, 2), (2, 1))


def send_first(half_index):
    index = lax.axis_index("aux")
    even, odd = STREAM_ORDERS[half_index][0], STREAM_ORDERS[half_index][1]
    bit = jnp.where(lax.axis_index("pair") % 2 == 0, even, odd)
    return (1 - (index // bit) % 2).astype(jnp.int32).reshape(1)


def sum_over_aux(halves, presplit):
    if not presplit:
        if not halving_ready(halves[0].shape[0]):
            return lax.psum(jnp.concatenate(halves, axis=0), "aux")
    index = lax.axis_index("aux")
    parity = lax.axis_index("pair") % 2
    first = halving_stream(halves[0], index, parity, STREAM_ORDERS[0], presplit)
    second = halving_stream(halves[1], index, parity, STREAM_ORDERS[1], presplit)
    return jnp.concatenate([first, second], axis=0)


def class_size(natural_orbital_class):
    return jnp.where(
        natural_orbital_class == 0,
        NPNO // 6,
        jnp.where(
            natural_orbital_class == 1,
            NPNO // 3,
            jnp.where(natural_orbital_class == 2, 2 * NPNO // 3, NPNO),
        ),
    ).astype(jnp.int32)


def fetch_block(sources, width, local, dst, sem):
    index = jnp.clip(local // width, 0, len(sources) - 1)
    row = local % width
    for k, src in enumerate(sources):

        @pl.when(index == k)
        def _():
            pltpu.make_async_copy(src.at[row], dst, sem).start()


def exchange_kernel(lead_ref, trail_ref, size_ref, flip_ref, *refs, occ, group, start, split):
    if split:
        t_left, t_own, t_right, coef_ref, send_ref, keep_ref, lbuf, tbuf, sems, res_ref = refs
    else:
        t_left, t_own, t_right, coef_ref, res_ref, lbuf, tbuf, sems = refs
    out_ref = res_ref
    i = pl.program_id(0)
    steps = pl.num_programs(0)
    sources = (t_left, t_own, t_right)

    def fetch(step, slot):
        for g in range(group):
            p = start + step * group + g
            pltpu.make_async_copy(t_own.at[lead_ref[p] % occ], lbuf.at[slot, g], sems.at[slot, 0, g]).start()
            fetch_block(sources, occ, trail_ref[p], tbuf.at[slot, g], sems.at[slot, 1, g])

    @pl.when(i == 0)
    def _():
        fetch(0, 0)

    @pl.when(i + 1 < steps)
    def _():
        fetch(i + 1, (i + 1) % 2)

    slot = i % 2
    transposed = (((1,), (1,)), ((), ()))
    for g in range(group):
        p = start + i * group + g
        pltpu.make_async_copy(t_own.at[0], lbuf.at[slot, g], sems.at[slot, 0, g]).wait()
        pltpu.make_async_copy(t_own.at[0], tbuf.at[slot, g], sems.at[slot, 1, g]).wait()
        size = size_ref[p]
        out_ref[g] = jnp.zeros((NPNO, NPNO), jnp.float32)
        for m in CLASS_SIZES:

            @pl.when(size == m)
            def _():
                first = coef_ref[g, 0, :m, :]
                second = coef_ref[g, 1, :m, :]
                left_t = lax.dot_general(first, lbuf[slot, g], transposed, preferred_element_type=jnp.float32)
                right = lax.dot_general(tbuf[slot, g], second, transposed, preferred_element_type=jnp.float32)
                out_ref[g, :m, :m] = jnp.dot(
                    left_t.astype(jnp.bfloat16), right.astype(jnp.bfloat16), preferred_element_type=jnp.float32
                )

    if split:
        @pl.when((i + flip_ref[0]) % 2 == 0)
        def _():
            send_ref[...] = res_ref[...]

        @pl.when((i + flip_ref[0]) % 2 == 1)
        def _():
            keep_ref[...] = res_ref[...]


def partial_exchange(lead, trail, sizes, sources, coef_t, start=0, count=None, flip=None):
    pairs = coef_t.shape[0]
    count = pairs if count is None else count
    group = next(g for g in (4, 2, 1) if count % g == 0 and start % g == 0)
    base = start // group
    steps = count // group
    split = flip is not None and steps == 2
    if not split:
        flip = jnp.zeros((1,), jnp.int32)
    occ, nfit, npao = sources[1].shape
    hbm = pl.BlockSpec(memory_space=pl.ANY)
    scratch = [
        pltpu.VMEM((2, group, nfit, npao), sources[1].dtype),
        pltpu.VMEM((2, group, nfit, npao), sources[1].dtype),
        pltpu.SemaphoreType.DMA((2, 2, group)),
    ]
    block = (group, NPNO, NPNO)
    if split:
        fixed = pl.BlockSpec(block, lambda i, a, b, s, f: (0, 0, 0))
        out_specs = [fixed, fixed]
        out_shape = [jax.ShapeDtypeStruct(block, jnp.float32)] * 2
        scratch.append(pltpu.VMEM(block, jnp.float32))
    else:
        out_specs = pl.BlockSpec(block, lambda i, a, b, s, f: (i, 0, 0))
        out_shape = jax.ShapeDtypeStruct((count, NPNO, NPNO), jnp.float32)
    grid_spec = pltpu.PrefetchScalarGridSpec(
        num_scalar_prefetch=4,
        grid=(steps,),
        in_specs=[
            hbm,
            hbm,
            hbm,
            pl.BlockSpec((group, 2, NPNO, npao), lambda i, a, b, s, f: (i + base, 0, 0, 0)),
        ],
        out_specs=out_specs,
        scratch_shapes=scratch,
    )
    flops = count * (2 * 2 * nfit * npao * NPNO + 2 * nfit * NPNO * NPNO)
    return pl.pallas_call(
        functools.partial(exchange_kernel, occ=occ, group=group, start=start, split=split),
        grid_spec=grid_spec,
        out_shape=out_shape,
        cost_estimate=pl.CostEstimate(
            flops=flops,
            bytes_accessed=count * (2 * nfit * npao * 2 + 2 * npao * NPNO * 2 + NPNO * NPNO * 4),
            transcendentals=0,
        ),
    )(lead, trail, sizes, flip, *sources, coef_t)


def split_bf16(value):
    hi = value.astype(jnp.bfloat16)
    lo = (value - hi.astype(jnp.float32)).astype(jnp.bfloat16)
    return hi, lo


def mm(lhs, rhs, dims=(((1,), (0,)), ((), ()))):
    return lax.dot_general(lhs, rhs, dims, preferred_element_type=jnp.float32)


def coupling_kernel(nb_ref, size_ref, fock_ref, *refs, final, width, group, start, nsrc):
    sources = refs[:nsrc]
    margin_ref, ex_ref, col_ref, row_ref, own_ref, out_ref, tbuf, sems = refs[nsrc:]
    i = pl.program_id(0)
    steps = pl.num_programs(0)

    def fetch(step, slot):
        for k in range(2 * group):
            fetch_block(sources, width, nb_ref[2 * (start + group * step) + k], tbuf.at[slot, k], sems.at[slot, k])

    @pl.when(i == 0)
    def _():
        fetch(0, 0)

    @pl.when(i + 1 < steps)
    def _():
        fetch(i + 1, (i + 1) % 2)

    slot = i % 2
    transposed = (((1,), (1,)), ((), ()))
    for g in range(group):
        p = start + i * group + g
        splits = []
        for n in range(2):
            k = 2 * g + n
            pltpu.make_async_copy(sources[0].at[0], tbuf.at[slot, k], sems.at[slot, k]).wait()
            splits.append(split_bf16(tbuf[slot, k]))
        size = size_ref[p]
        out_ref[g] = jnp.zeros((NPNO, NPNO), jnp.float32)
        for m in CLASS_SIZES:

            @pl.when(size == m)
            def _():
                total = None
                for n in range(2):
                    side = margin_ref[g, n, :m, :]
                    t_hi, t_lo = splits[n]
                    inner = mm(side, t_hi) + mm(side, t_lo)
                    w_hi, w_lo = split_bf16(fock_ref[2 * p + n] * inner)
                    outer = mm(w_hi, side, transposed) + mm(w_lo, side, transposed)
                    total = outer if total is None else total + outer
                denominator = col_ref[g, :m, :] + row_ref[g, :, :m]
                amplitudes = own_ref[g, :m, :m]
                residual = ex_ref[g, :m, :m] + denominator * amplitudes - total
                if final:
                    out_ref[g, :m, :m] = residual
                else:
                    out_ref[g, :m, :m] = amplitudes - residual / denominator


def coupling_step(nb, sizes, fock, sources, margin, exchange, energy, own, final, start=0, count=None):
    pairs = own.shape[0]
    count = pairs if count is None else count
    group = next(g for g in (4, 2, 1) if count % g == 0 and start % g == 0)
    base = start // group
    column = energy.reshape(pairs, NPNO, 1)
    row = energy.reshape(pairs, 1, NPNO)
    hbm = pl.BlockSpec(memory_space=pl.ANY)
    own_spec = pl.BlockSpec((group, NPNO, NPNO), lambda i, q, s, f: (i + base, 0, 0))
    grid_spec = pltpu.PrefetchScalarGridSpec(
        num_scalar_prefetch=3,
        grid=(count // group,),
        in_specs=[hbm] * len(sources)
        + [
            pl.BlockSpec((group, 2, NPNO, NPNO), lambda i, q, s, f: (i + base, 0, 0, 0)),
            own_spec,
            pl.BlockSpec((group, NPNO, 1), lambda i, q, s, f: (i + base, 0, 0)),
            pl.BlockSpec((group, 1, NPNO), lambda i, q, s, f: (i + base, 0, 0)),
            own_spec,
        ],
        out_specs=pl.BlockSpec((group, NPNO, NPNO), lambda i, q, s, f: (i, 0, 0)),
        scratch_shapes=[
            pltpu.VMEM((2, 2 * group, NPNO, NPNO), jnp.float32),
            pltpu.SemaphoreType.DMA((2, 2 * group)),
        ],
    )
    flops = count * 2 * 4 * 2 * NPNO * NPNO * NPNO
    kernel = functools.partial(
        coupling_kernel, final=final, width=sources[0].shape[0], group=group, start=start, nsrc=len(sources)
    )
    return pl.pallas_call(
        kernel,
        grid_spec=grid_spec,
        out_shape=jax.ShapeDtypeStruct((count, NPNO, NPNO), jnp.float32),
        cost_estimate=pl.CostEstimate(
            flops=flops,
            bytes_accessed=count * NPNO * NPNO * (2 * 4 + 2 * 2 + 3 * 4),
            transcendentals=0,
        ),
    )(nb, sizes, fock, *sources, margin, exchange, column, row, own)


def chunked_halo(chunks):
    received = [halo_sources(chunk, "pair") for chunk in chunks]
    return [r[k] for k in range(3) for r in received]


def per_device(
    three_index,
    pno_coef,
    pair_orbitals,
    natural_orbital_class,
    pno_energy,
    margin,
    neighbour_pairs,
    fock_coupling,
):
    occ_dev = three_index.shape[0]
    pair_dev = pno_coef.shape[0]
    position = lax.axis_index("pair")
    sizes = class_size(natural_orbital_class)
    blocks = halo_sources(three_index, "pair")
    local_orbitals = (pair_orbitals - (position - 1) * occ_dev).astype(jnp.int32)
    half = pair_dev // 2
    presplit = halving_ready(half) and half % 8 == 0
    halves = [
        partial_exchange(
            local_orbitals[:, 0] - occ_dev,
            local_orbitals[:, 1],
            sizes,
            blocks,
            jnp.swapaxes(pno_coef, 2, 3),
            c * half,
            half,
            send_first(c) if presplit else None,
        )
        for c in range(2)
    ]
    exchange_ints = sum_over_aux(halves, presplit)
    denominator = pno_energy[:, :, None] + pno_energy[:, None, :]
    local_rows = (neighbour_pairs - (position - 1) * pair_dev).astype(jnp.int32).reshape(-1)
    fock = fock_coupling.reshape(-1)

    chunk = pair_dev // 2 if pair_dev % 8 == 0 else pair_dev
    parts = [-(exchange_ints / denominator)]
    sources = chunked_halo(parts)
    amplitudes = jnp.concatenate(parts, axis=0)
    for iteration in range(1, ITERS):
        parts = [
            coupling_step(
                local_rows, sizes, fock, sources, margin, exchange_ints, pno_energy, amplitudes,
                False, c * chunk, chunk,
            )
            for c in range(pair_dev // chunk)
        ]
        sources = chunked_halo(parts)
        amplitudes = jnp.concatenate(parts, axis=0)
    residual = coupling_step(
        local_rows, sizes, fock, sources, margin, exchange_ints, pno_energy, amplitudes, True
    )
    return (amplitudes, residual)


def solution(mesh):
    return jax.shard_map(
        per_device,
        mesh=mesh,
        in_specs=(
            P("pair", "aux", None),
            P("pair", None, None, None),
            P("pair", None),
            P("pair"),
            P("pair", None),
            P("pair", None, None, None),
            P("pair", None),
            P("pair", None),
        ),
        out_specs=(P("pair", None, None), P("pair", None, None)),
        check_vma=False,
    )
```

```python
import functools

import jax
import jax.numpy as jnp
from jax import lax
from jax.experimental import pallas as pl
from jax.experimental.pallas import tpu as pltpu
from jax.sharding import PartitionSpec as P

NPNO = 192
ITERS = 2
CLASS_SIZES = (NPNO // 6, NPNO // 3, 2 * NPNO // 3, NPNO)


def halo_sources(cells, axis):
    count = lax.axis_size(axis)
    ends = count - 1
    from_left = lax.ppermute(cells, axis, [(i, i + 1) for i in range(ends)])
    from_right = lax.ppermute(cells, axis, [(i + 1, i) for i in range(ends)])
    return (from_left, cells, from_right)


def swap_over_aux(value, bit_even, bit_odd):
    pairs = lax.axis_size("pair")
    count = lax.axis_size("aux")
    perm = []
    for p in range(pairs):
        bit = bit_even if p % 2 == 0 else bit_odd
        perm += [(a * pairs + p, (a ^ bit) * pairs + p) for a in range(count)]
    return lax.ppermute(value, ("aux", "pair"), perm)


def halving_stream(piece, index, parity, bits, presplit=False):
    steps = [(b, o) for b, o in zip(bits, reversed(bits))]
    for step, (bit_even, bit_odd) in enumerate(steps):
        bit = jnp.where(parity == 0, bit_even, bit_odd)
        side = (index // bit) % 2
        half = piece[0].shape[0] if presplit and step == 0 else piece.shape[0] // 2
        if presplit and step == 0:
            send, keep = piece
        else:
            keep = lax.dynamic_slice_in_dim(piece, side * half, half, axis=0)
            send = lax.dynamic_slice_in_dim(piece, (1 - side) * half, half, axis=0)
        piece = keep + swap_over_aux(send, bit_even, bit_odd)
    for bit_even, bit_odd in reversed(steps):
        bit = jnp.where(parity == 0, bit_even, bit_odd)
        side = (index // bit) % 2
        other = swap_over_aux(piece, bit_even, bit_odd)
        length = piece.shape[0]
        full = jnp.zeros((2 * length,) + piece.shape[1:], piece.dtype)
        full = lax.dynamic_update_slice_in_dim(full, piece, side * length, axis=0)
        piece = lax.dynamic_update_slice_in_dim(full, other, (1 - side) * length, axis=0)
    return piece


def halving_ready(halves):
    return lax.axis_size("aux") == 4 and halves % 8 == 0


STREAM_ORDERS = ((1, 2), (2, 1))


def send_first(half_index):
    index = lax.axis_index("aux")
    even, odd = STREAM_ORDERS[half_index][0], STREAM_ORDERS[half_index][1]
    bit = jnp.where(lax.axis_index("pair") % 2 == 0, even, odd)
    return (1 - (index // bit) % 2).astype(jnp.int32).reshape(1)


def sum_over_aux(halves, presplit):
    if not presplit:
        if not halving_ready(halves[0].shape[0]):
            return lax.psum(jnp.concatenate(halves, axis=0), "aux")
    index = lax.axis_index("aux")
    parity = lax.axis_index("pair") % 2
    first = halving_stream(halves[0], index, parity, STREAM_ORDERS[0], presplit)
    second = halving_stream(halves[1], index, parity, STREAM_ORDERS[1], presplit)
    return jnp.concatenate([first, second], axis=0)


def class_size(natural_orbital_class):
    return jnp.where(
        natural_orbital_class == 0,
        NPNO // 6,
        jnp.where(
            natural_orbital_class == 1,
            NPNO // 3,
            jnp.where(natural_orbital_class == 2, 2 * NPNO // 3, NPNO),
        ),
    ).astype(jnp.int32)


def fetch_block(sources, width, local, dst, sem):
    index = jnp.clip(local // width, 0, len(sources) - 1)
    row = local % width
    for k, src in enumerate(sources):

        @pl.when(index == k)
        def _():
            pltpu.make_async_copy(src.at[row], dst, sem).start()


def left_kernel(lead_ref, size_ref, t_own, coef_ref, out_ref, lbuf, sems, *, occ, group):
    i = pl.program_id(0)
    steps = pl.num_programs(0)

    def fetch(step, slot):
        for g in range(group):
            p = step * group + g
            pltpu.make_async_copy(t_own.at[lead_ref[p] % occ], lbuf.at[slot, g], sems.at[slot, g]).start()

    @pl.when(i == 0)
    def _():
        fetch(0, 0)

    @pl.when(i + 1 < steps)
    def _():
        fetch(i + 1, (i + 1) % 2)

    slot = i % 2
    transposed = (((1,), (1,)), ((), ()))
    for g in range(group):
        p = i * group + g
        pltpu.make_async_copy(t_own.at[0], lbuf.at[slot, g], sems.at[slot, g]).wait()
        size = size_ref[p]
        out_ref[g] = jnp.zeros(out_ref.shape[1:], out_ref.dtype)
        for m in CLASS_SIZES:

            @pl.when(size == m)
            def _():
                first = coef_ref[g, 0, :m, :]
                left_t = lax.dot_general(first, lbuf[slot, g], transposed, preferred_element_type=jnp.float32)
                out_ref[g, :m, :] = left_t.astype(jnp.bfloat16)


def left_halves(lead, sizes, t_own, coef_t):
    pairs = coef_t.shape[0]
    group = next(g for g in (4, 2, 1) if pairs % g == 0)
    occ, nfit, npao = t_own.shape
    grid_spec = pltpu.PrefetchScalarGridSpec(
        num_scalar_prefetch=2,
        grid=(pairs // group,),
        in_specs=[
            pl.BlockSpec(memory_space=pl.ANY),
            pl.BlockSpec((group, 2, NPNO, npao), lambda i, a, s: (i, 0, 0, 0)),
        ],
        out_specs=pl.BlockSpec((group, NPNO, nfit), lambda i, a, s: (i, 0, 0)),
        scratch_shapes=[
            pltpu.VMEM((2, group, nfit, npao), t_own.dtype),
            pltpu.SemaphoreType.DMA((2, group)),
        ],
    )
    return pl.pallas_call(
        functools.partial(left_kernel, occ=occ, group=group),
        grid_spec=grid_spec,
        out_shape=jax.ShapeDtypeStruct((pairs, NPNO, nfit), jnp.bfloat16),
        cost_estimate=pl.CostEstimate(
            flops=pairs * 2 * nfit * npao * NPNO,
            bytes_accessed=pairs * (nfit * npao * 2 + 2 * npao * NPNO * 2 + NPNO * nfit * 2),
            transcendentals=0,
        ),
    )(lead, sizes, t_own, coef_t)


def exchange_kernel(lead_ref, trail_ref, size_ref, flip_ref, *refs, occ, group, start, split):
    if split:
        t_left, t_own, t_right, left_ref, coef_ref, send_ref, keep_ref, tbuf, sems, res_ref = refs
    else:
        t_left, t_own, t_right, left_ref, coef_ref, res_ref, tbuf, sems = refs
    out_ref = res_ref
    i = pl.program_id(0)
    steps = pl.num_programs(0)
    sources = (t_left, t_own, t_right)

    def fetch(step, slot):
        for g in range(group):
            p = start + step * group + g
            fetch_block(sources, occ, trail_ref[p], tbuf.at[slot, g], sems.at[slot, g])

    @pl.when(i == 0)
    def _():
        fetch(0, 0)

    @pl.when(i + 1 < steps)
    def _():
        fetch(i + 1, (i + 1) % 2)

    slot = i % 2
    transposed = (((1,), (1,)), ((), ()))
    for g in range(group):
        p = start + i * group + g
        pltpu.make_async_copy(t_own.at[0], tbuf.at[slot, g], sems.at[slot, g]).wait()
        size = size_ref[p]
        out_ref[g] = jnp.zeros((NPNO, NPNO), jnp.float32)
        for m in CLASS_SIZES:

            @pl.when(size == m)
            def _():
                second = coef_ref[g, 1, :m, :]
                right = lax.dot_general(tbuf[slot, g], second, transposed, preferred_element_type=jnp.float32)
                out_ref[g, :m, :m] = jnp.dot(
                    left_ref[g, :m, :], right.astype(jnp.bfloat16), preferred_element_type=jnp.float32
                )

    if split:
        @pl.when((i + flip_ref[0]) % 2 == 0)
        def _():
            send_ref[...] = res_ref[...]

        @pl.when((i + flip_ref[0]) % 2 == 1)
        def _():
            keep_ref[...] = res_ref[...]


def partial_exchange(lead, trail, sizes, sources, left_t, coef_t, start=0, count=None, flip=None):
    pairs = coef_t.shape[0]
    count = pairs if count is None else count
    group = next(g for g in (4, 2, 1) if count % g == 0 and start % g == 0)
    base = start // group
    steps = count // group
    split = flip is not None and steps == 2
    if not split:
        flip = jnp.zeros((1,), jnp.int32)
    occ, nfit, npao = sources[1].shape
    hbm = pl.BlockSpec(memory_space=pl.ANY)
    scratch = [
        pltpu.VMEM((2, group, nfit, npao), sources[1].dtype),
        pltpu.SemaphoreType.DMA((2, group)),
    ]
    block = (group, NPNO, NPNO)
    if split:
        fixed = pl.BlockSpec(block, lambda i, a, b, s, f: (0, 0, 0))
        out_specs = [fixed, fixed]
        out_shape = [jax.ShapeDtypeStruct(block, jnp.float32)] * 2
        scratch.append(pltpu.VMEM(block, jnp.float32))
    else:
        out_specs = pl.BlockSpec(block, lambda i, a, b, s, f: (i, 0, 0))
        out_shape = jax.ShapeDtypeStruct((count, NPNO, NPNO), jnp.float32)
    grid_spec = pltpu.PrefetchScalarGridSpec(
        num_scalar_prefetch=4,
        grid=(steps,),
        in_specs=[
            hbm,
            hbm,
            hbm,
            pl.BlockSpec((group, NPNO, nfit), lambda i, a, b, s, f: (i + base, 0, 0)),
            pl.BlockSpec((group, 2, NPNO, npao), lambda i, a, b, s, f: (i + base, 0, 0, 0)),
        ],
        out_specs=out_specs,
        scratch_shapes=scratch,
    )
    flops = count * (2 * 2 * nfit * npao * NPNO + 2 * nfit * NPNO * NPNO)
    return pl.pallas_call(
        functools.partial(exchange_kernel, occ=occ, group=group, start=start, split=split),
        grid_spec=grid_spec,
        out_shape=out_shape,
        cost_estimate=pl.CostEstimate(
            flops=flops,
            bytes_accessed=count * (2 * nfit * npao * 2 + 2 * npao * NPNO * 2 + NPNO * NPNO * 4),
            transcendentals=0,
        ),
    )(lead, trail, sizes, flip, *sources, left_t, coef_t)


def split_bf16(value):
    hi = value.astype(jnp.bfloat16)
    lo = (value - hi.astype(jnp.float32)).astype(jnp.bfloat16)
    return hi, lo


def mm(lhs, rhs, dims=(((1,), (0,)), ((), ()))):
    return lax.dot_general(lhs, rhs, dims, preferred_element_type=jnp.float32)


def coupling_kernel(nb_ref, size_ref, fock_ref, *refs, final, width, group, start, nsrc):
    sources = refs[:nsrc]
    margin_ref, ex_ref, col_ref, row_ref, own_ref, out_ref, tbuf, sems = refs[nsrc:]
    i = pl.program_id(0)
    steps = pl.num_programs(0)

    def fetch(step, slot):
        for k in range(2 * group):
            fetch_block(sources, width, nb_ref[2 * (start + group * step) + k], tbuf.at[slot, k], sems.at[slot, k])

    @pl.when(i == 0)
    def _():
        fetch(0, 0)

    @pl.when(i + 1 < steps)
    def _():
        fetch(i + 1, (i + 1) % 2)

    slot = i % 2
    transposed = (((1,), (1,)), ((), ()))
    for g in range(group):
        p = start + i * group + g
        splits = []
        for n in range(2):
            k = 2 * g + n
            pltpu.make_async_copy(sources[0].at[0], tbuf.at[slot, k], sems.at[slot, k]).wait()
            splits.append(split_bf16(tbuf[slot, k]))
        size = size_ref[p]
        out_ref[g] = jnp.zeros((NPNO, NPNO), jnp.float32)
        for m in CLASS_SIZES:

            @pl.when(size == m)
            def _():
                total = None
                for n in range(2):
                    side = margin_ref[g, n, :m, :]
                    t_hi, t_lo = splits[n]
                    inner = mm(side, t_hi) + mm(side, t_lo)
                    w_hi, w_lo = split_bf16(fock_ref[2 * p + n] * inner)
                    outer = mm(w_hi, side, transposed) + mm(w_lo, side, transposed)
                    total = outer if total is None else total + outer
                denominator = col_ref[g, :m, :] + row_ref[g, :, :m]
                amplitudes = own_ref[g, :m, :m]
                residual = ex_ref[g, :m, :m] + denominator * amplitudes - total
                if final:
                    out_ref[g, :m, :m] = residual
                else:
                    out_ref[g, :m, :m] = amplitudes - residual / denominator


def coupling_step(nb, sizes, fock, sources, margin, exchange, energy, own, final, start=0, count=None):
    pairs = own.shape[0]
    count = pairs if count is None else count
    group = next(g for g in (4, 2, 1) if count % g == 0 and start % g == 0)
    base = start // group
    column = energy.reshape(pairs, NPNO, 1)
    row = energy.reshape(pairs, 1, NPNO)
    hbm = pl.BlockSpec(memory_space=pl.ANY)
    own_spec = pl.BlockSpec((group, NPNO, NPNO), lambda i, q, s, f: (i + base, 0, 0))
    grid_spec = pltpu.PrefetchScalarGridSpec(
        num_scalar_prefetch=3,
        grid=(count // group,),
        in_specs=[hbm] * len(sources)
        + [
            pl.BlockSpec((group, 2, NPNO, NPNO), lambda i, q, s, f: (i + base, 0, 0, 0)),
            own_spec,
            pl.BlockSpec((group, NPNO, 1), lambda i, q, s, f: (i + base, 0, 0)),
            pl.BlockSpec((group, 1, NPNO), lambda i, q, s, f: (i + base, 0, 0)),
            own_spec,
        ],
        out_specs=pl.BlockSpec((group, NPNO, NPNO), lambda i, q, s, f: (i, 0, 0)),
        scratch_shapes=[
            pltpu.VMEM((2, 2 * group, NPNO, NPNO), jnp.float32),
            pltpu.SemaphoreType.DMA((2, 2 * group)),
        ],
    )
    flops = count * 2 * 4 * 2 * NPNO * NPNO * NPNO
    kernel = functools.partial(
        coupling_kernel, final=final, width=sources[0].shape[0], group=group, start=start, nsrc=len(sources)
    )
    return pl.pallas_call(
        kernel,
        grid_spec=grid_spec,
        out_shape=jax.ShapeDtypeStruct((count, NPNO, NPNO), jnp.float32),
        cost_estimate=pl.CostEstimate(
            flops=flops,
            bytes_accessed=count * NPNO * NPNO * (2 * 4 + 2 * 2 + 3 * 4),
            transcendentals=0,
        ),
    )(nb, sizes, fock, *sources, margin, exchange, column, row, own)


def chunked_halo(chunks):
    received = [halo_sources(chunk, "pair") for chunk in chunks]
    return [r[k] for k in range(3) for r in received]


def per_device(
    three_index,
    pno_coef,
    pair_orbitals,
    natural_orbital_class,
    pno_energy,
    margin,
    neighbour_pairs,
    fock_coupling,
):
    occ_dev = three_index.shape[0]
    pair_dev = pno_coef.shape[0]
    position = lax.axis_index("pair")
    sizes = class_size(natural_orbital_class)
    blocks = halo_sources(three_index, "pair")
    local_orbitals = (pair_orbitals - (position - 1) * occ_dev).astype(jnp.int32)
    half = pair_dev // 2
    presplit = halving_ready(half) and half % 8 == 0
    coef_t = jnp.swapaxes(pno_coef, 2, 3)
    left_t = left_halves(local_orbitals[:, 0] - occ_dev, sizes, three_index, coef_t)
    halves = [
        partial_exchange(
            local_orbitals[:, 0] - occ_dev,
            local_orbitals[:, 1],
            sizes,
            blocks,
            left_t,
            coef_t,
            c * half,
            half,
            send_first(c) if presplit else None,
        )
        for c in range(2)
    ]
    exchange_ints = sum_over_aux(halves, presplit)
    denominator = pno_energy[:, :, None] + pno_energy[:, None, :]
    local_rows = (neighbour_pairs - (position - 1) * pair_dev).astype(jnp.int32).reshape(-1)
    fock = fock_coupling.reshape(-1)

    chunk = pair_dev // 2 if pair_dev % 8 == 0 else pair_dev
    parts = [-(exchange_ints / denominator)]
    sources = chunked_halo(parts)
    amplitudes = jnp.concatenate(parts, axis=0)
    for iteration in range(1, ITERS):
        parts = [
            coupling_step(
                local_rows, sizes, fock, sources, margin, exchange_ints, pno_energy, amplitudes,
                False, c * chunk, chunk,
            )
            for c in range(pair_dev // chunk)
        ]
        sources = chunked_halo(parts)
        amplitudes = jnp.concatenate(parts, axis=0)
    residual = coupling_step(
        local_rows, sizes, fock, sources, margin, exchange_ints, pno_energy, amplitudes, True
    )
    return (amplitudes, residual)


def solution(mesh):
    return jax.shard_map(
        per_device,
        mesh=mesh,
        in_specs=(
            P("pair", "aux", None),
            P("pair", None, None, None),
            P("pair", None),
            P("pair"),
            P("pair", None),
            P("pair", None, None, None),
            P("pair", None),
            P("pair", None),
        ),
        out_specs=(P("pair", None, None), P("pair", None, None)),
        check_vma=False,
    )
```

```python
import functools

import jax
import jax.numpy as jnp
from jax import lax
from jax.experimental import pallas as pl
from jax.experimental.pallas import tpu as pltpu
from jax.sharding import PartitionSpec as P

NPNO = 192
ITERS = 2
CLASS_SIZES = (NPNO // 6, NPNO // 3, 2 * NPNO // 3, NPNO)


def halo_sources(cells, axis):
    count = lax.axis_size(axis)
    ends = count - 1
    from_left = lax.ppermute(cells, axis, [(i, i + 1) for i in range(ends)])
    from_right = lax.ppermute(cells, axis, [(i + 1, i) for i in range(ends)])
    return (from_left, cells, from_right)


def swap_over_aux(value, bit_even, bit_odd):
    pairs = lax.axis_size("pair")
    count = lax.axis_size("aux")
    perm = []
    for p in range(pairs):
        bit = bit_even if p % 2 == 0 else bit_odd
        perm += [(a * pairs + p, (a ^ bit) * pairs + p) for a in range(count)]
    return lax.ppermute(value, ("aux", "pair"), perm)


def halving_stream(piece, index, parity, bits, presplit=False):
    steps = [(b, o) for b, o in zip(bits, reversed(bits))]
    for step, (bit_even, bit_odd) in enumerate(steps):
        bit = jnp.where(parity == 0, bit_even, bit_odd)
        side = (index // bit) % 2
        half = piece[0].shape[0] if presplit and step == 0 else piece.shape[0] // 2
        if presplit and step == 0:
            send, keep = piece
        else:
            keep = lax.dynamic_slice_in_dim(piece, side * half, half, axis=0)
            send = lax.dynamic_slice_in_dim(piece, (1 - side) * half, half, axis=0)
        piece = keep + swap_over_aux(send, bit_even, bit_odd)
    for bit_even, bit_odd in reversed(steps):
        bit = jnp.where(parity == 0, bit_even, bit_odd)
        side = (index // bit) % 2
        other = swap_over_aux(piece, bit_even, bit_odd)
        length = piece.shape[0]
        full = jnp.zeros((2 * length,) + piece.shape[1:], piece.dtype)
        full = lax.dynamic_update_slice_in_dim(full, piece, side * length, axis=0)
        piece = lax.dynamic_update_slice_in_dim(full, other, (1 - side) * length, axis=0)
    return piece


def halving_ready(halves):
    return lax.axis_size("aux") == 4 and halves % 8 == 0


STREAM_ORDERS = ((1, 2), (2, 1))


def send_first(half_index):
    index = lax.axis_index("aux")
    even, odd = STREAM_ORDERS[half_index][0], STREAM_ORDERS[half_index][1]
    bit = jnp.where(lax.axis_index("pair") % 2 == 0, even, odd)
    return (1 - (index // bit) % 2).astype(jnp.int32).reshape(1)


def sum_over_aux(halves, presplit):
    if not presplit:
        if not halving_ready(halves[0].shape[0]):
            return lax.psum(jnp.concatenate(halves, axis=0), "aux")
    index = lax.axis_index("aux")
    parity = lax.axis_index("pair") % 2
    first = halving_stream(halves[0], index, parity, STREAM_ORDERS[0], presplit)
    second = halving_stream(halves[1], index, parity, STREAM_ORDERS[1], presplit)
    return jnp.concatenate([first, second], axis=0)


def class_size(natural_orbital_class):
    return jnp.where(
        natural_orbital_class == 0,
        NPNO // 6,
        jnp.where(
            natural_orbital_class == 1,
            NPNO // 3,
            jnp.where(natural_orbital_class == 2, 2 * NPNO // 3, NPNO),
        ),
    ).astype(jnp.int32)


def fetch_block(sources, width, local, dst, sem):
    index = jnp.clip(local // width, 0, len(sources) - 1)
    row = local % width
    for k, src in enumerate(sources):

        @pl.when(index == k)
        def _():
            pltpu.make_async_copy(src.at[row], dst, sem).start()


def left_kernel(lead_ref, size_ref, t_own, coef_ref, out_ref, lbuf, sems, *, occ, group):
    i = pl.program_id(0)
    steps = pl.num_programs(0)

    def fetch(step, slot):
        for g in range(group):
            p = step * group + g
            pltpu.make_async_copy(t_own.at[lead_ref[p] % occ], lbuf.at[slot, g], sems.at[slot, g]).start()

    @pl.when(i == 0)
    def _():
        fetch(0, 0)

    @pl.when(i + 1 < steps)
    def _():
        fetch(i + 1, (i + 1) % 2)

    slot = i % 2
    transposed = (((1,), (1,)), ((), ()))
    for g in range(group):
        p = i * group + g
        pltpu.make_async_copy(t_own.at[0], lbuf.at[slot, g], sems.at[slot, g]).wait()
        size = size_ref[p]
        out_ref[g] = jnp.zeros(out_ref.shape[1:], out_ref.dtype)
        for m in CLASS_SIZES:

            @pl.when(size == m)
            def _():
                first = coef_ref[g, 0, :m, :]
                left_t = lax.dot_general(first, lbuf[slot, g], transposed, preferred_element_type=jnp.float32)
                out_ref[g, :m, :] = left_t.astype(jnp.bfloat16)


def left_halves(lead, sizes, t_own, coef_t):
    pairs = coef_t.shape[0]
    group = next(g for g in (8, 4, 2, 1) if pairs % g == 0 and pairs // g >= 2)
    occ, nfit, npao = t_own.shape
    grid_spec = pltpu.PrefetchScalarGridSpec(
        num_scalar_prefetch=2,
        grid=(pairs // group,),
        in_specs=[
            pl.BlockSpec(memory_space=pl.ANY),
            pl.BlockSpec((group, 2, NPNO, npao), lambda i, a, s: (i, 0, 0, 0)),
        ],
        out_specs=pl.BlockSpec((group, NPNO, nfit), lambda i, a, s: (i, 0, 0)),
        scratch_shapes=[
            pltpu.VMEM((2, group, nfit, npao), t_own.dtype),
            pltpu.SemaphoreType.DMA((2, group)),
        ],
    )
    return pl.pallas_call(
        functools.partial(left_kernel, occ=occ, group=group),
        grid_spec=grid_spec,
        out_shape=jax.ShapeDtypeStruct((pairs, NPNO, nfit), jnp.bfloat16),
        cost_estimate=pl.CostEstimate(
            flops=pairs * 2 * nfit * npao * NPNO,
            bytes_accessed=pairs * (nfit * npao * 2 + 2 * npao * NPNO * 2 + NPNO * nfit * 2),
            transcendentals=0,
        ),
    )(lead, sizes, t_own, coef_t)


def exchange_kernel(lead_ref, trail_ref, size_ref, flip_ref, *refs, occ, group, start, split):
    if split:
        t_left, t_own, t_right, left_ref, coef_ref, send_ref, keep_ref, tbuf, sems, res_ref = refs
    else:
        t_left, t_own, t_right, left_ref, coef_ref, res_ref, tbuf, sems = refs
    out_ref = res_ref
    i = pl.program_id(0)
    steps = pl.num_programs(0)
    sources = (t_left, t_own, t_right)

    def fetch(step, slot):
        for g in range(group):
            p = start + step * group + g
            fetch_block(sources, occ, trail_ref[p], tbuf.at[slot, g], sems.at[slot, g])

    @pl.when(i == 0)
    def _():
        fetch(0, 0)

    @pl.when(i + 1 < steps)
    def _():
        fetch(i + 1, (i + 1) % 2)

    slot = i % 2
    transposed = (((1,), (1,)), ((), ()))
    for g in range(group):
        p = start + i * group + g
        pltpu.make_async_copy(t_own.at[0], tbuf.at[slot, g], sems.at[slot, g]).wait()
        size = size_ref[p]
        out_ref[g] = jnp.zeros((NPNO, NPNO), jnp.float32)
        for m in CLASS_SIZES:

            @pl.when(size == m)
            def _():
                second = coef_ref[g, 1, :m, :]
                right = lax.dot_general(tbuf[slot, g], second, transposed, preferred_element_type=jnp.float32)
                out_ref[g, :m, :m] = jnp.dot(
                    left_ref[g, :m, :], right.astype(jnp.bfloat16), preferred_element_type=jnp.float32
                )

    if split:
        @pl.when((i + flip_ref[0]) % 2 == 0)
        def _():
            send_ref[...] = res_ref[...]

        @pl.when((i + flip_ref[0]) % 2 == 1)
        def _():
            keep_ref[...] = res_ref[...]


def partial_exchange(lead, trail, sizes, sources, left_t, coef_t, start=0, count=None, flip=None):
    pairs = coef_t.shape[0]
    count = pairs if count is None else count
    group = next(g for g in (4, 2, 1) if count % g == 0 and start % g == 0)
    base = start // group
    steps = count // group
    split = flip is not None and steps == 2
    if not split:
        flip = jnp.zeros((1,), jnp.int32)
    occ, nfit, npao = sources[1].shape
    hbm = pl.BlockSpec(memory_space=pl.ANY)
    scratch = [
        pltpu.VMEM((2, group, nfit, npao), sources[1].dtype),
        pltpu.SemaphoreType.DMA((2, group)),
    ]
    block = (group, NPNO, NPNO)
    if split:
        fixed = pl.BlockSpec(block, lambda i, a, b, s, f: (0, 0, 0))
        out_specs = [fixed, fixed]
        out_shape = [jax.ShapeDtypeStruct(block, jnp.float32)] * 2
        scratch.append(pltpu.VMEM(block, jnp.float32))
    else:
        out_specs = pl.BlockSpec(block, lambda i, a, b, s, f: (i, 0, 0))
        out_shape = jax.ShapeDtypeStruct((count, NPNO, NPNO), jnp.float32)
    grid_spec = pltpu.PrefetchScalarGridSpec(
        num_scalar_prefetch=4,
        grid=(steps,),
        in_specs=[
            hbm,
            hbm,
            hbm,
            pl.BlockSpec((group, NPNO, nfit), lambda i, a, b, s, f: (i + base, 0, 0)),
            pl.BlockSpec((group, 2, NPNO, npao), lambda i, a, b, s, f: (i + base, 0, 0, 0)),
        ],
        out_specs=out_specs,
        scratch_shapes=scratch,
    )
    flops = count * (2 * 2 * nfit * npao * NPNO + 2 * nfit * NPNO * NPNO)
    return pl.pallas_call(
        functools.partial(exchange_kernel, occ=occ, group=group, start=start, split=split),
        grid_spec=grid_spec,
        out_shape=out_shape,
        cost_estimate=pl.CostEstimate(
            flops=flops,
            bytes_accessed=count * (2 * nfit * npao * 2 + 2 * npao * NPNO * 2 + NPNO * NPNO * 4),
            transcendentals=0,
        ),
    )(lead, trail, sizes, flip, *sources, left_t, coef_t)


def split_bf16(value):
    hi = value.astype(jnp.bfloat16)
    lo = (value - hi.astype(jnp.float32)).astype(jnp.bfloat16)
    return hi, lo


def mm(lhs, rhs, dims=(((1,), (0,)), ((), ()))):
    return lax.dot_general(lhs, rhs, dims, preferred_element_type=jnp.float32)


def coupling_kernel(nb_ref, size_ref, fock_ref, *refs, final, width, group, start, nsrc):
    sources = refs[:nsrc]
    margin_ref, ex_ref, col_ref, row_ref, own_ref, out_ref, tbuf, sems = refs[nsrc:]
    i = pl.program_id(0)
    steps = pl.num_programs(0)

    def fetch(step, slot):
        for k in range(2 * group):
            fetch_block(sources, width, nb_ref[2 * (start + group * step) + k], tbuf.at[slot, k], sems.at[slot, k])

    @pl.when(i == 0)
    def _():
        fetch(0, 0)

    @pl.when(i + 1 < steps)
    def _():
        fetch(i + 1, (i + 1) % 2)

    slot = i % 2
    transposed = (((1,), (1,)), ((), ()))
    for g in range(group):
        p = start + i * group + g
        splits = []
        for n in range(2):
            k = 2 * g + n
            pltpu.make_async_copy(sources[0].at[0], tbuf.at[slot, k], sems.at[slot, k]).wait()
            splits.append(split_bf16(tbuf[slot, k]))
        size = size_ref[p]
        out_ref[g] = jnp.zeros((NPNO, NPNO), jnp.float32)
        for m in CLASS_SIZES:

            @pl.when(size == m)
            def _():
                total = None
                for n in range(2):
                    side = margin_ref[g, n, :m, :]
                    t_hi, t_lo = splits[n]
                    inner = mm(side, t_hi) + mm(side, t_lo)
                    w_hi, w_lo = split_bf16(fock_ref[2 * p + n] * inner)
                    outer = mm(w_hi, side, transposed) + mm(w_lo, side, transposed)
                    total = outer if total is None else total + outer
                denominator = col_ref[g, :m, :] + row_ref[g, :, :m]
                amplitudes = own_ref[g, :m, :m]
                residual = ex_ref[g, :m, :m] + denominator * amplitudes - total
                if final:
                    out_ref[g, :m, :m] = residual
                else:
                    out_ref[g, :m, :m] = amplitudes - residual / denominator


def coupling_step(nb, sizes, fock, sources, margin, exchange, energy, own, final, start=0, count=None):
    pairs = own.shape[0]
    count = pairs if count is None else count
    group = next(g for g in (8, 4, 2, 1) if count % g == 0 and start % g == 0 and count // g >= 2)
    base = start // group
    column = energy.reshape(pairs, NPNO, 1)
    row = energy.reshape(pairs, 1, NPNO)
    hbm = pl.BlockSpec(memory_space=pl.ANY)
    own_spec = pl.BlockSpec((group, NPNO, NPNO), lambda i, q, s, f: (i + base, 0, 0))
    grid_spec = pltpu.PrefetchScalarGridSpec(
        num_scalar_prefetch=3,
        grid=(count // group,),
        in_specs=[hbm] * len(sources)
        + [
            pl.BlockSpec((group, 2, NPNO, NPNO), lambda i, q, s, f: (i + base, 0, 0, 0)),
            own_spec,
            pl.BlockSpec((group, NPNO, 1), lambda i, q, s, f: (i + base, 0, 0)),
            pl.BlockSpec((group, 1, NPNO), lambda i, q, s, f: (i + base, 0, 0)),
            own_spec,
        ],
        out_specs=pl.BlockSpec((group, NPNO, NPNO), lambda i, q, s, f: (i, 0, 0)),
        scratch_shapes=[
            pltpu.VMEM((2, 2 * group, NPNO, NPNO), jnp.float32),
            pltpu.SemaphoreType.DMA((2, 2 * group)),
        ],
    )
    flops = count * 2 * 4 * 2 * NPNO * NPNO * NPNO
    kernel = functools.partial(
        coupling_kernel, final=final, width=sources[0].shape[0], group=group, start=start, nsrc=len(sources)
    )
    return pl.pallas_call(
        kernel,
        grid_spec=grid_spec,
        out_shape=jax.ShapeDtypeStruct((count, NPNO, NPNO), jnp.float32),
        cost_estimate=pl.CostEstimate(
            flops=flops,
            bytes_accessed=count * NPNO * NPNO * (2 * 4 + 2 * 2 + 3 * 4),
            transcendentals=0,
        ),
    )(nb, sizes, fock, *sources, margin, exchange, column, row, own)


def chunked_halo(chunks):
    received = [halo_sources(chunk, "pair") for chunk in chunks]
    return [r[k] for k in range(3) for r in received]


def per_device(
    three_index,
    pno_coef,
    pair_orbitals,
    natural_orbital_class,
    pno_energy,
    margin,
    neighbour_pairs,
    fock_coupling,
):
    occ_dev = three_index.shape[0]
    pair_dev = pno_coef.shape[0]
    position = lax.axis_index("pair")
    sizes = class_size(natural_orbital_class)
    blocks = halo_sources(three_index, "pair")
    local_orbitals = (pair_orbitals - (position - 1) * occ_dev).astype(jnp.int32)
    half = pair_dev // 2
    presplit = halving_ready(half) and half % 8 == 0
    coef_t = jnp.swapaxes(pno_coef, 2, 3)
    left_t = left_halves(local_orbitals[:, 0] - occ_dev, sizes, three_index, coef_t)
    halves = [
        partial_exchange(
            local_orbitals[:, 0] - occ_dev,
            local_orbitals[:, 1],
            sizes,
            blocks,
            left_t,
            coef_t,
            c * half,
            half,
            send_first(c) if presplit else None,
        )
        for c in range(2)
    ]
    exchange_ints = sum_over_aux(halves, presplit)
    denominator = pno_energy[:, :, None] + pno_energy[:, None, :]
    local_rows = (neighbour_pairs - (position - 1) * pair_dev).astype(jnp.int32).reshape(-1)
    fock = fock_coupling.reshape(-1)

    chunk = pair_dev // 2 if pair_dev % 8 == 0 else pair_dev
    parts = [-(exchange_ints / denominator)]
    sources = chunked_halo(parts)
    amplitudes = jnp.concatenate(parts, axis=0)
    for iteration in range(1, ITERS):
        parts = [
            coupling_step(
                local_rows, sizes, fock, sources, margin, exchange_ints, pno_energy, amplitudes,
                False, c * chunk, chunk,
            )
            for c in range(pair_dev // chunk)
        ]
        sources = chunked_halo(parts)
        amplitudes = jnp.concatenate(parts, axis=0)
    residual = coupling_step(
        local_rows, sizes, fock, sources, margin, exchange_ints, pno_energy, amplitudes, True
    )
    return (amplitudes, residual)


def solution(mesh):
    return jax.shard_map(
        per_device,
        mesh=mesh,
        in_specs=(
            P("pair", "aux", None),
            P("pair", None, None, None),
            P("pair", None),
            P("pair"),
            P("pair", None),
            P("pair", None, None, None),
            P("pair", None),
            P("pair", None),
        ),
        out_specs=(P("pair", None, None), P("pair", None, None)),
        check_vma=False,
    )
```

```python
import functools

import jax
import jax.numpy as jnp
from jax import lax
from jax.experimental import pallas as pl
from jax.experimental.pallas import tpu as pltpu
from jax.sharding import PartitionSpec as P

NPNO = 192
ITERS = 2
CLASS_SIZES = (NPNO // 6, NPNO // 3, 2 * NPNO // 3, NPNO)


def halo_sources(cells, axis):
    count = lax.axis_size(axis)
    ends = count - 1
    from_left = lax.ppermute(cells, axis, [(i, i + 1) for i in range(ends)])
    from_right = lax.ppermute(cells, axis, [(i + 1, i) for i in range(ends)])
    return (from_left, cells, from_right)


def swap_over_aux(value, bit_even, bit_odd):
    pairs = lax.axis_size("pair")
    count = lax.axis_size("aux")
    perm = []
    for p in range(pairs):
        bit = bit_even if p % 2 == 0 else bit_odd
        perm += [(a * pairs + p, (a ^ bit) * pairs + p) for a in range(count)]
    return lax.ppermute(value, ("aux", "pair"), perm)


def sum_pair(kept, received):
    return kept + received


def halving_stream(piece, index, parity, bits, presplit=False):
    steps = [(b, o) for b, o in zip(bits, reversed(bits))]
    for step, (bit_even, bit_odd) in enumerate(steps):
        bit = jnp.where(parity == 0, bit_even, bit_odd)
        side = (index // bit) % 2
        half = piece[0].shape[0] if presplit and step == 0 else None
        if presplit and step == 0:
            send, keep = piece
        elif isinstance(piece, tuple):
            def cut(offset):
                return sum_pair(*(lax.dynamic_slice_in_dim(v, offset, half, axis=0) for v in piece))

            half = piece[0].shape[0] // 2
            keep, send = cut(side * half), cut((1 - side) * half)
        else:
            half = piece.shape[0] // 2
            keep = lax.dynamic_slice_in_dim(piece, side * half, half, axis=0)
            send = lax.dynamic_slice_in_dim(piece, (1 - side) * half, half, axis=0)
        piece = (keep, swap_over_aux(send, bit_even, bit_odd))
    piece = sum_pair(*piece)
    for bit_even, bit_odd in reversed(steps):
        bit = jnp.where(parity == 0, bit_even, bit_odd)
        side = (index // bit) % 2
        other = swap_over_aux(piece, bit_even, bit_odd)
        length = piece.shape[0]
        full = jnp.zeros((2 * length,) + piece.shape[1:], piece.dtype)
        full = lax.dynamic_update_slice_in_dim(full, piece, side * length, axis=0)
        piece = lax.dynamic_update_slice_in_dim(full, other, (1 - side) * length, axis=0)
    return piece


def halving_ready(halves):
    return lax.axis_size("aux") == 4 and halves % 8 == 0


STREAM_ORDERS = ((1, 2), (2, 1))


def send_first(half_index):
    index = lax.axis_index("aux")
    even, odd = STREAM_ORDERS[half_index][0], STREAM_ORDERS[half_index][1]
    bit = jnp.where(lax.axis_index("pair") % 2 == 0, even, odd)
    return (1 - (index // bit) % 2).astype(jnp.int32).reshape(1)


def sum_over_aux(halves, presplit):
    if not presplit:
        if not halving_ready(halves[0].shape[0]):
            return lax.psum(jnp.concatenate(halves, axis=0), "aux")
    index = lax.axis_index("aux")
    parity = lax.axis_index("pair") % 2
    first = halving_stream(halves[0], index, parity, STREAM_ORDERS[0], presplit)
    second = halving_stream(halves[1], index, parity, STREAM_ORDERS[1], presplit)
    return jnp.concatenate([first, second], axis=0)


def class_size(natural_orbital_class):
    return jnp.where(
        natural_orbital_class == 0,
        NPNO // 6,
        jnp.where(
            natural_orbital_class == 1,
            NPNO // 3,
            jnp.where(natural_orbital_class == 2, 2 * NPNO // 3, NPNO),
        ),
    ).astype(jnp.int32)


def fetch_block(sources, width, local, dst, sem):
    index = jnp.clip(local // width, 0, len(sources) - 1)
    row = local % width
    for k, src in enumerate(sources):

        @pl.when(index == k)
        def _():
            pltpu.make_async_copy(src.at[row], dst, sem).start()


def left_kernel(lead_ref, size_ref, t_own, coef_ref, out_ref, lbuf, sems, *, occ, group):
    i = pl.program_id(0)
    steps = pl.num_programs(0)

    def fetch(step, slot):
        for g in range(group):
            p = step * group + g
            pltpu.make_async_copy(t_own.at[lead_ref[p] % occ], lbuf.at[slot, g], sems.at[slot, g]).start()

    @pl.when(i == 0)
    def _():
        fetch(0, 0)

    @pl.when(i + 1 < steps)
    def _():
        fetch(i + 1, (i + 1) % 2)

    slot = i % 2
    transposed = (((1,), (1,)), ((), ()))
    for g in range(group):
        p = i * group + g
        pltpu.make_async_copy(t_own.at[0], lbuf.at[slot, g], sems.at[slot, g]).wait()
        size = size_ref[p]
        out_ref[g] = jnp.zeros(out_ref.shape[1:], out_ref.dtype)
        for m in CLASS_SIZES:

            @pl.when(size == m)
            def _():
                first = coef_ref[g, 0, :m, :]
                left_t = lax.dot_general(first, lbuf[slot, g], transposed, preferred_element_type=jnp.float32)
                out_ref[g, :m, :] = left_t.astype(jnp.bfloat16)


def left_halves(lead, sizes, t_own, coef_t):
    pairs = coef_t.shape[0]
    group = next(g for g in (4, 2, 1) if pairs % g == 0)
    occ, nfit, npao = t_own.shape
    grid_spec = pltpu.PrefetchScalarGridSpec(
        num_scalar_prefetch=2,
        grid=(pairs // group,),
        in_specs=[
            pl.BlockSpec(memory_space=pl.ANY),
            pl.BlockSpec((group, 2, NPNO, npao), lambda i, a, s: (i, 0, 0, 0)),
        ],
        out_specs=pl.BlockSpec((group, NPNO, nfit), lambda i, a, s: (i, 0, 0)),
        scratch_shapes=[
            pltpu.VMEM((2, group, nfit, npao), t_own.dtype),
            pltpu.SemaphoreType.DMA((2, group)),
        ],
    )
    return pl.pallas_call(
        functools.partial(left_kernel, occ=occ, group=group),
        grid_spec=grid_spec,
        out_shape=jax.ShapeDtypeStruct((pairs, NPNO, nfit), jnp.bfloat16),
        cost_estimate=pl.CostEstimate(
            flops=pairs * 2 * nfit * npao * NPNO,
            bytes_accessed=pairs * (nfit * npao * 2 + 2 * npao * NPNO * 2 + NPNO * nfit * 2),
            transcendentals=0,
        ),
    )(lead, sizes, t_own, coef_t)


def exchange_kernel(lead_ref, trail_ref, size_ref, flip_ref, *refs, occ, group, start, split):
    if split:
        t_left, t_own, t_right, left_ref, coef_ref, send_ref, keep_ref, tbuf, sems, res_ref = refs
    else:
        t_left, t_own, t_right, left_ref, coef_ref, res_ref, tbuf, sems = refs
    out_ref = res_ref
    i = pl.program_id(0)
    steps = pl.num_programs(0)
    sources = (t_left, t_own, t_right)

    def fetch(step, slot):
        for g in range(group):
            p = start + step * group + g
            fetch_block(sources, occ, trail_ref[p], tbuf.at[slot, g], sems.at[slot, g])

    @pl.when(i == 0)
    def _():
        fetch(0, 0)

    @pl.when(i + 1 < steps)
    def _():
        fetch(i + 1, (i + 1) % 2)

    slot = i % 2
    transposed = (((1,), (1,)), ((), ()))
    for g in range(group):
        p = start + i * group + g
        pltpu.make_async_copy(t_own.at[0], tbuf.at[slot, g], sems.at[slot, g]).wait()
        size = size_ref[p]
        out_ref[g] = jnp.zeros((NPNO, NPNO), jnp.float32)
        for m in CLASS_SIZES:

            @pl.when(size == m)
            def _():
                second = coef_ref[g, 1, :m, :]
                right = lax.dot_general(tbuf[slot, g], second, transposed, preferred_element_type=jnp.float32)
                out_ref[g, :m, :m] = jnp.dot(
                    left_ref[g, :m, :], right.astype(jnp.bfloat16), preferred_element_type=jnp.float32
                )

    if split:
        @pl.when((i + flip_ref[0]) % 2 == 0)
        def _():
            send_ref[...] = res_ref[...]

        @pl.when((i + flip_ref[0]) % 2 == 1)
        def _():
            keep_ref[...] = res_ref[...]


def partial_exchange(lead, trail, sizes, sources, left_t, coef_t, start=0, count=None, flip=None):
    pairs = coef_t.shape[0]
    count = pairs if count is None else count
    group = next(g for g in (4, 2, 1) if count % g == 0 and start % g == 0)
    base = start // group
    steps = count // group
    split = flip is not None and steps == 2
    if not split:
        flip = jnp.zeros((1,), jnp.int32)
    occ, nfit, npao = sources[1].shape
    hbm = pl.BlockSpec(memory_space=pl.ANY)
    scratch = [
        pltpu.VMEM((2, group, nfit, npao), sources[1].dtype),
        pltpu.SemaphoreType.DMA((2, group)),
    ]
    block = (group, NPNO, NPNO)
    if split:
        fixed = pl.BlockSpec(block, lambda i, a, b, s, f: (0, 0, 0))
        out_specs = [fixed, fixed]
        out_shape = [jax.ShapeDtypeStruct(block, jnp.float32)] * 2
        scratch.append(pltpu.VMEM(block, jnp.float32))
    else:
        out_specs = pl.BlockSpec(block, lambda i, a, b, s, f: (i, 0, 0))
        out_shape = jax.ShapeDtypeStruct((count, NPNO, NPNO), jnp.float32)
    grid_spec = pltpu.PrefetchScalarGridSpec(
        num_scalar_prefetch=4,
        grid=(steps,),
        in_specs=[
            hbm,
            hbm,
            hbm,
            pl.BlockSpec((group, NPNO, nfit), lambda i, a, b, s, f: (i + base, 0, 0)),
            pl.BlockSpec((group, 2, NPNO, npao), lambda i, a, b, s, f: (i + base, 0, 0, 0)),
        ],
        out_specs=out_specs,
        scratch_shapes=scratch,
    )
    flops = count * (2 * 2 * nfit * npao * NPNO + 2 * nfit * NPNO * NPNO)
    return pl.pallas_call(
        functools.partial(exchange_kernel, occ=occ, group=group, start=start, split=split),
        grid_spec=grid_spec,
        out_shape=out_shape,
        cost_estimate=pl.CostEstimate(
            flops=flops,
            bytes_accessed=count * (2 * nfit * npao * 2 + 2 * npao * NPNO * 2 + NPNO * NPNO * 4),
            transcendentals=0,
        ),
    )(lead, trail, sizes, flip, *sources, left_t, coef_t)


def split_bf16(value):
    hi = value.astype(jnp.bfloat16)
    lo = (value - hi.astype(jnp.float32)).astype(jnp.bfloat16)
    return hi, lo


def mm(lhs, rhs, dims=(((1,), (0,)), ((), ()))):
    return lax.dot_general(lhs, rhs, dims, preferred_element_type=jnp.float32)


def coupling_kernel(nb_ref, size_ref, fock_ref, *refs, final, width, group, start, nsrc):
    sources = refs[:nsrc]
    margin_ref, ex_ref, col_ref, row_ref, own_ref, out_ref, tbuf, sems = refs[nsrc:]
    i = pl.program_id(0)
    steps = pl.num_programs(0)

    def fetch(step, slot):
        for k in range(2 * group):
            fetch_block(sources, width, nb_ref[2 * (start + group * step) + k], tbuf.at[slot, k], sems.at[slot, k])

    @pl.when(i == 0)
    def _():
        fetch(0, 0)

    @pl.when(i + 1 < steps)
    def _():
        fetch(i + 1, (i + 1) % 2)

    slot = i % 2
    transposed = (((1,), (1,)), ((), ()))
    for g in range(group):
        p = start + i * group + g
        splits = []
        for n in range(2):
            k = 2 * g + n
            pltpu.make_async_copy(sources[0].at[0], tbuf.at[slot, k], sems.at[slot, k]).wait()
            splits.append(split_bf16(tbuf[slot, k]))
        size = size_ref[p]
        out_ref[g] = jnp.zeros((NPNO, NPNO), jnp.float32)
        for m in CLASS_SIZES:

            @pl.when(size == m)
            def _():
                total = None
                for n in range(2):
                    side = margin_ref[g, n, :m, :]
                    t_hi, t_lo = splits[n]
                    inner = mm(side, t_hi) + mm(side, t_lo)
                    w_hi, w_lo = split_bf16(fock_ref[2 * p + n] * inner)
                    outer = mm(w_hi, side, transposed) + mm(w_lo, side, transposed)
                    total = outer if total is None else total + outer
                denominator = col_ref[g, :m, :] + row_ref[g, :, :m]
                amplitudes = own_ref[g, :m, :m]
                residual = ex_ref[g, :m, :m] + denominator * amplitudes - total
                if final:
                    out_ref[g, :m, :m] = residual
                else:
                    out_ref[g, :m, :m] = amplitudes - residual / denominator


def coupling_step(nb, sizes, fock, sources, margin, exchange, energy, own, final, start=0, count=None):
    pairs = own.shape[0]
    count = pairs if count is None else count
    group = next(g for g in (4, 2, 1) if count % g == 0 and start % g == 0)
    base = start // group
    column = energy.reshape(pairs, NPNO, 1)
    row = energy.reshape(pairs, 1, NPNO)
    hbm = pl.BlockSpec(memory_space=pl.ANY)
    own_spec = pl.BlockSpec((group, NPNO, NPNO), lambda i, q, s, f: (i + base, 0, 0))
    grid_spec = pltpu.PrefetchScalarGridSpec(
        num_scalar_prefetch=3,
        grid=(count // group,),
        in_specs=[hbm] * len(sources)
        + [
            pl.BlockSpec((group, 2, NPNO, NPNO), lambda i, q, s, f: (i + base, 0, 0, 0)),
            own_spec,
            pl.BlockSpec((group, NPNO, 1), lambda i, q, s, f: (i + base, 0, 0)),
            pl.BlockSpec((group, 1, NPNO), lambda i, q, s, f: (i + base, 0, 0)),
            own_spec,
        ],
        out_specs=pl.BlockSpec((group, NPNO, NPNO), lambda i, q, s, f: (i, 0, 0)),
        scratch_shapes=[
            pltpu.VMEM((2, 2 * group, NPNO, NPNO), jnp.float32),
            pltpu.SemaphoreType.DMA((2, 2 * group)),
        ],
    )
    flops = count * 2 * 4 * 2 * NPNO * NPNO * NPNO
    kernel = functools.partial(
        coupling_kernel, final=final, width=sources[0].shape[0], group=group, start=start, nsrc=len(sources)
    )
    return pl.pallas_call(
        kernel,
        grid_spec=grid_spec,
        out_shape=jax.ShapeDtypeStruct((count, NPNO, NPNO), jnp.float32),
        cost_estimate=pl.CostEstimate(
            flops=flops,
            bytes_accessed=count * NPNO * NPNO * (2 * 4 + 2 * 2 + 3 * 4),
            transcendentals=0,
        ),
    )(nb, sizes, fock, *sources, margin, exchange, column, row, own)


def chunked_halo(chunks):
    received = [halo_sources(chunk, "pair") for chunk in chunks]
    return [r[k] for k in range(3) for r in received]


def per_device(
    three_index,
    pno_coef,
    pair_orbitals,
    natural_orbital_class,
    pno_energy,
    margin,
    neighbour_pairs,
    fock_coupling,
):
    occ_dev = three_index.shape[0]
    pair_dev = pno_coef.shape[0]
    position = lax.axis_index("pair")
    sizes = class_size(natural_orbital_class)
    blocks = halo_sources(three_index, "pair")
    local_orbitals = (pair_orbitals - (position - 1) * occ_dev).astype(jnp.int32)
    half = pair_dev // 2
    presplit = halving_ready(half) and half % 8 == 0
    coef_t = jnp.swapaxes(pno_coef, 2, 3)
    left_t = left_halves(local_orbitals[:, 0] - occ_dev, sizes, three_index, coef_t)
    halves = [
        partial_exchange(
            local_orbitals[:, 0] - occ_dev,
            local_orbitals[:, 1],
            sizes,
            blocks,
            left_t,
            coef_t,
            c * half,
            half,
            send_first(c) if presplit else None,
        )
        for c in range(2)
    ]
    exchange_ints = sum_over_aux(halves, presplit)
    denominator = pno_energy[:, :, None] + pno_energy[:, None, :]
    local_rows = (neighbour_pairs - (position - 1) * pair_dev).astype(jnp.int32).reshape(-1)
    fock = fock_coupling.reshape(-1)

    chunk = pair_dev // 2 if pair_dev % 8 == 0 else pair_dev
    parts = [-(exchange_ints / denominator)]
    sources = chunked_halo(parts)
    amplitudes = jnp.concatenate(parts, axis=0)
    for iteration in range(1, ITERS):
        parts = [
            coupling_step(
                local_rows, sizes, fock, sources, margin, exchange_ints, pno_energy, amplitudes,
                False, c * chunk, chunk,
            )
            for c in range(pair_dev // chunk)
        ]
        sources = chunked_halo(parts)
        amplitudes = jnp.concatenate(parts, axis=0)
    residual = coupling_step(
        local_rows, sizes, fock, sources, margin, exchange_ints, pno_energy, amplitudes, True
    )
    return (amplitudes, residual)


def solution(mesh):
    return jax.shard_map(
        per_device,
        mesh=mesh,
        in_specs=(
            P("pair", "aux", None),
            P("pair", None, None, None),
            P("pair", None),
            P("pair"),
            P("pair", None),
            P("pair", None, None, None),
            P("pair", None),
            P("pair", None),
        ),
        out_specs=(P("pair", None, None), P("pair", None, None)),
        check_vma=False,
    )
```

```python
import functools

import jax
import jax.numpy as jnp
from jax import lax
from jax.experimental import pallas as pl
from jax.experimental.pallas import tpu as pltpu
from jax.sharding import PartitionSpec as P

NPNO = 192
ITERS = 2
CLASS_SIZES = (NPNO // 6, NPNO // 3, 2 * NPNO // 3, NPNO)


def halo_sources(cells, axis):
    count = lax.axis_size(axis)
    ends = count - 1
    from_left = lax.ppermute(cells, axis, [(i, i + 1) for i in range(ends)])
    from_right = lax.ppermute(cells, axis, [(i + 1, i) for i in range(ends)])
    return (from_left, cells, from_right)


def swap_over_aux(value, bit_even, bit_odd):
    pairs = lax.axis_size("pair")
    count = lax.axis_size("aux")
    perm = []
    for p in range(pairs):
        bit = bit_even if p % 2 == 0 else bit_odd
        perm += [(a * pairs + p, (a ^ bit) * pairs + p) for a in range(count)]
    return lax.ppermute(value, ("aux", "pair"), perm)


def halving_stream(piece, index, parity, bits, presplit=False):
    steps = [(b, o) for b, o in zip(bits, reversed(bits))]
    for step, (bit_even, bit_odd) in enumerate(steps):
        bit = jnp.where(parity == 0, bit_even, bit_odd)
        side = (index // bit) % 2
        half = piece[0].shape[0] if presplit and step == 0 else piece.shape[0] // 2
        if presplit and step == 0:
            send, keep = piece
        else:
            keep = lax.dynamic_slice_in_dim(piece, side * half, half, axis=0)
            send = lax.dynamic_slice_in_dim(piece, (1 - side) * half, half, axis=0)
        piece = keep + swap_over_aux(send, bit_even, bit_odd)
    for bit_even, bit_odd in reversed(steps):
        bit = jnp.where(parity == 0, bit_even, bit_odd)
        side = (index // bit) % 2
        other = swap_over_aux(piece, bit_even, bit_odd)
        piece = jnp.where(
            side == 0, jnp.concatenate([piece, other], axis=0), jnp.concatenate([other, piece], axis=0)
        )
    return piece


def halving_ready(halves):
    return lax.axis_size("aux") == 4 and halves % 8 == 0


STREAM_ORDERS = ((1, 2), (2, 1))


def send_first(half_index):
    index = lax.axis_index("aux")
    even, odd = STREAM_ORDERS[half_index][0], STREAM_ORDERS[half_index][1]
    bit = jnp.where(lax.axis_index("pair") % 2 == 0, even, odd)
    return (1 - (index // bit) % 2).astype(jnp.int32).reshape(1)


def sum_over_aux(halves, presplit):
    if not presplit:
        if not halving_ready(halves[0].shape[0]):
            return lax.psum(jnp.concatenate(halves, axis=0), "aux")
    index = lax.axis_index("aux")
    parity = lax.axis_index("pair") % 2
    first = halving_stream(halves[0], index, parity, STREAM_ORDERS[0], presplit)
    second = halving_stream(halves[1], index, parity, STREAM_ORDERS[1], presplit)
    return jnp.concatenate([first, second], axis=0)


def class_size(natural_orbital_class):
    return jnp.where(
        natural_orbital_class == 0,
        NPNO // 6,
        jnp.where(
            natural_orbital_class == 1,
            NPNO // 3,
            jnp.where(natural_orbital_class == 2, 2 * NPNO // 3, NPNO),
        ),
    ).astype(jnp.int32)


def fetch_block(sources, width, local, dst, sem):
    index = jnp.clip(local // width, 0, len(sources) - 1)
    row = local % width
    for k, src in enumerate(sources):

        @pl.when(index == k)
        def _():
            pltpu.make_async_copy(src.at[row], dst, sem).start()


def left_kernel(lead_ref, size_ref, t_own, coef_ref, out_ref, lbuf, sems, *, occ, group):
    i = pl.program_id(0)
    steps = pl.num_programs(0)

    def fetch(step, slot):
        for g in range(group):
            p = step * group + g
            pltpu.make_async_copy(t_own.at[lead_ref[p] % occ], lbuf.at[slot, g], sems.at[slot, g]).start()

    @pl.when(i == 0)
    def _():
        fetch(0, 0)

    @pl.when(i + 1 < steps)
    def _():
        fetch(i + 1, (i + 1) % 2)

    slot = i % 2
    transposed = (((1,), (1,)), ((), ()))
    for g in range(group):
        p = i * group + g
        pltpu.make_async_copy(t_own.at[0], lbuf.at[slot, g], sems.at[slot, g]).wait()
        size = size_ref[p]
        out_ref[g] = jnp.zeros(out_ref.shape[1:], out_ref.dtype)
        for m in CLASS_SIZES:

            @pl.when(size == m)
            def _():
                first = coef_ref[g, 0, :m, :]
                left_t = lax.dot_general(first, lbuf[slot, g], transposed, preferred_element_type=jnp.float32)
                out_ref[g, :m, :] = left_t.astype(jnp.bfloat16)


def left_halves(lead, sizes, t_own, coef_t):
    pairs = coef_t.shape[0]
    group = next(g for g in (4, 2, 1) if pairs % g == 0)
    occ, nfit, npao = t_own.shape
    grid_spec = pltpu.PrefetchScalarGridSpec(
        num_scalar_prefetch=2,
        grid=(pairs // group,),
        in_specs=[
            pl.BlockSpec(memory_space=pl.ANY),
            pl.BlockSpec((group, 2, NPNO, npao), lambda i, a, s: (i, 0, 0, 0)),
        ],
        out_specs=pl.BlockSpec((group, NPNO, nfit), lambda i, a, s: (i, 0, 0)),
        scratch_shapes=[
            pltpu.VMEM((2, group, nfit, npao), t_own.dtype),
            pltpu.SemaphoreType.DMA((2, group)),
        ],
    )
    return pl.pallas_call(
        functools.partial(left_kernel, occ=occ, group=group),
        grid_spec=grid_spec,
        out_shape=jax.ShapeDtypeStruct((pairs, NPNO, nfit), jnp.bfloat16),
        cost_estimate=pl.CostEstimate(
            flops=pairs * 2 * nfit * npao * NPNO,
            bytes_accessed=pairs * (nfit * npao * 2 + 2 * npao * NPNO * 2 + NPNO * nfit * 2),
            transcendentals=0,
        ),
    )(lead, sizes, t_own, coef_t)


def exchange_kernel(lead_ref, trail_ref, size_ref, flip_ref, *refs, occ, group, start, split):
    if split:
        t_left, t_own, t_right, left_ref, coef_ref, send_ref, keep_ref, tbuf, sems, res_ref = refs
    else:
        t_left, t_own, t_right, left_ref, coef_ref, res_ref, tbuf, sems = refs
    out_ref = res_ref
    i = pl.program_id(0)
    steps = pl.num_programs(0)
    sources = (t_left, t_own, t_right)

    def fetch(step, slot):
        for g in range(group):
            p = start + step * group + g
            fetch_block(sources, occ, trail_ref[p], tbuf.at[slot, g], sems.at[slot, g])

    @pl.when(i == 0)
    def _():
        fetch(0, 0)

    @pl.when(i + 1 < steps)
    def _():
        fetch(i + 1, (i + 1) % 2)

    slot = i % 2
    transposed = (((1,), (1,)), ((), ()))
    for g in range(group):
        p = start + i * group + g
        pltpu.make_async_copy(t_own.at[0], tbuf.at[slot, g], sems.at[slot, g]).wait()
        size = size_ref[p]
        out_ref[g] = jnp.zeros((NPNO, NPNO), jnp.float32)
        for m in CLASS_SIZES:

            @pl.when(size == m)
            def _():
                second = coef_ref[g, 1, :m, :]
                right = lax.dot_general(tbuf[slot, g], second, transposed, preferred_element_type=jnp.float32)
                out_ref[g, :m, :m] = jnp.dot(
                    left_ref[g, :m, :], right.astype(jnp.bfloat16), preferred_element_type=jnp.float32
                )

    if split:
        @pl.when((i + flip_ref[0]) % 2 == 0)
        def _():
            send_ref[...] = res_ref[...]

        @pl.when((i + flip_ref[0]) % 2 == 1)
        def _():
            keep_ref[...] = res_ref[...]


def partial_exchange(lead, trail, sizes, sources, left_t, coef_t, start=0, count=None, flip=None):
    pairs = coef_t.shape[0]
    count = pairs if count is None else count
    group = next(g for g in (4, 2, 1) if count % g == 0 and start % g == 0)
    base = start // group
    steps = count // group
    split = flip is not None and steps == 2
    if not split:
        flip = jnp.zeros((1,), jnp.int32)
    occ, nfit, npao = sources[1].shape
    hbm = pl.BlockSpec(memory_space=pl.ANY)
    scratch = [
        pltpu.VMEM((2, group, nfit, npao), sources[1].dtype),
        pltpu.SemaphoreType.DMA((2, group)),
    ]
    block = (group, NPNO, NPNO)
    if split:
        fixed = pl.BlockSpec(block, lambda i, a, b, s, f: (0, 0, 0))
        out_specs = [fixed, fixed]
        out_shape = [jax.ShapeDtypeStruct(block, jnp.float32)] * 2
        scratch.append(pltpu.VMEM(block, jnp.float32))
    else:
        out_specs = pl.BlockSpec(block, lambda i, a, b, s, f: (i, 0, 0))
        out_shape = jax.ShapeDtypeStruct((count, NPNO, NPNO), jnp.float32)
    grid_spec = pltpu.PrefetchScalarGridSpec(
        num_scalar_prefetch=4,
        grid=(steps,),
        in_specs=[
            hbm,
            hbm,
            hbm,
            pl.BlockSpec((group, NPNO, nfit), lambda i, a, b, s, f: (i + base, 0, 0)),
            pl.BlockSpec((group, 2, NPNO, npao), lambda i, a, b, s, f: (i + base, 0, 0, 0)),
        ],
        out_specs=out_specs,
        scratch_shapes=scratch,
    )
    flops = count * (2 * 2 * nfit * npao * NPNO + 2 * nfit * NPNO * NPNO)
    return pl.pallas_call(
        functools.partial(exchange_kernel, occ=occ, group=group, start=start, split=split),
        grid_spec=grid_spec,
        out_shape=out_shape,
        cost_estimate=pl.CostEstimate(
            flops=flops,
            bytes_accessed=count * (2 * nfit * npao * 2 + 2 * npao * NPNO * 2 + NPNO * NPNO * 4),
            transcendentals=0,
        ),
    )(lead, trail, sizes, flip, *sources, left_t, coef_t)


def split_bf16(value):
    hi = value.astype(jnp.bfloat16)
    lo = (value - hi.astype(jnp.float32)).astype(jnp.bfloat16)
    return hi, lo


def mm(lhs, rhs, dims=(((1,), (0,)), ((), ()))):
    return lax.dot_general(lhs, rhs, dims, preferred_element_type=jnp.float32)


def coupling_kernel(nb_ref, size_ref, fock_ref, *refs, final, width, group, start, nsrc):
    sources = refs[:nsrc]
    margin_ref, ex_ref, col_ref, row_ref, own_ref, out_ref, tbuf, sems = refs[nsrc:]
    i = pl.program_id(0)
    steps = pl.num_programs(0)

    def fetch(step, slot):
        for k in range(2 * group):
            fetch_block(sources, width, nb_ref[2 * (start + group * step) + k], tbuf.at[slot, k], sems.at[slot, k])

    @pl.when(i == 0)
    def _():
        fetch(0, 0)

    @pl.when(i + 1 < steps)
    def _():
        fetch(i + 1, (i + 1) % 2)

    slot = i % 2
    transposed = (((1,), (1,)), ((), ()))
    for g in range(group):
        p = start + i * group + g
        splits = []
        for n in range(2):
            k = 2 * g + n
            pltpu.make_async_copy(sources[0].at[0], tbuf.at[slot, k], sems.at[slot, k]).wait()
            splits.append(split_bf16(tbuf[slot, k]))
        size = size_ref[p]
        out_ref[g] = jnp.zeros((NPNO, NPNO), jnp.float32)
        for m in CLASS_SIZES:

            @pl.when(size == m)
            def _():
                total = None
                for n in range(2):
                    side = margin_ref[g, n, :m, :]
                    t_hi, t_lo = splits[n]
                    inner = mm(side, t_hi) + mm(side, t_lo)
                    w_hi, w_lo = split_bf16(fock_ref[2 * p + n] * inner)
                    outer = mm(w_hi, side, transposed) + mm(w_lo, side, transposed)
                    total = outer if total is None else total + outer
                denominator = col_ref[g, :m, :] + row_ref[g, :, :m]
                amplitudes = own_ref[g, :m, :m]
                residual = ex_ref[g, :m, :m] + denominator * amplitudes - total
                if final:
                    out_ref[g, :m, :m] = residual
                else:
                    out_ref[g, :m, :m] = amplitudes - residual / denominator


def coupling_step(nb, sizes, fock, sources, margin, exchange, energy, own, final, start=0, count=None):
    pairs = own.shape[0]
    count = pairs if count is None else count
    group = next(g for g in (4, 2, 1) if count % g == 0 and start % g == 0)
    base = start // group
    column = energy.reshape(pairs, NPNO, 1)
    row = energy.reshape(pairs, 1, NPNO)
    hbm = pl.BlockSpec(memory_space=pl.ANY)
    own_spec = pl.BlockSpec((group, NPNO, NPNO), lambda i, q, s, f: (i + base, 0, 0))
    grid_spec = pltpu.PrefetchScalarGridSpec(
        num_scalar_prefetch=3,
        grid=(count // group,),
        in_specs=[hbm] * len(sources)
        + [
            pl.BlockSpec((group, 2, NPNO, NPNO), lambda i, q, s, f: (i + base, 0, 0, 0)),
            own_spec,
            pl.BlockSpec((group, NPNO, 1), lambda i, q, s, f: (i + base, 0, 0)),
            pl.BlockSpec((group, 1, NPNO), lambda i, q, s, f: (i + base, 0, 0)),
            own_spec,
        ],
        out_specs=pl.BlockSpec((group, NPNO, NPNO), lambda i, q, s, f: (i, 0, 0)),
        scratch_shapes=[
            pltpu.VMEM((2, 2 * group, NPNO, NPNO), jnp.float32),
            pltpu.SemaphoreType.DMA((2, 2 * group)),
        ],
    )
    flops = count * 2 * 4 * 2 * NPNO * NPNO * NPNO
    kernel = functools.partial(
        coupling_kernel, final=final, width=sources[0].shape[0], group=group, start=start, nsrc=len(sources)
    )
    return pl.pallas_call(
        kernel,
        grid_spec=grid_spec,
        out_shape=jax.ShapeDtypeStruct((count, NPNO, NPNO), jnp.float32),
        cost_estimate=pl.CostEstimate(
            flops=flops,
            bytes_accessed=count * NPNO * NPNO * (2 * 4 + 2 * 2 + 3 * 4),
            transcendentals=0,
        ),
    )(nb, sizes, fock, *sources, margin, exchange, column, row, own)


def chunked_halo(chunks):
    received = [halo_sources(chunk, "pair") for chunk in chunks]
    return [r[k] for k in range(3) for r in received]


def per_device(
    three_index,
    pno_coef,
    pair_orbitals,
    natural_orbital_class,
    pno_energy,
    margin,
    neighbour_pairs,
    fock_coupling,
):
    occ_dev = three_index.shape[0]
    pair_dev = pno_coef.shape[0]
    position = lax.axis_index("pair")
    sizes = class_size(natural_orbital_class)
    blocks = halo_sources(three_index, "pair")
    local_orbitals = (pair_orbitals - (position - 1) * occ_dev).astype(jnp.int32)
    half = pair_dev // 2
    presplit = halving_ready(half) and half % 8 == 0
    coef_t = jnp.swapaxes(pno_coef, 2, 3)
    left_t = left_halves(local_orbitals[:, 0] - occ_dev, sizes, three_index, coef_t)
    halves = [
        partial_exchange(
            local_orbitals[:, 0] - occ_dev,
            local_orbitals[:, 1],
            sizes,
            blocks,
            left_t,
            coef_t,
            c * half,
            half,
            send_first(c) if presplit else None,
        )
        for c in range(2)
    ]
    exchange_ints = sum_over_aux(halves, presplit)
    denominator = pno_energy[:, :, None] + pno_energy[:, None, :]
    local_rows = (neighbour_pairs - (position - 1) * pair_dev).astype(jnp.int32).reshape(-1)
    fock = fock_coupling.reshape(-1)

    chunk = pair_dev // 2 if pair_dev % 8 == 0 else pair_dev
    parts = [-(exchange_ints / denominator)]
    sources = chunked_halo(parts)
    amplitudes = jnp.concatenate(parts, axis=0)
    for iteration in range(1, ITERS):
        parts = [
            coupling_step(
                local_rows, sizes, fock, sources, margin, exchange_ints, pno_energy, amplitudes,
                False, c * chunk, chunk,
            )
            for c in range(pair_dev // chunk)
        ]
        sources = chunked_halo(parts)
        amplitudes = jnp.concatenate(parts, axis=0)
    residual = coupling_step(
        local_rows, sizes, fock, sources, margin, exchange_ints, pno_energy, amplitudes, True
    )
    return (amplitudes, residual)


def solution(mesh):
    return jax.shard_map(
        per_device,
        mesh=mesh,
        in_specs=(
            P("pair", "aux", None),
            P("pair", None, None, None),
            P("pair", None),
            P("pair"),
            P("pair", None),
            P("pair", None, None, None),
            P("pair", None),
            P("pair", None),
        ),
        out_specs=(P("pair", None, None), P("pair", None, None)),
        check_vma=False,
    )
```
